32 devices in a mesh: vis: 2 (over x), ctx: 8 (over z, y), tp: 2 (over core).
Axes of the slice: x: 2, y: 2, z: 4, core: 2. Of those that a mesh axis runs over, the one named last changes fastest.
Arguments:
- patch_rows: bfloat16 [1024, 1280], P('ctx'), may hold values from -6 to 6
- vit_gain: float32 [1280], replicated, may hold values from 0.25 to 1.75
- vit_bias: float32 [1280], replicated, may hold values from -3 to 3
- vit_qkv: bfloat16 [1280, 3, 16, 80], P(None, None, ('vis', 'tp')), as said below
- vit_out: bfloat16 [16, 80, 1280], P(('vis', 'tp')), may hold values from -0.15625 to 0.15625
- merge_gain: float32 [1280], replicated, may hold values from 0.25 to 1.75
- merge_bias: float32 [1280], replicated, may hold values from -3 to 3
- merge_weight: bfloat16 [5120, 4096], P('ctx', ('vis', 'tp')), may hold values from -0.078125 to 0.078125
- image_patches: int32 [8, 2], replicated, may hold values from 4 to 64, as said below
- window_ids: int32 [1024], P('ctx'), may hold values from 0 to 1023, as said below
- image_pos: int32 [256], replicated, may hold values from 0 to 1023, as said below
- slice_order: int32 [8], replicated, may hold values from 0 to 7, as said below
- doc_ids: int32 [1024], replicated, may hold values from 0 to 3, never falling along the last dimension, each value on 1 to 512 neighbouring positions
- text_rows: bfloat16 [1024, 4096], P('ctx', ('vis', 'tp')), may hold values from -6 to 6
- norm_gain: float32 [4096], replicated, may hold values from 0.25 to 1.75
- w_query: bfloat16 [4096, 8, 4, 128], P(None, 'vis', 'tp'), as said below
- w_keyval: bfloat16 [2, 4096, 8, 128], P('tp', None, 'vis'), as said below
Outputs:
- attention_out: bfloat16 [1024, 8, 512], P('ctx', 'vis', 'tp')
The draws below stay inside these ranges and needn't reach their ends.
Inputs may be any that keep to these rules, and one draw needn't show every extreme that they name: `image_patches`: each is h * w for an image of h by w patches, h and w even and at most 32; the images of one ctx shard hold at most 128 patches together, exactly 128 on some shard. `window_ids`: equal ids mark one attention window: consecutive slots of one ctx shard, a multiple of 4 of them and at most 64, never in two images; slots after a shard's live patches form windows of 4. `slice_order`: a permutation; ctx shard c holds the sequence slices slice_order[c] and 15 - slice_order[c] of 64 positions, in that order, as its 128 rows. `image_pos`: distinct positions, one for every merged slot, live or not; the 32 slots of any one ctx shard put exactly 4 positions into the rows of each ctx shard. `doc_ids`: never falling along positions; each document holds 1 to 512 positions. `vit_qkv`: independent centred entries. `w_query`: independent centred entries. `w_keyval`: independent centred entries.
All inputs are finite; a program needn't handle non-finite values.
Results may differ from the reference program's by a relative error of at most 0.022.
The reference program's roundings to bfloat16 on the way count: a program that leaves them out, or rounds other values in their place, can miss the bound.
Values may be sent and summed in bfloat16 or wider, within the bound.
No kernel may reach another device: no remote copies, remote signals or barrier semaphores. Data moves between devices by JAX's collectives and lax.ppermute only.
A program may use at most 64 MiB of HBM per device.

```python
import math
import jax
import jax.numpy as jnp
import numpy as np
from jax import lax

D = 4096
HD = 128
KVH = 8
QPG = 4
VD = 1280
VH = 16
VHD = 80
IMGS = 2
TOK = 128
PCAP = 128
SHARDS = 8
SEQ = 1024
HALF = 64
ICAP = 32
IMGMAX = 64
DOCS = 4
DOCMAX = 512


def image_grids(seed_key):
    base_key = jax.random.fold_in(seed_key, 101)
    height_key, width_key, full_key = jax.random.split(base_key, 3)
    heights = 2 * jax.random.randint(height_key, (SHARDS, IMGS), 1, 17)
    width_cap = jnp.minimum(32, IMGMAX // heights // 2 * 2)
    widths = 2 * jax.random.randint(width_key, (SHARDS, IMGS), 1, width_cap // 2 + 1)
    full_shard = jax.random.randint(full_key, (), 0, SHARDS)
    if IMGMAX <= 64:
        full_height = 8
    elif IMGMAX <= 256:
        full_height = 16
    else:
        full_height = 32
    is_full = (jnp.arange(SHARDS) == full_shard)[:, None]
    heights = jnp.where(is_full, full_height, heights)
    widths = jnp.where(is_full, IMGMAX // full_height, widths)
    return (heights.astype(jnp.int32), widths.astype(jnp.int32))


def draw_image_patches(key, part):
    heights, widths = image_grids(key)
    return (heights * widths).astype(jnp.int32)


def draw_window_ids(key, part):
    heights, widths = image_grids(key)
    corner = 8 * jnp.arange(4, dtype=jnp.int32)
    tall = jnp.clip(heights[:, :, None] - corner, 0, 8)
    broad = jnp.clip(widths[:, :, None] - corner, 0, 8)
    sizes = (tall[:, :, :, None] * broad[:, :, None, :]).reshape(SHARDS, IMGS * 16)
    ends = jnp.cumsum(sizes, axis=1)
    slot_ids = jnp.arange(PCAP, dtype=jnp.int32)
    inside = jnp.sum((ends[:, None, :] <= slot_ids[None, :, None]).astype(jnp.int32), axis=2)
    filled = ends[:, -1:]
    spare = IMGS * 16 + (slot_ids[None, :] - filled) // 4
    local_ids = jnp.where(slot_ids[None, :] >= filled, spare, inside)
    return (local_ids + jnp.arange(SHARDS, dtype=jnp.int32)[:, None] * PCAP).reshape(SHARDS * PCAP).astype(jnp.int32)


def shuffle_rows(seed_key):
    return jax.random.permutation(seed_key, TOK).astype(jnp.int32)


def shard_layout(seed_key):
    base_key = jax.random.fold_in(seed_key, 202)
    slice_key, order_key, row_key = jax.random.split(base_key, 3)
    slice_order = jax.random.permutation(slice_key, SHARDS).astype(jnp.int32)
    dest_order = jax.random.permutation(order_key, SHARDS).astype(jnp.int32)
    row_orders = jax.vmap(shuffle_rows)(jax.random.split(row_key, SHARDS))
    send_each = ICAP // SHARDS
    source = jnp.arange(SHARDS, dtype=jnp.int32)[:, None]
    slot_ids = jnp.arange(ICAP, dtype=jnp.int32)[None, :]
    target = dest_order[(source + slot_ids // send_each) % SHARDS]
    entry = source * send_each + slot_ids % send_each
    rows_at = row_orders[target, entry]
    slices = jnp.where(rows_at < HALF, slice_order[target], 2 * SHARDS - 1 - slice_order[target])
    positions = slices * HALF + rows_at % HALF
    return (slice_order, positions.reshape(SHARDS * ICAP).astype(jnp.int32))


def draw_slice_order(key, part):
    slice_order, positions = shard_layout(key)
    return slice_order


def draw_image_pos(key, part):
    slice_order, positions = shard_layout(key)
    return positions


def draw_vit_qkv(key, part):
    noise = jax.random.normal(jax.random.fold_in(key, 303), (VD, 3, VH, VHD), jnp.float32)
    return (noise * (1.0 / math.sqrt(VD))).astype(jnp.bfloat16)


def draw_w_query(key, part):
    noise = jax.random.normal(jax.random.fold_in(key, 404), (D, KVH, QPG, HD), jnp.float32)
    boost = 1.0
    return (noise * (boost / math.sqrt(D))).astype(jnp.bfloat16)


def draw_w_keyval(key, part):
    noise = jax.random.normal(jax.random.fold_in(key, 505), (2, D, KVH, HD), jnp.float32)
    return (noise * (1.0 / math.sqrt(D))).astype(jnp.bfloat16)


def block_scale(rng, shape, cuts, low, high):
    level = 1.0
    for position, blocks in cuts:
        steps = jax.random.uniform(jax.random.fold_in(jax.random.fold_in(rng, 6), position), (blocks,), jnp.float32, low / len(cuts), high / len(cuts))
        level = level * jnp.repeat(jnp.exp(steps), shape[position] // blocks).reshape((-1,) + (1,) * (len(shape) - 1 - position))
    return level


def profile(amount, total, most, skew):
    loads = [(1 << 20) // math.isqrt(grade ** skew) + 1 for grade in range(2, amount + 1)]
    surplus, holding = total - most - (amount - 1), [1] * (amount - 1)
    while surplus > 0:
        movable = [i for i in range(amount - 1) if holding[i] < most]
        whole, left = sum([loads[i] for i in movable]), surplus
        for i in movable:
            more = min(most - holding[i], max(1, left * loads[i] // whole), surplus)
            holding[i] = holding[i] + more
            surplus = surplus - more
    return np.array([most] + holding)


def uneven_parts(stream_key, amount, total, reach, slope):
    if amount == 2:
        one = jax.random.randint(stream_key, (), max(1, total - reach), min(reach, total - 1) + 1)
        return jnp.stack([one, total - one])
    sizes = jnp.asarray(profile(amount, total, reach, slope), jnp.int32)
    pairs = (amount - 1) // 2
    donor, receiver = sizes[1:1 + 2 * pairs:2], sizes[2:2 + 2 * pairs:2]
    room = jnp.minimum(donor - 1, reach - receiver)
    shifted = jax.random.randint(jax.random.fold_in(stream_key, 1), (pairs,), 0, 1 << 20) % (room + 1)
    sizes = sizes.at[1:1 + 2 * pairs:2].set(donor - shifted).at[2:2 + 2 * pairs:2].set(receiver + shifted)
    return sizes[jax.random.permutation(jax.random.fold_in(stream_key, 2), amount)]


def scatter_about(rng, dims, width, most, pieces=(), held_as=jnp.bfloat16):
    result = jax.random.normal(rng, dims, jnp.float32) * width
    if len(pieces) > 0:
        result = block_scale(rng, dims, pieces, -0.22, 0.18) * result
    return jnp.clip(result, min=-most, max=most).astype(held_as)


def setup_inputs(seed: int = 0) -> dict:
    key_list = jax.random.split(jax.random.key(seed), 18)
    return {
        "patch_rows": scatter_about(key_list[0], (SHARDS * PCAP, VD), 1.0, 6.0, ((0, 8),)),
        "vit_gain": jnp.clip(1.0 + 0.15 * jax.random.normal(key_list[1], (VD,), jnp.float32), 0.25, 1.75),
        "vit_bias": scatter_about(key_list[2], (VD,), 0.5, 3.0, (), jnp.float32),
        "vit_qkv": draw_vit_qkv(jax.random.fold_in(key_list[17], 71), 0),
        "vit_out": scatter_about(key_list[4], (VH, VHD, VD), (VH * VHD) ** -0.5, 0.15625, ((0, 4),)),
        "merge_gain": jnp.clip(1.0 + 0.15 * jax.random.normal(key_list[5], (VD,), jnp.float32), 0.25, 1.75),
        "merge_bias": scatter_about(key_list[6], (VD,), 0.5, 3.0, (), jnp.float32),
        "merge_weight": scatter_about(key_list[7], (4 * VD, D), (4 * VD) ** -0.5, 0.078125, ((0, 8), (1, 4))),
        "image_patches": draw_image_patches(jax.random.fold_in(key_list[17], 71), 0),
        "window_ids": draw_window_ids(jax.random.fold_in(key_list[17], 71), 0),
        "image_pos": draw_image_pos(jax.random.fold_in(key_list[17], 71), 0),
        "slice_order": draw_slice_order(jax.random.fold_in(key_list[17], 71), 0),
        "doc_ids": jnp.searchsorted(jnp.cumsum(uneven_parts(key_list[12], DOCS, SEQ, DOCMAX, 0)), jnp.arange(SEQ), side="right").astype(jnp.int32),
        "text_rows": scatter_about(key_list[13], (SEQ, D), 1.0, 6.0, ((0, 8), (1, 4))),
        "norm_gain": jnp.clip(1.0 + 0.15 * jax.random.normal(key_list[14], (D,), jnp.float32), 0.25, 1.75),
        "w_query": draw_w_query(jax.random.fold_in(key_list[17], 71), 0),
        "w_keyval": draw_w_keyval(jax.random.fold_in(key_list[17], 71), 0),
    }


norm_eps = 1e-06
rope_base = 1000000.0
big_negative = -1e+30

def layer_norm(values, scale_vec, shift_vec):
    centre = lax.optimization_barrier(jnp.mean(values, axis=-1, keepdims=True))
    offset = values - centre
    spread = lax.optimization_barrier(jnp.mean(offset * offset, axis=-1, keepdims=True))
    return offset * lax.rsqrt(spread + norm_eps) * scale_vec + shift_vec

def rotate(values, positions):
    half_dim = values.shape[-1] // 2
    exponent = jnp.arange(half_dim, dtype=jnp.float32) * (-2.0 / values.shape[-1])
    frequency = jnp.power(jnp.float32(rope_base), exponent)
    angles = positions.astype(jnp.float32)[:, None] * frequency[None, :]
    shape_out = (values.shape[0],) + (1,) * (values.ndim - 2) + (half_dim,)
    cosine = jnp.cos(angles).reshape(shape_out)
    sine_part = jnp.sin(angles).reshape(shape_out)
    lead_half = values[..., :half_dim]
    tail_half = values[..., half_dim:]
    return jnp.concatenate([lead_half * cosine - tail_half * sine_part, tail_half * cosine + lead_half * sine_part], axis=-1)

def row_positions(row_ids, slice_order, tokens_dev):
    shards = slice_order.shape[0]
    device_of = row_ids // tokens_dev
    local_row = row_ids % tokens_dev
    half_tok = tokens_dev // 2
    matches = device_of[:, None] == jnp.arange(shards, dtype=jnp.int32)[None, :]
    first_slice = lax.optimization_barrier(jnp.sum(jnp.where(matches, slice_order[None, :], 0), axis=1)).astype(jnp.int32)
    slice_ids = jnp.where(local_row < half_tok, first_slice, 2 * shards - 1 - first_slice)
    return (slice_ids * half_tok + local_row % half_tok).astype(jnp.int32)

def place_of(positions, slice_order, tokens_dev):
    shards = slice_order.shape[0]
    half_tok = tokens_dev // 2
    slice_ids = positions // half_tok
    paired = jnp.minimum(slice_ids, 2 * shards - 1 - slice_ids)
    owner_hot = (paired[..., None] == slice_order).astype(jnp.int32)
    owner_dev = lax.optimization_barrier(jnp.sum(owner_hot * jnp.arange(shards, dtype=jnp.int32), axis=-1)).astype(jnp.int32)
    local_row = (jnp.where(slice_ids < shards, 0, half_tok) + positions % half_tok).astype(jnp.int32)
    return (owner_dev, local_row, owner_hot)

def vision_block(patch_block, window_block, vit_gain, vit_bias, vit_qkv, vit_out, merge_gain, merge_bias):
    vit_width = vit_qkv.shape[0]
    vit_heads = vit_qkv.shape[2]
    head_dim = vit_qkv.shape[3]
    slot_count = patch_block.shape[0]
    normed = layer_norm(patch_block.astype(jnp.float32), vit_gain, vit_bias).astype(jnp.bfloat16)
    projected = jnp.dot(normed, vit_qkv.reshape(vit_width, 3 * vit_heads * head_dim), preferred_element_type=jnp.float32)
    projected = lax.optimization_barrier(projected.astype(jnp.bfloat16)).astype(jnp.float32)
    projected = projected.reshape(slot_count, 3, vit_heads, head_dim)
    scores = jnp.einsum('qhd,khd->hqk', projected[:, 0], projected[:, 1]) / math.sqrt(head_dim)
    allowed = window_block[:, None] == window_block[None, :]
    scores = jnp.where(allowed[None], scores, big_negative)
    powers = jnp.exp(scores - lax.optimization_barrier(jnp.max(scores, axis=-1, keepdims=True)))
    totals = lax.optimization_barrier(jnp.sum(powers, axis=-1))
    rounded = lax.optimization_barrier(powers.astype(jnp.bfloat16)).astype(jnp.float32)
    blended = jnp.einsum('hqk,khd->qhd', rounded, projected[:, 2]) / jnp.transpose(totals)[:, :, None]
    blended = blended.astype(jnp.bfloat16).reshape(slot_count, vit_heads * head_dim)
    branch_sum = jnp.dot(blended, vit_out.reshape(vit_heads * head_dim, vit_width), preferred_element_type=jnp.float32)
    hidden = patch_block.astype(jnp.float32) + branch_sum
    merged = layer_norm(hidden, merge_gain, merge_bias).astype(jnp.bfloat16)
    return merged.reshape(slot_count // 4, 4 * vit_width)

def reference(patch_rows, vit_gain, vit_bias, vit_qkv, vit_out, merge_gain, merge_bias, merge_weight, image_patches, window_ids, image_pos, slice_order, doc_ids, text_rows, norm_gain, w_query, w_keyval):

    def one_shard(inputs_now):
        patch_block, window_block = inputs_now
        return vision_block(patch_block, window_block, vit_gain, vit_bias, vit_qkv, vit_out, merge_gain, merge_bias)
    merged = lax.map(one_shard, (patch_rows.reshape(SHARDS, PCAP, VD), window_ids.reshape(SHARDS, PCAP)))
    image_emb = jnp.dot(merged.reshape(SHARDS * ICAP, 4 * VD), merge_weight, preferred_element_type=jnp.float32).astype(jnp.bfloat16)
    live_count = (lax.optimization_barrier(jnp.sum(image_patches, axis=1)) // 4).astype(jnp.int32)
    slot_ids = jnp.arange(ICAP, dtype=jnp.int32)
    is_live = (slot_ids[None, :] < live_count[:, None]).reshape(SHARDS * ICAP)
    owner_dev, local_row, owner_hot = place_of(image_pos, slice_order, TOK)
    target = jnp.where(is_live, owner_dev * TOK + local_row, SEQ).astype(jnp.int32)
    embeds = text_rows.at[target].set(image_emb, mode='drop')
    widened = embeds.astype(jnp.float32)
    normed = (widened * lax.rsqrt(lax.optimization_barrier(jnp.mean(widened * widened, axis=1, keepdims=True)) + norm_eps) * norm_gain).astype(jnp.bfloat16)
    positions = row_positions(jnp.arange(SEQ, dtype=jnp.int32), slice_order, TOK)
    doc_of = jnp.take(doc_ids, positions)
    queries = jnp.dot(normed, w_query.reshape(D, KVH * QPG * HD), preferred_element_type=jnp.float32).reshape(SEQ, KVH, QPG, HD)
    queries = rotate(queries, positions).astype(jnp.bfloat16)
    keys_all = jnp.dot(normed, w_keyval[0].reshape(D, KVH * HD), preferred_element_type=jnp.float32).reshape(SEQ, KVH, HD)
    keys_all = rotate(keys_all, positions).astype(jnp.bfloat16)
    values_all = jnp.dot(normed, w_keyval[1].reshape(D, KVH * HD), preferred_element_type=jnp.float32).astype(jnp.bfloat16).reshape(SEQ, KVH, HD)
    keys_heads = jnp.transpose(keys_all, (1, 0, 2)).astype(jnp.float32)
    values_heads = jnp.transpose(values_all, (1, 0, 2)).astype(jnp.float32)
    query_block = math.gcd(SEQ, 512)

    def one_block(block_index):
        first_row = block_index * query_block
        query_rows = lax.dynamic_slice_in_dim(queries, first_row, query_block, 0).astype(jnp.float32)
        query_pos = lax.dynamic_slice_in_dim(positions, first_row, query_block, 0)
        query_doc = lax.dynamic_slice_in_dim(doc_of, first_row, query_block, 0)
        allowed = (positions[None, :] <= query_pos[:, None]) & (doc_of[None, :] == query_doc[:, None])

        def one_head(inputs_now):
            head_queries, head_keys, head_values = inputs_now
            scores = jnp.einsum('qgd,kd->gqk', head_queries, head_keys) / math.sqrt(HD)
            scores = jnp.where(allowed[None], scores, big_negative)
            powers = jnp.exp(scores - lax.optimization_barrier(jnp.max(scores, axis=-1, keepdims=True)))
            totals = lax.optimization_barrier(jnp.sum(powers, axis=-1))
            rounded = lax.optimization_barrier(powers.astype(jnp.bfloat16)).astype(jnp.float32)
            blended = jnp.einsum('gqk,kd->qgd', rounded, head_values) / jnp.transpose(totals)[:, :, None]
            return blended.astype(jnp.bfloat16)
        per_head = lax.map(one_head, (jnp.transpose(query_rows, (1, 0, 2, 3)), keys_heads, values_heads))
        return jnp.transpose(per_head, (1, 0, 2, 3)).reshape(query_block, KVH, QPG * HD)
    blocks = lax.map(one_block, jnp.arange(SEQ // query_block, dtype=jnp.int32))
    return blocks.reshape(SEQ, KVH, QPG * HD)
```

```python
import math

import jax
import jax.numpy as jnp
from jax import lax
from jax.sharding import PartitionSpec as P

D = 4096
HD = 128
VD = 1280
VHD = 80
TOK = 128
PCAP = 128
ICAP = 32


norm_eps = 1e-06
rope_base = 1000000.0
big_negative = -1e30


def swapped(value, axis, stride):
    return lax.ppermute(value, axis, [(i, i ^ 1 << stride) for i in range(lax.axis_size(axis))])


def layer_norm(values, scale_vec, shift_vec):
    centre = jnp.mean(values, axis=-1, keepdims=True)
    offset = values - centre
    spread = jnp.mean(offset * offset, axis=-1, keepdims=True)
    return offset * lax.rsqrt(spread + norm_eps) * scale_vec + shift_vec


def rotate(values, positions):
    half_dim = values.shape[-1] // 2
    exponent = jnp.arange(half_dim, dtype=jnp.float32) * (-2.0 / values.shape[-1])
    frequency = jnp.power(jnp.float32(rope_base), exponent)
    angles = positions.astype(jnp.float32)[:, None] * frequency[None, :]
    shape_out = (values.shape[0],) + (1,) * (values.ndim - 2) + (half_dim,)
    cosine = jnp.cos(angles).reshape(shape_out)
    sine_part = jnp.sin(angles).reshape(shape_out)
    lead_half = values[..., :half_dim]
    tail_half = values[..., half_dim:]
    return jnp.concatenate(
        [lead_half * cosine - tail_half * sine_part, tail_half * cosine + lead_half * sine_part],
        axis=-1,
    )


def row_positions(row_ids, slice_order, tokens_dev):
    shards = slice_order.shape[0]
    device_of = row_ids // tokens_dev
    local_row = row_ids % tokens_dev
    half_tok = tokens_dev // 2
    matches = device_of[:, None] == jnp.arange(shards, dtype=jnp.int32)[None, :]
    first_slice = jnp.sum(jnp.where(matches, slice_order[None, :], 0), axis=1)
    slice_ids = jnp.where(local_row < half_tok, first_slice, 2 * shards - 1 - first_slice)
    return slice_ids * half_tok + local_row % half_tok


def place_of(positions, slice_order, tokens_dev):
    shards = slice_order.shape[0]
    half_tok = tokens_dev // 2
    slice_ids = positions // half_tok
    paired = jnp.minimum(slice_ids, 2 * shards - 1 - slice_ids)
    owner_hot = (paired[..., None] == slice_order).astype(jnp.int32)
    owner_dev = jnp.sum(owner_hot * jnp.arange(shards, dtype=jnp.int32), axis=-1)
    local_row = jnp.where(slice_ids < shards, 0, half_tok) + positions % half_tok
    return (owner_dev, local_row, owner_hot)


def local(
    patch_rows,
    vit_gain,
    vit_bias,
    vit_qkv,
    vit_out,
    merge_gain,
    merge_bias,
    merge_weight,
    image_patches,
    window_ids,
    image_pos,
    slice_order,
    doc_ids,
    text_rows,
    norm_gain,
    w_query,
    w_keyval,
):
    shards = lax.axis_size("ctx")
    ctx_index = lax.axis_index("ctx")
    tp_index = lax.axis_index("tp")
    block_feats = merge_weight.shape[0]
    normed = layer_norm(patch_rows.astype(jnp.float32), vit_gain, vit_bias).astype(jnp.bfloat16)
    projected = jnp.einsum(
        "pf,fxhd->pxhd", normed, vit_qkv, preferred_element_type=jnp.float32
    ).astype(jnp.bfloat16)
    scores = jnp.einsum(
        "qhd,khd->hqk", projected[:, 0], projected[:, 1], preferred_element_type=jnp.float32
    ) / math.sqrt(VHD)
    allowed = window_ids[:, None] == window_ids[None, :]
    scores = jnp.where(allowed[None], scores, big_negative)
    powers = jnp.exp(scores - jnp.max(scores, axis=-1, keepdims=True))
    totals = jnp.sum(powers, axis=-1)
    blended = jnp.einsum(
        "hqk,khd->qhd",
        powers.astype(jnp.bfloat16),
        projected[:, 2],
        preferred_element_type=jnp.float32,
    )
    blended = (blended / jnp.transpose(totals)[:, :, None]).astype(jnp.bfloat16)
    branch_part = jnp.einsum("phd,hdf->pf", blended, vit_out, preferred_element_type=jnp.float32)
    branch_sum = lax.psum(branch_part, ("vis", "tp"))
    hidden = patch_rows.astype(jnp.float32) + branch_sum
    merged = layer_norm(hidden, merge_gain, merge_bias).astype(jnp.bfloat16).reshape(ICAP, 4 * VD)
    send_each = ICAP // shards
    slot_ids = jnp.arange(ICAP, dtype=jnp.int32)
    shard_ids = jnp.arange(shards, dtype=jnp.int32)
    live_count = jnp.sum(image_patches, axis=1) // 4
    all_pos = image_pos.reshape(shards, ICAP)
    owner_dev, local_row, owner_hot = place_of(all_pos, slice_order, TOK)
    before = jnp.cumsum(owner_hot, axis=1) - owner_hot
    rank_in = jnp.sum(before * owner_hot, axis=-1)
    is_live = slot_ids[None, :] < live_count[:, None]
    own_hot = (shard_ids == ctx_index)[:, None]
    own_owner = jnp.sum(jnp.where(own_hot, owner_dev, 0), axis=0)
    own_rank = jnp.sum(jnp.where(own_hot, rank_in, 0), axis=0)
    target_slot = own_owner * send_each + own_rank
    picker = (target_slot[None, :] == slot_ids[:, None]).astype(jnp.bfloat16)
    ordered = jnp.dot(picker, merged, preferred_element_type=jnp.float32).astype(jnp.bfloat16)
    blocks = jnp.transpose(ordered.reshape(ICAP, shards, block_feats), (1, 0, 2))
    received = lax.all_to_all(blocks, "ctx", split_axis=0, concat_axis=0, tiled=True)
    by_dest = jnp.transpose(
        received.reshape(shards, shards, send_each, block_feats), (1, 0, 2, 3)
    ).reshape(shards * ICAP, block_feats)
    partial = jnp.dot(by_dest, merge_weight, preferred_element_type=jnp.float32)
    incoming = lax.psum_scatter(partial, "ctx", scatter_dimension=0, tiled=True).astype(
        jnp.bfloat16
    )
    mine_live = ((owner_dev == ctx_index) & is_live).reshape(-1)
    column_of = (shard_ids[:, None] * send_each + rank_in).reshape(-1)
    row_hot = (
        (local_row.reshape(-1)[None, :] == jnp.arange(TOK, dtype=jnp.int32)[:, None])
        & mine_live[None, :]
    ).astype(jnp.bfloat16)
    column_hot = (column_of[:, None] == slot_ids[None, :]).astype(jnp.bfloat16)
    placing = jnp.dot(row_hot, column_hot, preferred_element_type=jnp.float32)
    is_image = jnp.sum(placing, axis=1) > 0.5
    image_part = jnp.dot(placing.astype(jnp.bfloat16), incoming, preferred_element_type=jnp.float32)
    embeds = jnp.where(is_image[:, None], image_part.astype(jnp.bfloat16), text_rows)
    full_rows = lax.all_gather(embeds, ("vis", "tp"), axis=1, tiled=True)
    widened = full_rows.astype(jnp.float32)
    normed_rows = (
        widened
        * lax.rsqrt(jnp.mean(widened * widened, axis=1, keepdims=True) + norm_eps)
        * norm_gain
    ).astype(jnp.bfloat16)
    own_positions = row_positions(
        ctx_index * TOK + jnp.arange(TOK, dtype=jnp.int32), slice_order, TOK
    )
    own_doc = jnp.take(doc_ids, own_positions)
    kv_heads = w_query.shape[1]
    groups = w_query.shape[2]
    queries = jnp.einsum(
        "td,dhgk->thgk", normed_rows, w_query, preferred_element_type=jnp.float32
    )
    queries = rotate(queries, own_positions).astype(jnp.bfloat16)
    projected_half = jnp.einsum(
        "td,dhk->thk", normed_rows, w_keyval[0], preferred_element_type=jnp.float32
    )
    own_half = jnp.where(
        tp_index == 0, rotate(projected_half, own_positions), projected_half
    ).astype(jnp.bfloat16)
    both = lax.all_gather(own_half, ("ctx", "tp"), axis=0, tiled=False).reshape(
        shards, 2, TOK, kv_heads, HD
    )
    key_count = shards * TOK
    keys_every = both[:, 0].reshape(key_count, kv_heads, HD)
    values_every = both[:, 1].reshape(key_count, kv_heads, HD)
    key_pos = row_positions(jnp.arange(key_count, dtype=jnp.int32), slice_order, TOK)
    key_doc = jnp.take(doc_ids, key_pos)
    allowed_now = (key_pos[None, :] <= own_positions[:, None]) & (
        key_doc[None, :] == own_doc[:, None]
    )
    scores_now = jnp.einsum(
        "qkgd,nkd->kgqn", queries, keys_every, preferred_element_type=jnp.float32
    ) / math.sqrt(HD)
    scores_now = jnp.where(allowed_now[None, None], scores_now, big_negative)
    best = jnp.max(scores_now, axis=-1, keepdims=True)
    powers_now = jnp.exp(scores_now - best)
    total_final = jnp.sum(powers_now, axis=-1)
    accum_final = jnp.einsum(
        "kgqn,nkd->kgqd",
        powers_now.astype(jnp.bfloat16),
        values_every,
        preferred_element_type=jnp.float32,
    )
    result = accum_final / total_final[..., None]
    return (
        jnp.transpose(result, (2, 0, 1, 3)).reshape(TOK, kv_heads, groups * HD).astype(jnp.bfloat16)
    )


def solution(mesh):
    placed = (
        P("ctx", None),
        P(),
        P(),
        P(None, None, ("vis", "tp"), None),
        P(("vis", "tp"), None, None),
        P(),
        P(),
        P("ctx", ("vis", "tp")),
        P(),
        P("ctx"),
        P(),
        P(),
        P(),
        P("ctx", ("vis", "tp")),
        P(),
        P(None, "vis", "tp", None),
        P("tp", None, "vis", None),
    )
    return jax.shard_map(
        local, mesh=mesh, in_specs=placed, out_specs=P("ctx", "vis", "tp"), check_vma=False
    )
```

```python
import math

import jax
import jax.numpy as jnp
from jax import lax
from jax.sharding import PartitionSpec as P

D = 4096
HD = 128
VD = 1280
VHD = 80
TOK = 128
PCAP = 128
ICAP = 32


norm_eps = 1e-06
rope_base = 1000000.0
big_negative = -1e30


def swapped(value, axis, stride):
    return lax.ppermute(value, axis, [(i, i ^ 1 << stride) for i in range(lax.axis_size(axis))])


def layer_norm(values, scale_vec, shift_vec):
    centre = jnp.mean(values, axis=-1, keepdims=True)
    offset = values - centre
    spread = jnp.mean(offset * offset, axis=-1, keepdims=True)
    return offset * lax.rsqrt(spread + norm_eps) * scale_vec + shift_vec


def rotate(values, positions):
    half_dim = values.shape[-1] // 2
    exponent = jnp.arange(half_dim, dtype=jnp.float32) * (-2.0 / values.shape[-1])
    frequency = jnp.power(jnp.float32(rope_base), exponent)
    angles = positions.astype(jnp.float32)[:, None] * frequency[None, :]
    shape_out = (values.shape[0],) + (1,) * (values.ndim - 2) + (half_dim,)
    cosine = jnp.cos(angles).reshape(shape_out)
    sine_part = jnp.sin(angles).reshape(shape_out)
    lead_half = values[..., :half_dim]
    tail_half = values[..., half_dim:]
    return jnp.concatenate(
        [lead_half * cosine - tail_half * sine_part, tail_half * cosine + lead_half * sine_part],
        axis=-1,
    )


def row_positions(row_ids, slice_order, tokens_dev):
    shards = slice_order.shape[0]
    device_of = row_ids // tokens_dev
    local_row = row_ids % tokens_dev
    half_tok = tokens_dev // 2
    matches = device_of[:, None] == jnp.arange(shards, dtype=jnp.int32)[None, :]
    first_slice = jnp.sum(jnp.where(matches, slice_order[None, :], 0), axis=1)
    slice_ids = jnp.where(local_row < half_tok, first_slice, 2 * shards - 1 - first_slice)
    return slice_ids * half_tok + local_row % half_tok


def place_of(positions, slice_order, tokens_dev):
    shards = slice_order.shape[0]
    half_tok = tokens_dev // 2
    slice_ids = positions // half_tok
    paired = jnp.minimum(slice_ids, 2 * shards - 1 - slice_ids)
    owner_hot = (paired[..., None] == slice_order).astype(jnp.int32)
    owner_dev = jnp.sum(owner_hot * jnp.arange(shards, dtype=jnp.int32), axis=-1)
    local_row = jnp.where(slice_ids < shards, 0, half_tok) + positions % half_tok
    return (owner_dev, local_row, owner_hot)


def halving_scatter(blocks, index, count):
    remaining = count
    bit = 0
    while remaining > 1:
        lower = blocks.reshape((remaining // 2, 2) + blocks.shape[1:])
        mine = (index >> bit) & 1
        keep = jnp.where(mine == 0, lower[:, 0], lower[:, 1])
        give = jnp.where(mine == 0, lower[:, 1], lower[:, 0])
        blocks = keep + swapped(give, "ctx", bit)
        remaining //= 2
        bit += 1
    return blocks[0]


def rotate_rows(values, positions):
    half_dim = values.shape[-1] // 2
    exponent = jnp.arange(half_dim, dtype=jnp.float32) * (-2.0 / values.shape[-1])
    frequency = jnp.power(jnp.float32(rope_base), exponent)
    angles = positions.astype(jnp.float32)[:, None] * frequency[None, :]
    cosine = jnp.cos(angles)
    sine_part = jnp.sin(angles)
    lead_half = values[..., :half_dim]
    tail_half = values[..., half_dim:]
    return jnp.concatenate(
        [lead_half * cosine - tail_half * sine_part, tail_half * cosine + lead_half * sine_part],
        axis=-1,
    )


def local(
    patch_rows,
    vit_gain,
    vit_bias,
    vit_qkv,
    vit_out,
    merge_gain,
    merge_bias,
    merge_weight,
    image_patches,
    window_ids,
    image_pos,
    slice_order,
    doc_ids,
    text_rows,
    norm_gain,
    w_query,
    w_keyval,
):
    shards = lax.axis_size("ctx")
    ctx_index = lax.axis_index("ctx")
    tp_index = lax.axis_index("tp")
    block_feats = merge_weight.shape[0]
    normed = layer_norm(patch_rows.astype(jnp.float32), vit_gain, vit_bias).astype(jnp.bfloat16)
    projected = jnp.einsum(
        "pf,fxhd->pxhd", normed, vit_qkv, preferred_element_type=jnp.float32
    ).astype(jnp.bfloat16)
    scores = jnp.einsum(
        "qhd,khd->hqk", projected[:, 0], projected[:, 1], preferred_element_type=jnp.float32
    ) / math.sqrt(VHD)
    allowed = window_ids[:, None] == window_ids[None, :]
    scores = jnp.where(allowed[None], scores, big_negative)
    powers = jnp.exp(scores - jnp.max(scores, axis=-1, keepdims=True))
    totals = jnp.sum(powers, axis=-1)
    blended = jnp.einsum(
        "hqk,khd->qhd",
        powers.astype(jnp.bfloat16),
        projected[:, 2],
        preferred_element_type=jnp.float32,
    )
    blended = (blended / jnp.transpose(totals)[:, :, None]).astype(jnp.bfloat16)
    branch_part = jnp.einsum("phd,hdf->pf", blended, vit_out, preferred_element_type=jnp.float32)
    branch_sum = branch_part + swapped(branch_part, "tp", 0)
    branch_sum = branch_sum + swapped(branch_sum, "vis", 0)
    hidden = patch_rows.astype(jnp.float32) + branch_sum
    merged = layer_norm(hidden, merge_gain, merge_bias).astype(jnp.bfloat16).reshape(ICAP, 4 * VD)
    send_each = ICAP // shards
    slot_ids = jnp.arange(ICAP, dtype=jnp.int32)
    shard_ids = jnp.arange(shards, dtype=jnp.int32)
    live_count = jnp.sum(image_patches, axis=1) // 4
    all_pos = image_pos.reshape(shards, ICAP)
    owner_dev, local_row, owner_hot = place_of(all_pos, slice_order, TOK)
    before = jnp.cumsum(owner_hot, axis=1) - owner_hot
    rank_in = jnp.sum(before * owner_hot, axis=-1)
    is_live = slot_ids[None, :] < live_count[:, None]
    own_hot = (shard_ids == ctx_index)[:, None]
    own_owner = jnp.sum(jnp.where(own_hot, owner_dev, 0), axis=0)
    own_rank = jnp.sum(jnp.where(own_hot, rank_in, 0), axis=0)
    target_slot = own_owner * send_each + own_rank
    picker = (target_slot[None, :] == slot_ids[:, None]).astype(jnp.bfloat16)
    ordered = jnp.dot(picker, merged, preferred_element_type=jnp.float32).astype(jnp.bfloat16)
    blocks = jnp.transpose(ordered.reshape(ICAP, shards, block_feats), (1, 0, 2))
    received = lax.all_to_all(blocks, "ctx", split_axis=0, concat_axis=0, tiled=True)
    by_dest = jnp.transpose(
        received.reshape(shards, shards, send_each, block_feats), (1, 0, 2, 3)
    ).reshape(shards * ICAP, block_feats)
    partial = jnp.dot(by_dest, merge_weight, preferred_element_type=jnp.float32)
    incoming = halving_scatter(partial.reshape(shards, ICAP, -1), ctx_index, shards).astype(
        jnp.bfloat16
    )
    mine_live = ((owner_dev == ctx_index) & is_live).reshape(-1)
    column_of = (shard_ids[:, None] * send_each + rank_in).reshape(-1)
    row_hot = (
        (local_row.reshape(-1)[None, :] == jnp.arange(TOK, dtype=jnp.int32)[:, None])
        & mine_live[None, :]
    ).astype(jnp.bfloat16)
    column_hot = (column_of[:, None] == slot_ids[None, :]).astype(jnp.bfloat16)
    placing = jnp.dot(row_hot, column_hot, preferred_element_type=jnp.float32)
    is_image = jnp.sum(placing, axis=1) > 0.5
    image_part = jnp.dot(placing.astype(jnp.bfloat16), incoming, preferred_element_type=jnp.float32)
    embeds = jnp.where(is_image[:, None], image_part.astype(jnp.bfloat16), text_rows)
    full_rows = lax.all_gather(embeds, ("vis", "tp"), axis=1, tiled=True)
    widened = full_rows.astype(jnp.float32)
    normed_rows = (
        widened
        * lax.rsqrt(jnp.mean(widened * widened, axis=1, keepdims=True) + norm_eps)
        * norm_gain
    ).astype(jnp.bfloat16)
    own_positions = row_positions(
        ctx_index * TOK + jnp.arange(TOK, dtype=jnp.int32), slice_order, TOK
    )
    own_doc = jnp.take(doc_ids, own_positions)
    kv_heads = w_query.shape[1]
    groups = w_query.shape[2]
    queries = jnp.einsum(
        "td,dhgk->hgtk", normed_rows, w_query, preferred_element_type=jnp.float32
    )
    queries = rotate_rows(queries, own_positions).astype(jnp.bfloat16)
    projected_half = jnp.einsum(
        "td,dhk->htk", normed_rows, w_keyval[0], preferred_element_type=jnp.float32
    )
    own_half = jnp.where(
        tp_index == 0, rotate_rows(projected_half, own_positions), projected_half
    ).astype(jnp.bfloat16)
    both = lax.all_gather(own_half, ("ctx", "tp"), axis=1, tiled=True).reshape(
        kv_heads, shards, 2, TOK, HD
    )
    key_count = shards * TOK
    keys_every = both[:, :, 0].reshape(kv_heads, key_count, HD)
    values_every = both[:, :, 1].reshape(kv_heads, key_count, HD)
    key_pos = row_positions(jnp.arange(key_count, dtype=jnp.int32), slice_order, TOK)
    key_doc = jnp.take(doc_ids, key_pos)
    allowed_now = (key_pos[None, :] <= own_positions[:, None]) & (
        key_doc[None, :] == own_doc[:, None]
    )
    scores_now = jnp.einsum(
        "hgtd,hnd->hgtn", queries, keys_every, preferred_element_type=jnp.float32
    ) / math.sqrt(HD)
    scores_now = jnp.where(allowed_now[None, None], scores_now, big_negative)
    best = jnp.max(scores_now, axis=-1, keepdims=True)
    powers_now = jnp.exp(scores_now - best)
    total_final = jnp.sum(powers_now, axis=-1)
    accum_final = jnp.einsum(
        "hgtn,hnd->hgtd",
        powers_now.astype(jnp.bfloat16),
        values_every,
        preferred_element_type=jnp.float32,
    )
    result = accum_final / total_final[..., None]
    return (
        jnp.transpose(result, (2, 0, 1, 3)).reshape(TOK, kv_heads, groups * HD).astype(jnp.bfloat16)
    )


def solution(mesh):
    placed = (
        P("ctx", None),
        P(),
        P(),
        P(None, None, ("vis", "tp"), None),
        P(("vis", "tp"), None, None),
        P(),
        P(),
        P("ctx", ("vis", "tp")),
        P(),
        P("ctx"),
        P(),
        P(),
        P(),
        P("ctx", ("vis", "tp")),
        P(),
        P(None, "vis", "tp", None),
        P("tp", None, "vis", None),
    )
    return jax.shard_map(
        local, mesh=mesh, in_specs=placed, out_specs=P("ctx", "vis", "tp"), check_vma=False
    )
```

```python
import math

import jax
import jax.numpy as jnp
from jax import lax
from jax.sharding import PartitionSpec as P

D = 4096
HD = 128
VD = 1280
VHD = 80
TOK = 128
PCAP = 128
ICAP = 32


norm_eps = 1e-06
rope_base = 1000000.0
big_negative = -1e30


def swapped(value, axis, stride):
    return lax.ppermute(value, axis, [(i, i ^ 1 << stride) for i in range(lax.axis_size(axis))])


def layer_norm(values, scale_vec, shift_vec):
    centre = jnp.mean(values, axis=-1, keepdims=True)
    offset = values - centre
    spread = jnp.mean(offset * offset, axis=-1, keepdims=True)
    return offset * lax.rsqrt(spread + norm_eps) * scale_vec + shift_vec


def rotate(values, positions):
    half_dim = values.shape[-1] // 2
    exponent = jnp.arange(half_dim, dtype=jnp.float32) * (-2.0 / values.shape[-1])
    frequency = jnp.power(jnp.float32(rope_base), exponent)
    angles = positions.astype(jnp.float32)[:, None] * frequency[None, :]
    shape_out = (values.shape[0],) + (1,) * (values.ndim - 2) + (half_dim,)
    cosine = jnp.cos(angles).reshape(shape_out)
    sine_part = jnp.sin(angles).reshape(shape_out)
    lead_half = values[..., :half_dim]
    tail_half = values[..., half_dim:]
    return jnp.concatenate(
        [lead_half * cosine - tail_half * sine_part, tail_half * cosine + lead_half * sine_part],
        axis=-1,
    )


def row_positions(row_ids, slice_order, tokens_dev):
    shards = slice_order.shape[0]
    device_of = row_ids // tokens_dev
    local_row = row_ids % tokens_dev
    half_tok = tokens_dev // 2
    matches = device_of[:, None] == jnp.arange(shards, dtype=jnp.int32)[None, :]
    first_slice = jnp.sum(jnp.where(matches, slice_order[None, :], 0), axis=1)
    slice_ids = jnp.where(local_row < half_tok, first_slice, 2 * shards - 1 - first_slice)
    return slice_ids * half_tok + local_row % half_tok


def place_of(positions, slice_order, tokens_dev):
    shards = slice_order.shape[0]
    half_tok = tokens_dev // 2
    slice_ids = positions // half_tok
    paired = jnp.minimum(slice_ids, 2 * shards - 1 - slice_ids)
    owner_hot = (paired[..., None] == slice_order).astype(jnp.int32)
    owner_dev = jnp.sum(owner_hot * jnp.arange(shards, dtype=jnp.int32), axis=-1)
    local_row = jnp.where(slice_ids < shards, 0, half_tok) + positions % half_tok
    return (owner_dev, local_row, owner_hot)


def halving_scatter(blocks, index, count):
    remaining = count
    bit = 0
    while remaining > 1:
        lower = blocks.reshape((remaining // 2, 2) + blocks.shape[1:])
        mine = (index >> bit) & 1
        keep = jnp.where(mine == 0, lower[:, 0], lower[:, 1])
        give = jnp.where(mine == 0, lower[:, 1], lower[:, 0])
        blocks = keep + swapped(give, "ctx", bit)
        remaining //= 2
        bit += 1
    return blocks[0]


def rotate_rows(values, positions):
    half_dim = values.shape[-1] // 2
    exponent = jnp.arange(half_dim, dtype=jnp.float32) * (-2.0 / values.shape[-1])
    frequency = jnp.power(jnp.float32(rope_base), exponent)
    angles = positions.astype(jnp.float32)[:, None] * frequency[None, :]
    cosine = jnp.cos(angles)
    sine_part = jnp.sin(angles)
    lead_half = values[..., :half_dim]
    tail_half = values[..., half_dim:]
    return jnp.concatenate(
        [lead_half * cosine - tail_half * sine_part, tail_half * cosine + lead_half * sine_part],
        axis=-1,
    )


def local(
    patch_rows,
    vit_gain,
    vit_bias,
    vit_qkv,
    vit_out,
    merge_gain,
    merge_bias,
    merge_weight,
    image_patches,
    window_ids,
    image_pos,
    slice_order,
    doc_ids,
    text_rows,
    norm_gain,
    w_query,
    w_keyval,
):
    shards = lax.axis_size("ctx")
    ctx_index = lax.axis_index("ctx")
    tp_index = lax.axis_index("tp")
    block_feats = merge_weight.shape[0]
    normed = layer_norm(patch_rows.astype(jnp.float32), vit_gain, vit_bias).astype(jnp.bfloat16)
    projected = jnp.einsum(
        "pf,fxhd->pxhd", normed, vit_qkv, preferred_element_type=jnp.float32
    ).astype(jnp.bfloat16)
    scores = jnp.einsum(
        "qhd,khd->hqk", projected[:, 0], projected[:, 1], preferred_element_type=jnp.float32
    ) / math.sqrt(VHD)
    allowed = window_ids[:, None] == window_ids[None, :]
    scores = jnp.where(allowed[None], scores, big_negative)
    powers = jnp.exp(scores - jnp.max(scores, axis=-1, keepdims=True))
    totals = jnp.sum(powers, axis=-1)
    blended = jnp.einsum(
        "hqk,khd->qhd",
        powers.astype(jnp.bfloat16),
        projected[:, 2],
        preferred_element_type=jnp.float32,
    )
    blended = (blended / jnp.transpose(totals)[:, :, None]).astype(jnp.bfloat16)
    branch_part = jnp.einsum("phd,hdf->pf", blended, vit_out, preferred_element_type=jnp.float32)
    branch_sum = branch_part + swapped(branch_part, "tp", 0)
    branch_sum = branch_sum + swapped(branch_sum, "vis", 0)
    hidden = patch_rows.astype(jnp.float32) + branch_sum
    merged = layer_norm(hidden, merge_gain, merge_bias).astype(jnp.bfloat16).reshape(ICAP, 4 * VD)
    send_each = ICAP // shards
    slot_ids = jnp.arange(ICAP, dtype=jnp.int32)
    shard_ids = jnp.arange(shards, dtype=jnp.int32)
    live_count = jnp.sum(image_patches, axis=1) // 4
    all_pos = image_pos.reshape(shards, ICAP)
    owner_dev, local_row, owner_hot = place_of(all_pos, slice_order, TOK)
    before = jnp.cumsum(owner_hot, axis=1) - owner_hot
    rank_in = jnp.sum(before * owner_hot, axis=-1)
    is_live = slot_ids[None, :] < live_count[:, None]
    own_hot = (shard_ids == ctx_index)[:, None]
    own_owner = jnp.sum(jnp.where(own_hot, owner_dev, 0), axis=0)
    own_rank = jnp.sum(jnp.where(own_hot, rank_in, 0), axis=0)
    target_slot = own_owner * send_each + own_rank
    picker = (target_slot[None, :] == slot_ids[:, None]).astype(jnp.bfloat16)
    ordered = jnp.dot(picker, merged, preferred_element_type=jnp.float32).astype(jnp.bfloat16)
    blocks = jnp.transpose(ordered.reshape(ICAP, shards, block_feats), (1, 0, 2))
    received = lax.all_to_all(blocks, "ctx", split_axis=0, concat_axis=0, tiled=True)
    by_dest = jnp.transpose(
        received.reshape(shards, shards, send_each, block_feats), (1, 0, 2, 3)
    ).reshape(shards * ICAP, block_feats)
    partial = jnp.dot(by_dest, merge_weight, preferred_element_type=jnp.float32)
    incoming = halving_scatter(partial.reshape(shards, ICAP, -1), ctx_index, shards).astype(
        jnp.bfloat16
    )
    mine_live = ((owner_dev == ctx_index) & is_live).reshape(-1)
    column_of = (shard_ids[:, None] * send_each + rank_in).reshape(-1)
    row_hot = (
        (local_row.reshape(-1)[None, :] == jnp.arange(TOK, dtype=jnp.int32)[:, None])
        & mine_live[None, :]
    ).astype(jnp.bfloat16)
    column_hot = (column_of[:, None] == slot_ids[None, :]).astype(jnp.bfloat16)
    placing = jnp.dot(row_hot, column_hot, preferred_element_type=jnp.float32)
    is_image = jnp.sum(placing, axis=1) > 0.5
    image_part = jnp.dot(placing.astype(jnp.bfloat16), incoming, preferred_element_type=jnp.float32)
    embeds = jnp.where(is_image[:, None], image_part.astype(jnp.bfloat16), text_rows)
    full_rows = lax.all_gather(embeds, ("vis", "tp"), axis=1, tiled=True)
    widened = full_rows.astype(jnp.float32)
    normed_rows = (
        widened
        * lax.rsqrt(jnp.mean(widened * widened, axis=1, keepdims=True) + norm_eps)
        * norm_gain
    ).astype(jnp.bfloat16)
    own_positions = row_positions(
        ctx_index * TOK + jnp.arange(TOK, dtype=jnp.int32), slice_order, TOK
    )
    own_doc = jnp.take(doc_ids, own_positions)
    kv_heads = w_query.shape[1]
    groups = w_query.shape[2]
    queries = jnp.einsum(
        "td,dhgk->thgk", normed_rows, w_query, preferred_element_type=jnp.float32
    )
    queries = rotate(queries, own_positions).astype(jnp.bfloat16)
    projected_half = jnp.einsum(
        "td,dhk->thk", normed_rows, w_keyval[0], preferred_element_type=jnp.float32
    )
    own_half = jnp.where(
        tp_index == 0, rotate(projected_half, own_positions), projected_half
    ).astype(jnp.bfloat16)
    gathered = lax.all_gather(own_half, "ctx", axis=0, tiled=True)
    partner_all = swapped(gathered, "tp", 0)
    keys_every = jnp.where(tp_index == 0, gathered, partner_all)
    values_every = jnp.where(tp_index == 0, partner_all, gathered)
    key_count = keys_every.shape[0]
    key_pos = row_positions(jnp.arange(key_count, dtype=jnp.int32), slice_order, TOK)
    key_doc = jnp.take(doc_ids, key_pos)
    allowed_now = (key_pos[None, :] <= own_positions[:, None]) & (
        key_doc[None, :] == own_doc[:, None]
    )
    scores_now = jnp.einsum(
        "qkgd,nkd->kgqn", queries, keys_every, preferred_element_type=jnp.float32
    ) / math.sqrt(HD)
    scores_now = jnp.where(allowed_now[None, None], scores_now, big_negative)
    best = jnp.max(scores_now, axis=-1, keepdims=True)
    powers_now = jnp.exp(scores_now - best)
    total_final = jnp.sum(powers_now, axis=-1)
    accum_final = jnp.einsum(
        "kgqn,nkd->kgqd",
        powers_now.astype(jnp.bfloat16),
        values_every,
        preferred_element_type=jnp.float32,
    )
    result = accum_final / total_final[..., None]
    return (
        jnp.transpose(result, (2, 0, 1, 3)).reshape(TOK, kv_heads, groups * HD).astype(jnp.bfloat16)
    )


def solution(mesh):
    placed = (
        P("ctx", None),
        P(),
        P(),
        P(None, None, ("vis", "tp"), None),
        P(("vis", "tp"), None, None),
        P(),
        P(),
        P("ctx", ("vis", "tp")),
        P(),
        P("ctx"),
        P(),
        P(),
        P(),
        P("ctx", ("vis", "tp")),
        P(),
        P(None, "vis", "tp", None),
        P("tp", None, "vis", None),
    )
    return jax.shard_map(
        local, mesh=mesh, in_specs=placed, out_specs=P("ctx", "vis", "tp"), check_vma=False
    )
```

```python
import math

import jax
import jax.numpy as jnp
from jax import lax
from jax.sharding import PartitionSpec as P

D = 4096
HD = 128
VD = 1280
VHD = 80
TOK = 128
PCAP = 128
ICAP = 32


norm_eps = 1e-06
rope_base = 1000000.0
big_negative = -1e30


def swapped(value, axis, stride):
    return lax.ppermute(value, axis, [(i, i ^ 1 << stride) for i in range(lax.axis_size(axis))])


def layer_norm(values, scale_vec, shift_vec):
    centre = jnp.mean(values, axis=-1, keepdims=True)
    offset = values - centre
    spread = jnp.mean(offset * offset, axis=-1, keepdims=True)
    return offset * lax.rsqrt(spread + norm_eps) * scale_vec + shift_vec


def rotate(values, positions):
    half_dim = values.shape[-1] // 2
    exponent = jnp.arange(half_dim, dtype=jnp.float32) * (-2.0 / values.shape[-1])
    frequency = jnp.power(jnp.float32(rope_base), exponent)
    angles = positions.astype(jnp.float32)[:, None] * frequency[None, :]
    shape_out = (values.shape[0],) + (1,) * (values.ndim - 2) + (half_dim,)
    cosine = jnp.cos(angles).reshape(shape_out)
    sine_part = jnp.sin(angles).reshape(shape_out)
    lead_half = values[..., :half_dim]
    tail_half = values[..., half_dim:]
    return jnp.concatenate(
        [lead_half * cosine - tail_half * sine_part, tail_half * cosine + lead_half * sine_part],
        axis=-1,
    )


def row_positions(row_ids, slice_order, tokens_dev):
    shards = slice_order.shape[0]
    device_of = row_ids // tokens_dev
    local_row = row_ids % tokens_dev
    half_tok = tokens_dev // 2
    matches = device_of[:, None] == jnp.arange(shards, dtype=jnp.int32)[None, :]
    first_slice = jnp.sum(jnp.where(matches, slice_order[None, :], 0), axis=1)
    slice_ids = jnp.where(local_row < half_tok, first_slice, 2 * shards - 1 - first_slice)
    return slice_ids * half_tok + local_row % half_tok


def place_of(positions, slice_order, tokens_dev):
    shards = slice_order.shape[0]
    half_tok = tokens_dev // 2
    slice_ids = positions // half_tok
    paired = jnp.minimum(slice_ids, 2 * shards - 1 - slice_ids)
    owner_hot = (paired[..., None] == slice_order).astype(jnp.int32)
    owner_dev = jnp.sum(owner_hot * jnp.arange(shards, dtype=jnp.int32), axis=-1)
    local_row = jnp.where(slice_ids < shards, 0, half_tok) + positions % half_tok
    return (owner_dev, local_row, owner_hot)


def halving_scatter(blocks, index, count, rider):
    remaining = count
    bit = 0
    while remaining > 1:
        lower = blocks.reshape((remaining // 2, 2) + blocks.shape[1:])
        mine = (index >> bit) & 1
        keep = jnp.where(mine == 0, lower[:, 0], lower[:, 1])
        give = jnp.where(mine == 0, lower[:, 1], lower[:, 0])
        arrived = swapped(give, "ctx", bit)
        if bit == 0:
            rider, arrived = lax.optimization_barrier((rider, arrived))
        blocks = keep + arrived
        remaining //= 2
        bit += 1
    return blocks[0], rider


def rotate_rows(values, positions):
    half_dim = values.shape[-1] // 2
    exponent = jnp.arange(half_dim, dtype=jnp.float32) * (-2.0 / values.shape[-1])
    frequency = jnp.power(jnp.float32(rope_base), exponent)
    angles = positions.astype(jnp.float32)[:, None] * frequency[None, :]
    cosine = jnp.cos(angles)
    sine_part = jnp.sin(angles)
    lead_half = values[..., :half_dim]
    tail_half = values[..., half_dim:]
    return jnp.concatenate(
        [lead_half * cosine - tail_half * sine_part, tail_half * cosine + lead_half * sine_part],
        axis=-1,
    )


def local(
    patch_rows,
    vit_gain,
    vit_bias,
    vit_qkv,
    vit_out,
    merge_gain,
    merge_bias,
    merge_weight,
    image_patches,
    window_ids,
    image_pos,
    slice_order,
    doc_ids,
    text_rows,
    norm_gain,
    w_query,
    w_keyval,
):
    shards = lax.axis_size("ctx")
    ctx_index = lax.axis_index("ctx")
    tp_index = lax.axis_index("tp")
    block_feats = merge_weight.shape[0]
    normed = layer_norm(patch_rows.astype(jnp.float32), vit_gain, vit_bias).astype(jnp.bfloat16)
    projected = jnp.einsum(
        "pf,fxhd->pxhd", normed, vit_qkv, preferred_element_type=jnp.float32
    ).astype(jnp.bfloat16)
    scores = jnp.einsum(
        "qhd,khd->hqk", projected[:, 0], projected[:, 1], preferred_element_type=jnp.float32
    ) / math.sqrt(VHD)
    allowed = window_ids[:, None] == window_ids[None, :]
    scores = jnp.where(allowed[None], scores, big_negative)
    powers = jnp.exp(scores - jnp.max(scores, axis=-1, keepdims=True))
    totals = jnp.sum(powers, axis=-1)
    blended = jnp.einsum(
        "hqk,khd->qhd",
        powers.astype(jnp.bfloat16),
        projected[:, 2],
        preferred_element_type=jnp.float32,
    )
    blended = (blended / jnp.transpose(totals)[:, :, None]).astype(jnp.bfloat16)
    branch_part = jnp.einsum("phd,hdf->pf", blended, vit_out, preferred_element_type=jnp.float32)
    own_positions = row_positions(
        ctx_index * TOK + jnp.arange(TOK, dtype=jnp.int32), slice_order, TOK
    )
    kv_heads = w_query.shape[1]
    groups = w_query.shape[2]

    def normalize(rows):
        full_rows = lax.all_gather(rows, ("vis", "tp"), axis=1, tiled=True)
        widened = full_rows.astype(jnp.float32)
        return (
            widened
            * lax.rsqrt(jnp.mean(widened * widened, axis=1, keepdims=True) + norm_eps)
            * norm_gain
        ).astype(jnp.bfloat16)

    def query_part(normed_rows, positions, weights):
        queries = jnp.einsum(
            "td,dhgk->thgk", normed_rows, weights, preferred_element_type=jnp.float32
        )
        return rotate(queries, positions).astype(jnp.bfloat16)

    def keyval_part(normed_rows, positions, weights):
        projected_half = jnp.einsum(
            "td,dhk->thk", normed_rows, weights, preferred_element_type=jnp.float32
        )
        return jnp.where(
            tp_index == 0, rotate(projected_half, positions), projected_half
        ).astype(jnp.bfloat16)

    def after(value, anchor):
        return lax.optimization_barrier((value, anchor))[0]

    text_normed = normalize(text_rows)
    from_tp = swapped(branch_part, "tp", 0)
    query_weights = after(w_query, from_tp)
    text_queries = query_part(text_normed, own_positions, query_weights)
    branch_sum = branch_part + from_tp
    from_vis = swapped(branch_sum, "vis", 0)
    text_queries, from_vis = lax.optimization_barrier((text_queries, from_vis))
    branch_sum = branch_sum + from_vis
    keyval_weights = after(w_keyval[0], from_vis)
    text_half = keyval_part(text_normed, own_positions, keyval_weights)
    hidden = patch_rows.astype(jnp.float32) + branch_sum
    merged = layer_norm(hidden, merge_gain, merge_bias).astype(jnp.bfloat16).reshape(ICAP, 4 * VD)
    send_each = ICAP // shards
    slot_ids = jnp.arange(ICAP, dtype=jnp.int32)
    shard_ids = jnp.arange(shards, dtype=jnp.int32)
    live_count = jnp.sum(image_patches, axis=1) // 4
    all_pos = image_pos.reshape(shards, ICAP)
    owner_dev, local_row, owner_hot = place_of(all_pos, slice_order, TOK)
    before = jnp.cumsum(owner_hot, axis=1) - owner_hot
    rank_in = jnp.sum(before * owner_hot, axis=-1)
    is_live = slot_ids[None, :] < live_count[:, None]
    own_hot = (shard_ids == ctx_index)[:, None]
    own_owner = jnp.sum(jnp.where(own_hot, owner_dev, 0), axis=0)
    own_rank = jnp.sum(jnp.where(own_hot, rank_in, 0), axis=0)
    target_slot = own_owner * send_each + own_rank
    picker = (target_slot[None, :] == slot_ids[:, None]).astype(jnp.bfloat16)
    ordered = jnp.dot(picker, merged, preferred_element_type=jnp.float32).astype(jnp.bfloat16)
    blocks = jnp.transpose(ordered.reshape(ICAP, shards, block_feats), (1, 0, 2))
    received = lax.all_to_all(blocks, "ctx", split_axis=0, concat_axis=0, tiled=True)
    by_dest = jnp.transpose(
        received.reshape(shards, shards, send_each, block_feats), (1, 0, 2, 3)
    ).reshape(shards * ICAP, block_feats)
    partial = jnp.dot(by_dest, merge_weight, preferred_element_type=jnp.float32)
    incoming, text_half = halving_scatter(
        partial.reshape(shards, ICAP, -1), ctx_index, shards, text_half
    )
    incoming = incoming.astype(jnp.bfloat16)
    mine_all = (owner_dev == ctx_index).reshape(-1)
    mine_live = mine_all & is_live.reshape(-1)
    column_of = (shard_ids[:, None] * send_each + rank_in).reshape(-1)
    row_hot = (
        (local_row.reshape(-1)[None, :] == jnp.arange(TOK, dtype=jnp.int32)[:, None])
        & mine_live[None, :]
    ).astype(jnp.bfloat16)
    column_match = column_of[:, None] == slot_ids[None, :]
    column_hot = column_match.astype(jnp.bfloat16)
    placing = jnp.dot(row_hot, column_hot, preferred_element_type=jnp.float32)
    is_image = jnp.sum(placing, axis=1) > 0.5
    placing = placing.astype(jnp.bfloat16)
    incoming_pos = jnp.sum(
        jnp.where(column_match & mine_all[:, None], image_pos[:, None], 0), axis=0
    )
    image_normed = normalize(incoming)
    image_queries = query_part(image_normed, incoming_pos, query_weights)
    image_half = keyval_part(image_normed, incoming_pos, keyval_weights)
    placed_queries = jnp.einsum(
        "tq,qhgk->thgk", placing, image_queries, preferred_element_type=jnp.float32
    ).astype(jnp.bfloat16)
    placed_half = jnp.einsum(
        "tq,qhk->thk", placing, image_half, preferred_element_type=jnp.float32
    ).astype(jnp.bfloat16)
    queries = jnp.where(is_image[:, None, None, None], placed_queries, text_queries)
    own_half = jnp.where(is_image[:, None, None], placed_half, text_half)
    doc_slices = doc_ids.reshape(2 * shards, TOK // 2)
    slice_ids = jnp.stack([slice_order, 2 * shards - 1 - slice_order], axis=1)
    slice_hot = slice_ids[:, :, None] == jnp.arange(2 * shards, dtype=jnp.int32)[None, None, :]
    key_doc = jnp.sum(
        jnp.where(slice_hot[..., None], doc_slices[None, None], 0), axis=2
    ).reshape(shards * TOK)
    own_doc = jnp.sum(
        jnp.where((shard_ids == ctx_index)[:, None], key_doc.reshape(shards, TOK), 0), axis=0
    )
    gathered = lax.all_gather(own_half, "ctx", axis=0, tiled=True)
    partner_all = swapped(gathered, "tp", 0)
    keys_every = jnp.where(tp_index == 0, gathered, partner_all)
    values_every = jnp.where(tp_index == 0, partner_all, gathered)
    key_count = keys_every.shape[0]
    key_pos = row_positions(jnp.arange(key_count, dtype=jnp.int32), slice_order, TOK)
    allowed_now = (key_pos[None, :] <= own_positions[:, None]) & (
        key_doc[None, :] == own_doc[:, None]
    )
    scores_now = jnp.einsum(
        "qkgd,nkd->kgqn", queries, keys_every, preferred_element_type=jnp.float32
    ) / math.sqrt(HD)
    scores_now = jnp.where(allowed_now[None, None], scores_now, big_negative)
    best = jnp.max(scores_now, axis=-1, keepdims=True)
    powers_now = jnp.exp(scores_now - best)
    total_final = jnp.sum(powers_now, axis=-1)
    accum_final = jnp.einsum(
        "kgqn,nkd->kgqd",
        powers_now.astype(jnp.bfloat16),
        values_every,
        preferred_element_type=jnp.float32,
    )
    result = accum_final / total_final[..., None]
    return (
        jnp.transpose(result, (2, 0, 1, 3)).reshape(TOK, kv_heads, groups * HD).astype(jnp.bfloat16)
    )


def solution(mesh):
    placed = (
        P("ctx", None),
        P(),
        P(),
        P(None, None, ("vis", "tp"), None),
        P(("vis", "tp"), None, None),
        P(),
        P(),
        P("ctx", ("vis", "tp")),
        P(),
        P("ctx"),
        P(),
        P(),
        P(),
        P("ctx", ("vis", "tp")),
        P(),
        P(None, "vis", "tp", None),
        P("tp", None, "vis", None),
    )
    return jax.shard_map(
        local, mesh=mesh, in_specs=placed, out_specs=P("ctx", "vis", "tp"), check_vma=False
    )
```

```python
import math

import jax
import jax.numpy as jnp
from jax import lax
from jax.sharding import PartitionSpec as P

D = 4096
HD = 128
VD = 1280
VHD = 80
TOK = 128
PCAP = 128
ICAP = 32


norm_eps = 1e-06
rope_base = 1000000.0
big_negative = -1e30


def swapped(value, axis, stride):
    return lax.ppermute(value, axis, [(i, i ^ 1 << stride) for i in range(lax.axis_size(axis))])


def layer_norm(values, scale_vec, shift_vec):
    centre = jnp.mean(values, axis=-1, keepdims=True)
    offset = values - centre
    spread = jnp.mean(offset * offset, axis=-1, keepdims=True)
    return offset * lax.rsqrt(spread + norm_eps) * scale_vec + shift_vec


def rotate(values, positions):
    half_dim = values.shape[-1] // 2
    exponent = jnp.arange(half_dim, dtype=jnp.float32) * (-2.0 / values.shape[-1])
    frequency = jnp.power(jnp.float32(rope_base), exponent)
    angles = positions.astype(jnp.float32)[:, None] * frequency[None, :]
    shape_out = (values.shape[0],) + (1,) * (values.ndim - 2) + (half_dim,)
    cosine = jnp.cos(angles).reshape(shape_out)
    sine_part = jnp.sin(angles).reshape(shape_out)
    lead_half = values[..., :half_dim]
    tail_half = values[..., half_dim:]
    return jnp.concatenate(
        [lead_half * cosine - tail_half * sine_part, tail_half * cosine + lead_half * sine_part],
        axis=-1,
    )


def row_positions(row_ids, slice_order, tokens_dev):
    shards = slice_order.shape[0]
    device_of = row_ids // tokens_dev
    local_row = row_ids % tokens_dev
    half_tok = tokens_dev // 2
    matches = device_of[:, None] == jnp.arange(shards, dtype=jnp.int32)[None, :]
    first_slice = jnp.sum(jnp.where(matches, slice_order[None, :], 0), axis=1)
    slice_ids = jnp.where(local_row < half_tok, first_slice, 2 * shards - 1 - first_slice)
    return slice_ids * half_tok + local_row % half_tok


def place_of(positions, slice_order, tokens_dev):
    shards = slice_order.shape[0]
    half_tok = tokens_dev // 2
    slice_ids = positions // half_tok
    paired = jnp.minimum(slice_ids, 2 * shards - 1 - slice_ids)
    owner_hot = (paired[..., None] == slice_order).astype(jnp.int32)
    owner_dev = jnp.sum(owner_hot * jnp.arange(shards, dtype=jnp.int32), axis=-1)
    local_row = jnp.where(slice_ids < shards, 0, half_tok) + positions % half_tok
    return (owner_dev, local_row, owner_hot)


def halving_scatter(blocks, index, count, rider):
    remaining = count
    bit = 0
    while remaining > 1:
        lower = blocks.reshape((remaining // 2, 2) + blocks.shape[1:])
        mine = (index >> bit) & 1
        keep = jnp.where(mine == 0, lower[:, 0], lower[:, 1])
        give = jnp.where(mine == 0, lower[:, 1], lower[:, 0])
        arrived = swapped(give, "ctx", bit)
        if bit == 0:
            rider, arrived = lax.optimization_barrier((rider, arrived))
        blocks = keep + arrived
        remaining //= 2
        bit += 1
    return blocks[0], rider


def doubling_gather(block, axis, index, count, bits):
    have = block[None]
    for bit in bits:
        arrived = swapped(have, axis, bit)
        mine = (index >> bit) & 1
        have = jnp.where(
            mine == 0,
            jnp.concatenate([have, arrived], axis=0),
            jnp.concatenate([arrived, have], axis=0),
        )
    order = list(bits)
    have = have.reshape((2,) * len(order) + block.shape)
    by_bit = {bit: len(order) - 1 - place for place, bit in enumerate(order)}
    wanted = [by_bit[bit] for bit in sorted(order, reverse=True)]
    have = jnp.transpose(have, wanted + list(range(len(order), have.ndim)))
    return have.reshape((count,) + block.shape)


def rotate_rows(values, positions):
    half_dim = values.shape[-1] // 2
    exponent = jnp.arange(half_dim, dtype=jnp.float32) * (-2.0 / values.shape[-1])
    frequency = jnp.power(jnp.float32(rope_base), exponent)
    angles = positions.astype(jnp.float32)[:, None] * frequency[None, :]
    cosine = jnp.cos(angles)
    sine_part = jnp.sin(angles)
    lead_half = values[..., :half_dim]
    tail_half = values[..., half_dim:]
    return jnp.concatenate(
        [lead_half * cosine - tail_half * sine_part, tail_half * cosine + lead_half * sine_part],
        axis=-1,
    )


def local(
    patch_rows,
    vit_gain,
    vit_bias,
    vit_qkv,
    vit_out,
    merge_gain,
    merge_bias,
    merge_weight,
    image_patches,
    window_ids,
    image_pos,
    slice_order,
    doc_ids,
    text_rows,
    norm_gain,
    w_query,
    w_keyval,
):
    shards = lax.axis_size("ctx")
    ctx_index = lax.axis_index("ctx")
    tp_index = lax.axis_index("tp")
    block_feats = merge_weight.shape[0]
    normed = layer_norm(patch_rows.astype(jnp.float32), vit_gain, vit_bias).astype(jnp.bfloat16)
    projected = jnp.einsum(
        "pf,fxhd->pxhd", normed, vit_qkv, preferred_element_type=jnp.float32
    ).astype(jnp.bfloat16)
    scores = jnp.einsum(
        "qhd,khd->hqk", projected[:, 0], projected[:, 1], preferred_element_type=jnp.float32
    ) / math.sqrt(VHD)
    allowed = window_ids[:, None] == window_ids[None, :]
    scores = jnp.where(allowed[None], scores, big_negative)
    powers = jnp.exp(scores - jnp.max(scores, axis=-1, keepdims=True))
    totals = jnp.sum(powers, axis=-1)
    blended = jnp.einsum(
        "hqk,khd->qhd",
        powers.astype(jnp.bfloat16),
        projected[:, 2],
        preferred_element_type=jnp.float32,
    )
    blended = (blended / jnp.transpose(totals)[:, :, None]).astype(jnp.bfloat16)
    branch_part = jnp.einsum("phd,hdf->pf", blended, vit_out, preferred_element_type=jnp.float32)
    own_positions = row_positions(
        ctx_index * TOK + jnp.arange(TOK, dtype=jnp.int32), slice_order, TOK
    )
    kv_heads = w_query.shape[1]
    groups = w_query.shape[2]

    def normalize(rows, by_swaps=False):
        if by_swaps:
            tp_size = lax.axis_size("tp")
            vis_size = lax.axis_size("vis")
            stacked = doubling_gather(
                rows, "tp", tp_index, tp_size, list(range(tp_size.bit_length() - 1))
            )
            stacked = doubling_gather(
                stacked,
                "vis",
                lax.axis_index("vis"),
                vis_size,
                list(range(vis_size.bit_length() - 1)),
            )
            full_rows = jnp.transpose(stacked, (2, 0, 1, 3)).reshape(rows.shape[0], -1)
        else:
            full_rows = lax.all_gather(rows, ("vis", "tp"), axis=1, tiled=True)
        widened = full_rows.astype(jnp.float32)
        return (
            widened
            * lax.rsqrt(jnp.mean(widened * widened, axis=1, keepdims=True) + norm_eps)
            * norm_gain
        ).astype(jnp.bfloat16)

    def query_part(normed_rows, positions, weights):
        queries = jnp.einsum(
            "td,dhgk->thgk", normed_rows, weights, preferred_element_type=jnp.float32
        )
        return rotate(queries, positions).astype(jnp.bfloat16)

    def keyval_part(normed_rows, positions, weights):
        projected_half = jnp.einsum(
            "td,dhk->thk", normed_rows, weights, preferred_element_type=jnp.float32
        )
        return jnp.where(
            tp_index == 0, rotate(projected_half, positions), projected_half
        ).astype(jnp.bfloat16)

    def after(value, anchor):
        return lax.optimization_barrier((value, anchor))[0]

    text_normed = normalize(text_rows)
    from_tp = swapped(branch_part, "tp", 0)
    query_weights = after(w_query, from_tp)
    text_queries = query_part(text_normed, own_positions, query_weights)
    branch_sum = branch_part + from_tp
    from_vis = swapped(branch_sum, "vis", 0)
    text_queries, from_vis = lax.optimization_barrier((text_queries, from_vis))
    branch_sum = branch_sum + from_vis
    keyval_weights = after(w_keyval[0], from_vis)
    text_half = keyval_part(text_normed, own_positions, keyval_weights)
    hidden = patch_rows.astype(jnp.float32) + branch_sum
    merged = layer_norm(hidden, merge_gain, merge_bias).astype(jnp.bfloat16).reshape(ICAP, 4 * VD)
    send_each = ICAP // shards
    slot_ids = jnp.arange(ICAP, dtype=jnp.int32)
    shard_ids = jnp.arange(shards, dtype=jnp.int32)
    live_count = jnp.sum(image_patches, axis=1) // 4
    all_pos = image_pos.reshape(shards, ICAP)
    owner_dev, local_row, owner_hot = place_of(all_pos, slice_order, TOK)
    before = jnp.cumsum(owner_hot, axis=1) - owner_hot
    rank_in = jnp.sum(before * owner_hot, axis=-1)
    is_live = slot_ids[None, :] < live_count[:, None]
    own_hot = (shard_ids == ctx_index)[:, None]
    own_owner = jnp.sum(jnp.where(own_hot, owner_dev, 0), axis=0)
    own_rank = jnp.sum(jnp.where(own_hot, rank_in, 0), axis=0)
    target_slot = own_owner * send_each + own_rank
    picker = (target_slot[None, :] == slot_ids[:, None]).astype(jnp.bfloat16)
    ordered = jnp.dot(picker, merged, preferred_element_type=jnp.float32).astype(jnp.bfloat16)
    blocks = jnp.transpose(ordered.reshape(ICAP, shards, block_feats), (1, 0, 2))
    received = lax.all_to_all(blocks, "ctx", split_axis=0, concat_axis=0, tiled=True)
    by_dest = jnp.transpose(
        received.reshape(shards, shards, send_each, block_feats), (1, 0, 2, 3)
    ).reshape(shards * ICAP, block_feats)
    partial = jnp.dot(by_dest, merge_weight, preferred_element_type=jnp.float32)
    incoming, text_half = halving_scatter(
        partial.reshape(shards, ICAP, -1), ctx_index, shards, text_half
    )
    incoming = incoming.astype(jnp.bfloat16)
    mine_all = (owner_dev == ctx_index).reshape(-1)
    mine_live = mine_all & is_live.reshape(-1)
    column_of = (shard_ids[:, None] * send_each + rank_in).reshape(-1)
    row_hot = (
        (local_row.reshape(-1)[None, :] == jnp.arange(TOK, dtype=jnp.int32)[:, None])
        & mine_live[None, :]
    ).astype(jnp.bfloat16)
    column_match = column_of[:, None] == slot_ids[None, :]
    column_hot = column_match.astype(jnp.bfloat16)
    placing = jnp.dot(row_hot, column_hot, preferred_element_type=jnp.float32)
    is_image = jnp.sum(placing, axis=1) > 0.5
    placing = placing.astype(jnp.bfloat16)
    incoming_pos = jnp.sum(
        jnp.where(column_match & mine_all[:, None], image_pos[:, None], 0), axis=0
    )
    image_normed = normalize(incoming, by_swaps=True)
    image_queries = query_part(image_normed, incoming_pos, query_weights)
    image_half = keyval_part(image_normed, incoming_pos, keyval_weights)
    placed_queries = jnp.einsum(
        "tq,qhgk->thgk", placing, image_queries, preferred_element_type=jnp.float32
    ).astype(jnp.bfloat16)
    placed_half = jnp.einsum(
        "tq,qhk->thk", placing, image_half, preferred_element_type=jnp.float32
    ).astype(jnp.bfloat16)
    queries = jnp.where(is_image[:, None, None, None], placed_queries, text_queries)
    own_half = jnp.where(is_image[:, None, None], placed_half, text_half)
    doc_slices = doc_ids.reshape(2 * shards, TOK // 2)
    slice_ids = jnp.stack([slice_order, 2 * shards - 1 - slice_order], axis=1)
    slice_hot = slice_ids[:, :, None] == jnp.arange(2 * shards, dtype=jnp.int32)[None, None, :]
    key_doc = jnp.sum(
        jnp.where(slice_hot[..., None], doc_slices[None, None], 0), axis=2
    ).reshape(shards * TOK)
    own_doc = jnp.sum(
        jnp.where((shard_ids == ctx_index)[:, None], key_doc.reshape(shards, TOK), 0), axis=0
    )
    ctx_bits = list(range(shards.bit_length() - 1))[::-1]
    gathered = doubling_gather(own_half, "ctx", ctx_index, shards, ctx_bits).reshape(
        (shards * TOK,) + own_half.shape[1:]
    )
    partner_all = swapped(gathered, "tp", 0)
    keys_every = jnp.where(tp_index == 0, gathered, partner_all)
    values_every = jnp.where(tp_index == 0, partner_all, gathered)
    key_count = keys_every.shape[0]
    key_pos = row_positions(jnp.arange(key_count, dtype=jnp.int32), slice_order, TOK)
    allowed_now = (key_pos[None, :] <= own_positions[:, None]) & (
        key_doc[None, :] == own_doc[:, None]
    )
    scores_now = jnp.einsum(
        "qkgd,nkd->kgqn", queries, keys_every, preferred_element_type=jnp.float32
    ) / math.sqrt(HD)
    scores_now = jnp.where(allowed_now[None, None], scores_now, big_negative)
    best = jnp.max(scores_now, axis=-1, keepdims=True)
    powers_now = jnp.exp(scores_now - best)
    total_final = jnp.sum(powers_now, axis=-1)
    accum_final = jnp.einsum(
        "kgqn,nkd->kgqd",
        powers_now.astype(jnp.bfloat16),
        values_every,
        preferred_element_type=jnp.float32,
    )
    result = accum_final / total_final[..., None]
    return (
        jnp.transpose(result, (2, 0, 1, 3)).reshape(TOK, kv_heads, groups * HD).astype(jnp.bfloat16)
    )


def solution(mesh):
    placed = (
        P("ctx", None),
        P(),
        P(),
        P(None, None, ("vis", "tp"), None),
        P(("vis", "tp"), None, None),
        P(),
        P(),
        P("ctx", ("vis", "tp")),
        P(),
        P("ctx"),
        P(),
        P(),
        P(),
        P("ctx", ("vis", "tp")),
        P(),
        P(None, "vis", "tp", None),
        P("tp", None, "vis", None),
    )
    return jax.shard_map(
        local, mesh=mesh, in_specs=placed, out_specs=P("ctx", "vis", "tp"), check_vma=False
    )
```

```python
import math

import jax
import jax.numpy as jnp
from jax import lax
from jax.sharding import PartitionSpec as P

D = 4096
HD = 128
VD = 1280
VHD = 80
TOK = 128
PCAP = 128
ICAP = 32


norm_eps = 1e-06
rope_base = 1000000.0
big_negative = -1e30


def swapped(value, axis, stride):
    return lax.ppermute(value, axis, [(i, i ^ 1 << stride) for i in range(lax.axis_size(axis))])


def layer_norm(values, scale_vec, shift_vec):
    centre = jnp.mean(values, axis=-1, keepdims=True)
    offset = values - centre
    spread = jnp.mean(offset * offset, axis=-1, keepdims=True)
    return offset * lax.rsqrt(spread + norm_eps) * scale_vec + shift_vec


def rotate(values, positions):
    half_dim = values.shape[-1] // 2
    exponent = jnp.arange(half_dim, dtype=jnp.float32) * (-2.0 / values.shape[-1])
    frequency = jnp.power(jnp.float32(rope_base), exponent)
    angles = positions.astype(jnp.float32)[:, None] * frequency[None, :]
    shape_out = (values.shape[0],) + (1,) * (values.ndim - 2) + (half_dim,)
    cosine = jnp.cos(angles).reshape(shape_out)
    sine_part = jnp.sin(angles).reshape(shape_out)
    lead_half = values[..., :half_dim]
    tail_half = values[..., half_dim:]
    return jnp.concatenate(
        [lead_half * cosine - tail_half * sine_part, tail_half * cosine + lead_half * sine_part],
        axis=-1,
    )


def row_positions(row_ids, slice_order, tokens_dev):
    shards = slice_order.shape[0]
    device_of = row_ids // tokens_dev
    local_row = row_ids % tokens_dev
    half_tok = tokens_dev // 2
    matches = device_of[:, None] == jnp.arange(shards, dtype=jnp.int32)[None, :]
    first_slice = jnp.sum(jnp.where(matches, slice_order[None, :], 0), axis=1)
    slice_ids = jnp.where(local_row < half_tok, first_slice, 2 * shards - 1 - first_slice)
    return slice_ids * half_tok + local_row % half_tok


def place_of(positions, slice_order, tokens_dev):
    shards = slice_order.shape[0]
    half_tok = tokens_dev // 2
    slice_ids = positions // half_tok
    paired = jnp.minimum(slice_ids, 2 * shards - 1 - slice_ids)
    owner_hot = (paired[..., None] == slice_order).astype(jnp.int32)
    owner_dev = jnp.sum(owner_hot * jnp.arange(shards, dtype=jnp.int32), axis=-1)
    local_row = jnp.where(slice_ids < shards, 0, half_tok) + positions % half_tok
    return (owner_dev, local_row, owner_hot)


def halving_scatter(blocks, index, count):
    remaining = count
    bit = 0
    while remaining > 1:
        lower = blocks.reshape((remaining // 2, 2) + blocks.shape[1:])
        mine = (index >> bit) & 1
        keep = jnp.where(mine == 0, lower[:, 0], lower[:, 1])
        give = jnp.where(mine == 0, lower[:, 1], lower[:, 0])
        blocks = keep + swapped(give, "ctx", bit)
        remaining //= 2
        bit += 1
    return blocks[0]


def doubling_gather(block, axis, index, count, bits):
    have = block[None]
    for bit in bits:
        arrived = swapped(have, axis, bit)
        mine = (index >> bit) & 1
        have = jnp.where(
            mine == 0,
            jnp.concatenate([have, arrived], axis=0),
            jnp.concatenate([arrived, have], axis=0),
        )
    order = list(bits)
    have = have.reshape((2,) * len(order) + block.shape)
    by_bit = {bit: len(order) - 1 - place for place, bit in enumerate(order)}
    wanted = [by_bit[bit] for bit in sorted(order, reverse=True)]
    have = jnp.transpose(have, wanted + list(range(len(order), have.ndim)))
    return have.reshape((count,) + block.shape)


def rotate_rows(values, positions):
    half_dim = values.shape[-1] // 2
    exponent = jnp.arange(half_dim, dtype=jnp.float32) * (-2.0 / values.shape[-1])
    frequency = jnp.power(jnp.float32(rope_base), exponent)
    angles = positions.astype(jnp.float32)[:, None] * frequency[None, :]
    cosine = jnp.cos(angles)
    sine_part = jnp.sin(angles)
    lead_half = values[..., :half_dim]
    tail_half = values[..., half_dim:]
    return jnp.concatenate(
        [lead_half * cosine - tail_half * sine_part, tail_half * cosine + lead_half * sine_part],
        axis=-1,
    )


def local(
    patch_rows,
    vit_gain,
    vit_bias,
    vit_qkv,
    vit_out,
    merge_gain,
    merge_bias,
    merge_weight,
    image_patches,
    window_ids,
    image_pos,
    slice_order,
    doc_ids,
    text_rows,
    norm_gain,
    w_query,
    w_keyval,
):
    shards = lax.axis_size("ctx")
    ctx_index = lax.axis_index("ctx")
    tp_index = lax.axis_index("tp")
    block_feats = merge_weight.shape[0]
    normed = layer_norm(patch_rows.astype(jnp.float32), vit_gain, vit_bias).astype(jnp.bfloat16)
    projected = jnp.einsum(
        "pf,fxhd->pxhd", normed, vit_qkv, preferred_element_type=jnp.float32
    ).astype(jnp.bfloat16)
    scores = jnp.einsum(
        "qhd,khd->hqk", projected[:, 0], projected[:, 1], preferred_element_type=jnp.float32
    ) / math.sqrt(VHD)
    allowed = window_ids[:, None] == window_ids[None, :]
    scores = jnp.where(allowed[None], scores, big_negative)
    powers = jnp.exp(scores - jnp.max(scores, axis=-1, keepdims=True))
    totals = jnp.sum(powers, axis=-1)
    blended = jnp.einsum(
        "hqk,khd->qhd",
        powers.astype(jnp.bfloat16),
        projected[:, 2],
        preferred_element_type=jnp.float32,
    )
    blended = (blended / jnp.transpose(totals)[:, :, None]).astype(jnp.bfloat16)
    branch_part = jnp.einsum("phd,hdf->pf", blended, vit_out, preferred_element_type=jnp.float32)
    branch_sum = branch_part + swapped(branch_part, "tp", 0)
    branch_sum = branch_sum + swapped(branch_sum, "vis", 0)
    hidden = patch_rows.astype(jnp.float32) + branch_sum
    merged = layer_norm(hidden, merge_gain, merge_bias).astype(jnp.bfloat16).reshape(ICAP, 4 * VD)
    send_each = ICAP // shards
    slot_ids = jnp.arange(ICAP, dtype=jnp.int32)
    shard_ids = jnp.arange(shards, dtype=jnp.int32)
    live_count = jnp.sum(image_patches, axis=1) // 4
    all_pos = image_pos.reshape(shards, ICAP)
    owner_dev, local_row, owner_hot = place_of(all_pos, slice_order, TOK)
    before = jnp.cumsum(owner_hot, axis=1) - owner_hot
    rank_in = jnp.sum(before * owner_hot, axis=-1)
    is_live = slot_ids[None, :] < live_count[:, None]
    own_hot = (shard_ids == ctx_index)[:, None]
    own_owner = jnp.sum(jnp.where(own_hot, owner_dev, 0), axis=0)
    own_rank = jnp.sum(jnp.where(own_hot, rank_in, 0), axis=0)
    target_slot = own_owner * send_each + own_rank
    picker = (target_slot[None, :] == slot_ids[:, None]).astype(jnp.bfloat16)
    ordered = jnp.dot(picker, merged, preferred_element_type=jnp.float32).astype(jnp.bfloat16)
    blocks = jnp.transpose(ordered.reshape(ICAP, shards, block_feats), (1, 0, 2))
    received = lax.all_to_all(blocks, "ctx", split_axis=0, concat_axis=0, tiled=True)
    by_dest = jnp.transpose(
        received.reshape(shards, shards, send_each, block_feats), (1, 0, 2, 3)
    ).reshape(shards * ICAP, block_feats)
    partial = jnp.dot(by_dest, merge_weight, preferred_element_type=jnp.float32)
    incoming = halving_scatter(partial.reshape(shards, ICAP, -1), ctx_index, shards).astype(
        jnp.bfloat16
    )
    mine_live = ((owner_dev == ctx_index) & is_live).reshape(-1)
    column_of = (shard_ids[:, None] * send_each + rank_in).reshape(-1)
    row_hot = (
        (local_row.reshape(-1)[None, :] == jnp.arange(TOK, dtype=jnp.int32)[:, None])
        & mine_live[None, :]
    ).astype(jnp.bfloat16)
    column_hot = (column_of[:, None] == slot_ids[None, :]).astype(jnp.bfloat16)
    placing = jnp.dot(row_hot, column_hot, preferred_element_type=jnp.float32)
    is_image = jnp.sum(placing, axis=1) > 0.5
    image_part = jnp.dot(placing.astype(jnp.bfloat16), incoming, preferred_element_type=jnp.float32)
    embeds = jnp.where(is_image[:, None], image_part.astype(jnp.bfloat16), text_rows)
    full_rows = lax.all_gather(embeds, ("vis", "tp"), axis=1, tiled=True)
    widened = full_rows.astype(jnp.float32)
    normed_rows = (
        widened
        * lax.rsqrt(jnp.mean(widened * widened, axis=1, keepdims=True) + norm_eps)
        * norm_gain
    ).astype(jnp.bfloat16)
    own_positions = row_positions(
        ctx_index * TOK + jnp.arange(TOK, dtype=jnp.int32), slice_order, TOK
    )
    kv_heads = w_query.shape[1]
    groups = w_query.shape[2]
    queries = jnp.einsum(
        "td,dhgk->thgk", normed_rows, w_query, preferred_element_type=jnp.float32
    )
    queries = rotate(queries, own_positions).astype(jnp.bfloat16)
    projected_half = jnp.einsum(
        "td,dhk->thk", normed_rows, w_keyval[0], preferred_element_type=jnp.float32
    )
    own_half = jnp.where(
        tp_index == 0, rotate(projected_half, own_positions), projected_half
    ).astype(jnp.bfloat16)
    ctx_bits = list(range(shards.bit_length() - 1))[::-1]
    gathered = doubling_gather(own_half, "ctx", ctx_index, shards, ctx_bits).reshape(
        (shards * TOK,) + own_half.shape[1:]
    )
    partner_all = swapped(gathered, "tp", 0)
    keys_every = jnp.where(tp_index == 0, gathered, partner_all)
    values_every = jnp.where(tp_index == 0, partner_all, gathered)
    key_count = keys_every.shape[0]
    key_pos = row_positions(jnp.arange(key_count, dtype=jnp.int32), slice_order, TOK)
    doc_slices = doc_ids.reshape(2 * shards, TOK // 2)
    slice_ids = jnp.stack([slice_order, 2 * shards - 1 - slice_order], axis=1)
    slice_hot = slice_ids[:, :, None] == jnp.arange(2 * shards, dtype=jnp.int32)[None, None, :]
    key_doc = jnp.sum(
        jnp.where(slice_hot[..., None], doc_slices[None, None], 0), axis=2
    ).reshape(shards * TOK)
    own_doc = jnp.sum(
        jnp.where((shard_ids == ctx_index)[:, None], key_doc.reshape(shards, TOK), 0), axis=0
    )
    allowed_now = (key_pos[None, :] <= own_positions[:, None]) & (
        key_doc[None, :] == own_doc[:, None]
    )
    scores_now = jnp.einsum(
        "qkgd,nkd->kgqn", queries, keys_every, preferred_element_type=jnp.float32
    ) / math.sqrt(HD)
    scores_now = jnp.where(allowed_now[None, None], scores_now, big_negative)
    best = jnp.max(scores_now, axis=-1, keepdims=True)
    powers_now = jnp.exp(scores_now - best)
    total_final = jnp.sum(powers_now, axis=-1)
    accum_final = jnp.einsum(
        "kgqn,nkd->kgqd",
        powers_now.astype(jnp.bfloat16),
        values_every,
        preferred_element_type=jnp.float32,
    )
    result = accum_final / total_final[..., None]
    return (
        jnp.transpose(result, (2, 0, 1, 3)).reshape(TOK, kv_heads, groups * HD).astype(jnp.bfloat16)
    )


def solution(mesh):
    placed = (
        P("ctx", None),
        P(),
        P(),
        P(None, None, ("vis", "tp"), None),
        P(("vis", "tp"), None, None),
        P(),
        P(),
        P("ctx", ("vis", "tp")),
        P(),
        P("ctx"),
        P(),
        P(),
        P(),
        P("ctx", ("vis", "tp")),
        P(),
        P(None, "vis", "tp", None),
        P("tp", None, "vis", None),
    )
    return jax.shard_map(
        local, mesh=mesh, in_specs=placed, out_specs=P("ctx", "vis", "tp"), check_vma=False
    )
```

```python
import math

import jax
import jax.numpy as jnp
from jax import lax
from jax.sharding import PartitionSpec as P

D = 4096
HD = 128
VD = 1280
VHD = 80
TOK = 128
PCAP = 128
ICAP = 32


norm_eps = 1e-06
rope_base = 1000000.0
big_negative = -1e30


def swapped(value, axis, stride):
    return lax.ppermute(value, axis, [(i, i ^ 1 << stride) for i in range(lax.axis_size(axis))])


def layer_norm(values, scale_vec, shift_vec):
    centre = jnp.mean(values, axis=-1, keepdims=True)
    offset = values - centre
    spread = jnp.mean(offset * offset, axis=-1, keepdims=True)
    return offset * lax.rsqrt(spread + norm_eps) * scale_vec + shift_vec


def rotate(values, positions):
    half_dim = values.shape[-1] // 2
    exponent = jnp.arange(half_dim, dtype=jnp.float32) * (-2.0 / values.shape[-1])
    frequency = jnp.power(jnp.float32(rope_base), exponent)
    angles = positions.astype(jnp.float32)[:, None] * frequency[None, :]
    shape_out = (values.shape[0],) + (1,) * (values.ndim - 2) + (half_dim,)
    cosine = jnp.cos(angles).reshape(shape_out)
    sine_part = jnp.sin(angles).reshape(shape_out)
    lead_half = values[..., :half_dim]
    tail_half = values[..., half_dim:]
    return jnp.concatenate(
        [lead_half * cosine - tail_half * sine_part, tail_half * cosine + lead_half * sine_part],
        axis=-1,
    )


def row_positions(row_ids, slice_order, tokens_dev):
    shards = slice_order.shape[0]
    device_of = row_ids // tokens_dev
    local_row = row_ids % tokens_dev
    half_tok = tokens_dev // 2
    matches = device_of[:, None] == jnp.arange(shards, dtype=jnp.int32)[None, :]
    first_slice = jnp.sum(jnp.where(matches, slice_order[None, :], 0), axis=1)
    slice_ids = jnp.where(local_row < half_tok, first_slice, 2 * shards - 1 - first_slice)
    return slice_ids * half_tok + local_row % half_tok


def place_of(positions, slice_order, tokens_dev):
    shards = slice_order.shape[0]
    half_tok = tokens_dev // 2
    slice_ids = positions // half_tok
    paired = jnp.minimum(slice_ids, 2 * shards - 1 - slice_ids)
    owner_hot = (paired[..., None] == slice_order).astype(jnp.int32)
    owner_dev = jnp.sum(owner_hot * jnp.arange(shards, dtype=jnp.int32), axis=-1)
    local_row = jnp.where(slice_ids < shards, 0, half_tok) + positions % half_tok
    return (owner_dev, local_row, owner_hot)


def halving_scatter(blocks, index, count):
    remaining = count
    bit = 0
    while remaining > 1:
        lower = blocks.reshape((remaining // 2, 2) + blocks.shape[1:])
        mine = (index >> bit) & 1
        keep = jnp.where(mine == 0, lower[:, 0], lower[:, 1])
        give = jnp.where(mine == 0, lower[:, 1], lower[:, 0])
        blocks = keep + swapped(give, "ctx", bit)
        remaining //= 2
        bit += 1
    return blocks[0]


def doubling_gather(block, axis, index, count, bits):
    have = block[None]
    for bit in bits:
        arrived = swapped(have, axis, bit)
        mine = (index >> bit) & 1
        have = jnp.where(
            mine == 0,
            jnp.concatenate([have, arrived], axis=0),
            jnp.concatenate([arrived, have], axis=0),
        )
    order = list(bits)
    have = have.reshape((2,) * len(order) + block.shape)
    by_bit = {bit: len(order) - 1 - place for place, bit in enumerate(order)}
    wanted = [by_bit[bit] for bit in sorted(order, reverse=True)]
    have = jnp.transpose(have, wanted + list(range(len(order), have.ndim)))
    return have.reshape((count,) + block.shape)


def rotate_rows(values, positions):
    half_dim = values.shape[-1] // 2
    exponent = jnp.arange(half_dim, dtype=jnp.float32) * (-2.0 / values.shape[-1])
    frequency = jnp.power(jnp.float32(rope_base), exponent)
    angles = positions.astype(jnp.float32)[:, None] * frequency[None, :]
    cosine = jnp.cos(angles)
    sine_part = jnp.sin(angles)
    lead_half = values[..., :half_dim]
    tail_half = values[..., half_dim:]
    return jnp.concatenate(
        [lead_half * cosine - tail_half * sine_part, tail_half * cosine + lead_half * sine_part],
        axis=-1,
    )


def local(
    patch_rows,
    vit_gain,
    vit_bias,
    vit_qkv,
    vit_out,
    merge_gain,
    merge_bias,
    merge_weight,
    image_patches,
    window_ids,
    image_pos,
    slice_order,
    doc_ids,
    text_rows,
    norm_gain,
    w_query,
    w_keyval,
):
    shards = lax.axis_size("ctx")
    ctx_index = lax.axis_index("ctx")
    tp_index = lax.axis_index("tp")
    block_feats = merge_weight.shape[0]
    normed = layer_norm(patch_rows.astype(jnp.float32), vit_gain, vit_bias).astype(jnp.bfloat16)
    projected = jnp.einsum(
        "pf,fxhd->pxhd", normed, vit_qkv, preferred_element_type=jnp.float32
    ).astype(jnp.bfloat16)
    scores = jnp.einsum(
        "qhd,khd->hqk", projected[:, 0], projected[:, 1], preferred_element_type=jnp.float32
    ) / math.sqrt(VHD)
    allowed = window_ids[:, None] == window_ids[None, :]
    scores = jnp.where(allowed[None], scores, big_negative)
    powers = jnp.exp(scores - jnp.max(scores, axis=-1, keepdims=True))
    totals = jnp.sum(powers, axis=-1)
    blended = jnp.einsum(
        "hqk,khd->qhd",
        powers.astype(jnp.bfloat16),
        projected[:, 2],
        preferred_element_type=jnp.float32,
    )
    blended = (blended / jnp.transpose(totals)[:, :, None]).astype(jnp.bfloat16)
    branch_part = jnp.einsum("phd,hdf->pf", blended, vit_out, preferred_element_type=jnp.float32)
    own_positions = row_positions(
        ctx_index * TOK + jnp.arange(TOK, dtype=jnp.int32), slice_order, TOK
    )

    def keyval_part(normed_part, positions):
        projected_half = jnp.einsum(
            "td,dhk->thk", normed_part, w_keyval[0], preferred_element_type=jnp.float32
        )
        return jnp.where(
            tp_index == 0, rotate(projected_half, positions), projected_half
        ).astype(jnp.bfloat16)

    text_wide = lax.all_gather(text_rows, ("vis", "tp"), axis=1, tiled=True).astype(jnp.float32)
    text_normed = (
        text_wide
        * lax.rsqrt(jnp.mean(text_wide * text_wide, axis=1, keepdims=True) + norm_eps)
        * norm_gain
    ).astype(jnp.bfloat16)
    text_half = keyval_part(text_normed, own_positions)
    branch_sum = branch_part + swapped(branch_part, "tp", 0)
    branch_sum = branch_sum + swapped(branch_sum, "vis", 0)
    hidden = patch_rows.astype(jnp.float32) + branch_sum
    merged = layer_norm(hidden, merge_gain, merge_bias).astype(jnp.bfloat16).reshape(ICAP, 4 * VD)
    send_each = ICAP // shards
    slot_ids = jnp.arange(ICAP, dtype=jnp.int32)
    shard_ids = jnp.arange(shards, dtype=jnp.int32)
    live_count = jnp.sum(image_patches, axis=1) // 4
    all_pos = image_pos.reshape(shards, ICAP)
    owner_dev, local_row, owner_hot = place_of(all_pos, slice_order, TOK)
    before = jnp.cumsum(owner_hot, axis=1) - owner_hot
    rank_in = jnp.sum(before * owner_hot, axis=-1)
    is_live = slot_ids[None, :] < live_count[:, None]
    own_hot = (shard_ids == ctx_index)[:, None]
    own_owner = jnp.sum(jnp.where(own_hot, owner_dev, 0), axis=0)
    own_rank = jnp.sum(jnp.where(own_hot, rank_in, 0), axis=0)
    target_slot = own_owner * send_each + own_rank
    picker = (target_slot[None, :] == slot_ids[:, None]).astype(jnp.bfloat16)
    ordered = jnp.dot(picker, merged, preferred_element_type=jnp.float32).astype(jnp.bfloat16)
    blocks = jnp.transpose(ordered.reshape(ICAP, shards, block_feats), (1, 0, 2))
    received = lax.all_to_all(blocks, "ctx", split_axis=0, concat_axis=0, tiled=True)
    text_half, received = lax.optimization_barrier((text_half, received))
    text_all = lax.all_gather(text_half, "ctx", axis=0, tiled=True)
    by_dest = jnp.transpose(
        received.reshape(shards, shards, send_each, block_feats), (1, 0, 2, 3)
    ).reshape(shards * ICAP, block_feats)
    partial = jnp.dot(by_dest, merge_weight, preferred_element_type=jnp.float32)
    incoming = halving_scatter(partial.reshape(shards, ICAP, -1), ctx_index, shards).astype(
        jnp.bfloat16
    )
    text_all, incoming = lax.optimization_barrier((text_all, incoming))
    mine_live = ((owner_dev == ctx_index) & is_live).reshape(-1)
    column_of = (shard_ids[:, None] * send_each + rank_in).reshape(-1)
    row_hot = (
        (local_row.reshape(-1)[None, :] == jnp.arange(TOK, dtype=jnp.int32)[:, None])
        & mine_live[None, :]
    ).astype(jnp.bfloat16)
    column_hot = (column_of[:, None] == slot_ids[None, :]).astype(jnp.bfloat16)
    placing = jnp.dot(row_hot, column_hot, preferred_element_type=jnp.float32)
    is_image = jnp.sum(placing, axis=1) > 0.5
    placing = placing.astype(jnp.bfloat16)
    image_part = jnp.dot(placing, incoming, preferred_element_type=jnp.float32)
    embeds = jnp.where(is_image[:, None], image_part.astype(jnp.bfloat16), text_rows)
    full_rows = lax.all_gather(embeds, ("vis", "tp"), axis=1, tiled=True)
    widened = full_rows.astype(jnp.float32)
    normed_rows = (
        widened
        * lax.rsqrt(jnp.mean(widened * widened, axis=1, keepdims=True) + norm_eps)
        * norm_gain
    ).astype(jnp.bfloat16)
    kv_heads = w_query.shape[1]
    groups = w_query.shape[2]
    queries = jnp.einsum(
        "td,dhgk->thgk", normed_rows, w_query, preferred_element_type=jnp.float32
    )
    queries = rotate(queries, own_positions).astype(jnp.bfloat16)
    image_normed = jnp.einsum(
        "tq,td->qd", placing, normed_rows, preferred_element_type=jnp.float32
    ).astype(jnp.bfloat16)
    mine_all = (owner_dev == ctx_index).reshape(-1)
    incoming_pos = jnp.sum(
        jnp.where((column_of[:, None] == slot_ids[None, :]) & mine_all[:, None], image_pos[:, None], 0),
        axis=0,
    )
    image_half = keyval_part(image_normed, incoming_pos)
    ctx_bits = list(range(shards.bit_length() - 1))[::-1]
    image_all = doubling_gather(image_half, "ctx", ctx_index, shards, ctx_bits).reshape(
        shards * ICAP, -1
    )
    slot_row = (owner_dev * TOK + local_row).reshape(-1)
    slot_col = (owner_dev * ICAP + column_of.reshape(shards, ICAP)).reshape(-1)
    key_rows = jnp.arange(shards * TOK, dtype=jnp.int32)
    all_cols = jnp.arange(shards * ICAP, dtype=jnp.int32)
    global_rows = (
        (slot_row[None, :] == key_rows[:, None]) & is_live.reshape(-1)[None, :]
    ).astype(jnp.bfloat16)
    global_cols = (slot_col[:, None] == all_cols[None, :]).astype(jnp.bfloat16)
    global_place = jnp.dot(global_rows, global_cols, preferred_element_type=jnp.float32)
    is_image_key = jnp.sum(global_place, axis=1) > 0.5
    placed_all = jnp.dot(
        global_place.astype(jnp.bfloat16), image_all, preferred_element_type=jnp.float32
    ).astype(jnp.bfloat16)
    gathered = jnp.where(
        is_image_key[:, None, None], placed_all.reshape(text_all.shape), text_all
    )
    partner_all = swapped(gathered, "tp", 0)
    keys_every = jnp.where(tp_index == 0, gathered, partner_all)
    values_every = jnp.where(tp_index == 0, partner_all, gathered)
    key_count = keys_every.shape[0]
    key_pos = row_positions(jnp.arange(key_count, dtype=jnp.int32), slice_order, TOK)
    doc_slices = doc_ids.reshape(2 * shards, TOK // 2)
    slice_ids = jnp.stack([slice_order, 2 * shards - 1 - slice_order], axis=1)
    slice_hot = slice_ids[:, :, None] == jnp.arange(2 * shards, dtype=jnp.int32)[None, None, :]
    key_doc = jnp.sum(
        jnp.where(slice_hot[..., None], doc_slices[None, None], 0), axis=2
    ).reshape(shards * TOK)
    own_doc = jnp.sum(
        jnp.where((shard_ids == ctx_index)[:, None], key_doc.reshape(shards, TOK), 0), axis=0
    )
    allowed_now = (key_pos[None, :] <= own_positions[:, None]) & (
        key_doc[None, :] == own_doc[:, None]
    )
    scores_now = jnp.einsum(
        "qkgd,nkd->kgqn", queries, keys_every, preferred_element_type=jnp.float32
    ) / math.sqrt(HD)
    scores_now = jnp.where(allowed_now[None, None], scores_now, big_negative)
    best = jnp.max(scores_now, axis=-1, keepdims=True)
    powers_now = jnp.exp(scores_now - best)
    total_final = jnp.sum(powers_now, axis=-1)
    accum_final = jnp.einsum(
        "kgqn,nkd->kgqd",
        powers_now.astype(jnp.bfloat16),
        values_every,
        preferred_element_type=jnp.float32,
    )
    result = accum_final / total_final[..., None]
    return (
        jnp.transpose(result, (2, 0, 1, 3)).reshape(TOK, kv_heads, groups * HD).astype(jnp.bfloat16)
    )


def solution(mesh):
    placed = (
        P("ctx", None),
        P(),
        P(),
        P(None, None, ("vis", "tp"), None),
        P(("vis", "tp"), None, None),
        P(),
        P(),
        P("ctx", ("vis", "tp")),
        P(),
        P("ctx"),
        P(),
        P(),
        P(),
        P("ctx", ("vis", "tp")),
        P(),
        P(None, "vis", "tp", None),
        P("tp", None, "vis", None),
    )
    return jax.shard_map(
        local, mesh=mesh, in_specs=placed, out_specs=P("ctx", "vis", "tp"), check_vma=False
    )
```

```python
import math

import jax
import jax.numpy as jnp
from jax import lax
from jax.sharding import PartitionSpec as P

D = 4096
HD = 128
VD = 1280
VHD = 80
TOK = 128
PCAP = 128
ICAP = 32


norm_eps = 1e-06
rope_base = 1000000.0
big_negative = -1e30


def swapped(value, axis, stride):
    return lax.ppermute(value, axis, [(i, i ^ 1 << stride) for i in range(lax.axis_size(axis))])


def layer_norm(values, scale_vec, shift_vec):
    centre = jnp.mean(values, axis=-1, keepdims=True)
    offset = values - centre
    spread = jnp.mean(offset * offset, axis=-1, keepdims=True)
    return offset * lax.rsqrt(spread + norm_eps) * scale_vec + shift_vec


def rotate(values, positions):
    half_dim = values.shape[-1] // 2
    exponent = jnp.arange(half_dim, dtype=jnp.float32) * (-2.0 / values.shape[-1])
    frequency = jnp.power(jnp.float32(rope_base), exponent)
    angles = positions.astype(jnp.float32)[:, None] * frequency[None, :]
    shape_out = (values.shape[0],) + (1,) * (values.ndim - 2) + (half_dim,)
    cosine = jnp.cos(angles).reshape(shape_out)
    sine_part = jnp.sin(angles).reshape(shape_out)
    lead_half = values[..., :half_dim]
    tail_half = values[..., half_dim:]
    return jnp.concatenate(
        [lead_half * cosine - tail_half * sine_part, tail_half * cosine + lead_half * sine_part],
        axis=-1,
    )


def row_positions(row_ids, slice_order, tokens_dev):
    shards = slice_order.shape[0]
    device_of = row_ids // tokens_dev
    local_row = row_ids % tokens_dev
    half_tok = tokens_dev // 2
    matches = device_of[:, None] == jnp.arange(shards, dtype=jnp.int32)[None, :]
    first_slice = jnp.sum(jnp.where(matches, slice_order[None, :], 0), axis=1)
    slice_ids = jnp.where(local_row < half_tok, first_slice, 2 * shards - 1 - first_slice)
    return slice_ids * half_tok + local_row % half_tok


def place_of(positions, slice_order, tokens_dev):
    shards = slice_order.shape[0]
    half_tok = tokens_dev // 2
    slice_ids = positions // half_tok
    paired = jnp.minimum(slice_ids, 2 * shards - 1 - slice_ids)
    owner_hot = (paired[..., None] == slice_order).astype(jnp.int32)
    owner_dev = jnp.sum(owner_hot * jnp.arange(shards, dtype=jnp.int32), axis=-1)
    local_row = jnp.where(slice_ids < shards, 0, half_tok) + positions % half_tok
    return (owner_dev, local_row, owner_hot)


def halving_scatter(blocks, index, count, axis="ctx"):
    remaining = count
    bit = 0
    while remaining > 1:
        lower = blocks.reshape((remaining // 2, 2) + blocks.shape[1:])
        mine = (index >> bit) & 1
        keep = jnp.where(mine == 0, lower[:, 0], lower[:, 1])
        give = jnp.where(mine == 0, lower[:, 1], lower[:, 0])
        blocks = keep + swapped(give, axis, bit)
        remaining //= 2
        bit += 1
    return blocks[0]


def doubling_gather(block, axis, index, count, bits):
    have = block[None]
    for bit in bits:
        arrived = swapped(have, axis, bit)
        mine = (index >> bit) & 1
        have = jnp.where(
            mine == 0,
            jnp.concatenate([have, arrived], axis=0),
            jnp.concatenate([arrived, have], axis=0),
        )
    order = list(bits)
    have = have.reshape((2,) * len(order) + block.shape)
    by_bit = {bit: len(order) - 1 - place for place, bit in enumerate(order)}
    wanted = [by_bit[bit] for bit in sorted(order, reverse=True)]
    have = jnp.transpose(have, wanted + list(range(len(order), have.ndim)))
    return have.reshape((count,) + block.shape)


def rotate_rows(values, positions):
    half_dim = values.shape[-1] // 2
    exponent = jnp.arange(half_dim, dtype=jnp.float32) * (-2.0 / values.shape[-1])
    frequency = jnp.power(jnp.float32(rope_base), exponent)
    angles = positions.astype(jnp.float32)[:, None] * frequency[None, :]
    cosine = jnp.cos(angles)
    sine_part = jnp.sin(angles)
    lead_half = values[..., :half_dim]
    tail_half = values[..., half_dim:]
    return jnp.concatenate(
        [lead_half * cosine - tail_half * sine_part, tail_half * cosine + lead_half * sine_part],
        axis=-1,
    )


def local(
    patch_rows,
    vit_gain,
    vit_bias,
    vit_qkv,
    vit_out,
    merge_gain,
    merge_bias,
    merge_weight,
    image_patches,
    window_ids,
    image_pos,
    slice_order,
    doc_ids,
    text_rows,
    norm_gain,
    w_query,
    w_keyval,
):
    shards = lax.axis_size("ctx")
    ctx_index = lax.axis_index("ctx")
    tp_index = lax.axis_index("tp")
    block_feats = merge_weight.shape[0]
    normed = layer_norm(patch_rows.astype(jnp.float32), vit_gain, vit_bias).astype(jnp.bfloat16)
    projected = jnp.einsum(
        "pf,fxhd->pxhd", normed, vit_qkv, preferred_element_type=jnp.float32
    ).astype(jnp.bfloat16)
    scores = jnp.einsum(
        "qhd,khd->hqk", projected[:, 0], projected[:, 1], preferred_element_type=jnp.float32
    ) / math.sqrt(VHD)
    allowed = window_ids[:, None] == window_ids[None, :]
    scores = jnp.where(allowed[None], scores, big_negative)
    powers = jnp.exp(scores - jnp.max(scores, axis=-1, keepdims=True))
    totals = jnp.sum(powers, axis=-1)
    blended = jnp.einsum(
        "hqk,khd->qhd",
        powers.astype(jnp.bfloat16),
        projected[:, 2],
        preferred_element_type=jnp.float32,
    )
    blended = (blended / jnp.transpose(totals)[:, :, None]).astype(jnp.bfloat16)
    branch_part = jnp.einsum("phd,hdf->pf", blended, vit_out, preferred_element_type=jnp.float32)
    tp_size = lax.axis_size("tp")
    vis_size = lax.axis_size("vis")
    vis_index = lax.axis_index("vis")
    tp_rows = PCAP // tp_size
    part_rows = tp_rows // vis_size
    branch_sum = halving_scatter(
        branch_part.reshape(tp_size, tp_rows, VD), tp_index, tp_size, "tp"
    )
    branch_sum = halving_scatter(
        branch_sum.reshape(vis_size, part_rows, VD), vis_index, vis_size, "vis"
    )
    first_row = tp_index * tp_rows + vis_index * part_rows
    hidden = lax.dynamic_slice_in_dim(patch_rows, first_row, part_rows, 0).astype(
        jnp.float32
    ) + branch_sum
    merged_part = layer_norm(hidden, merge_gain, merge_bias).astype(jnp.bfloat16).reshape(
        part_rows // 4, 4 * VD
    )
    merged_part = doubling_gather(
        merged_part, "vis", vis_index, vis_size, list(range(vis_size.bit_length() - 1))
    )
    merged = doubling_gather(merged_part, "tp", tp_index, tp_size, [0]).reshape(ICAP, 4 * VD)
    send_each = ICAP // shards
    slot_ids = jnp.arange(ICAP, dtype=jnp.int32)
    shard_ids = jnp.arange(shards, dtype=jnp.int32)
    live_count = jnp.sum(image_patches, axis=1) // 4
    all_pos = image_pos.reshape(shards, ICAP)
    owner_dev, local_row, owner_hot = place_of(all_pos, slice_order, TOK)
    before = jnp.cumsum(owner_hot, axis=1) - owner_hot
    rank_in = jnp.sum(before * owner_hot, axis=-1)
    is_live = slot_ids[None, :] < live_count[:, None]
    own_hot = (shard_ids == ctx_index)[:, None]
    own_owner = jnp.sum(jnp.where(own_hot, owner_dev, 0), axis=0)
    own_rank = jnp.sum(jnp.where(own_hot, rank_in, 0), axis=0)
    target_slot = own_owner * send_each + own_rank
    picker = (target_slot[None, :] == slot_ids[:, None]).astype(jnp.bfloat16)
    ordered = jnp.dot(picker, merged, preferred_element_type=jnp.float32).astype(jnp.bfloat16)
    blocks = jnp.transpose(ordered.reshape(ICAP, shards, block_feats), (1, 0, 2))
    received = lax.all_to_all(blocks, "ctx", split_axis=0, concat_axis=0, tiled=True)
    by_dest = jnp.transpose(
        received.reshape(shards, shards, send_each, block_feats), (1, 0, 2, 3)
    ).reshape(shards * ICAP, block_feats)
    partial = jnp.dot(by_dest, merge_weight, preferred_element_type=jnp.float32)
    incoming = halving_scatter(partial.reshape(shards, ICAP, -1), ctx_index, shards).astype(
        jnp.bfloat16
    )
    mine_live = ((owner_dev == ctx_index) & is_live).reshape(-1)
    column_of = (shard_ids[:, None] * send_each + rank_in).reshape(-1)
    row_hot = (
        (local_row.reshape(-1)[None, :] == jnp.arange(TOK, dtype=jnp.int32)[:, None])
        & mine_live[None, :]
    ).astype(jnp.bfloat16)
    column_hot = (column_of[:, None] == slot_ids[None, :]).astype(jnp.bfloat16)
    placing = jnp.dot(row_hot, column_hot, preferred_element_type=jnp.float32)
    is_image = jnp.sum(placing, axis=1) > 0.5
    image_part = jnp.dot(placing.astype(jnp.bfloat16), incoming, preferred_element_type=jnp.float32)
    embeds = jnp.where(is_image[:, None], image_part.astype(jnp.bfloat16), text_rows)
    full_rows = lax.all_gather(embeds, ("vis", "tp"), axis=1, tiled=True)
    widened = full_rows.astype(jnp.float32)
    normed_rows = (
        widened
        * lax.rsqrt(jnp.mean(widened * widened, axis=1, keepdims=True) + norm_eps)
        * norm_gain
    ).astype(jnp.bfloat16)
    own_positions = row_positions(
        ctx_index * TOK + jnp.arange(TOK, dtype=jnp.int32), slice_order, TOK
    )
    own_doc = jnp.take(doc_ids, own_positions)
    kv_heads = w_query.shape[1]
    groups = w_query.shape[2]
    queries = jnp.einsum(
        "td,dhgk->thgk", normed_rows, w_query, preferred_element_type=jnp.float32
    )
    queries = rotate(queries, own_positions).astype(jnp.bfloat16)
    projected_half = jnp.einsum(
        "td,dhk->thk", normed_rows, w_keyval[0], preferred_element_type=jnp.float32
    )
    own_half = jnp.where(
        tp_index == 0, rotate(projected_half, own_positions), projected_half
    ).astype(jnp.bfloat16)
    gathered = lax.all_gather(own_half, "ctx", axis=0, tiled=True)
    partner_all = swapped(gathered, "tp", 0)
    keys_every = jnp.where(tp_index == 0, gathered, partner_all)
    values_every = jnp.where(tp_index == 0, partner_all, gathered)
    key_count = keys_every.shape[0]
    key_pos = row_positions(jnp.arange(key_count, dtype=jnp.int32), slice_order, TOK)
    key_doc = jnp.take(doc_ids, key_pos)
    allowed_now = (key_pos[None, :] <= own_positions[:, None]) & (
        key_doc[None, :] == own_doc[:, None]
    )
    scores_now = jnp.einsum(
        "qkgd,nkd->kgqn", queries, keys_every, preferred_element_type=jnp.float32
    ) / math.sqrt(HD)
    scores_now = jnp.where(allowed_now[None, None], scores_now, big_negative)
    best = jnp.max(scores_now, axis=-1, keepdims=True)
    powers_now = jnp.exp(scores_now - best)
    total_final = jnp.sum(powers_now, axis=-1)
    accum_final = jnp.einsum(
        "kgqn,nkd->kgqd",
        powers_now.astype(jnp.bfloat16),
        values_every,
        preferred_element_type=jnp.float32,
    )
    result = accum_final / total_final[..., None]
    return (
        jnp.transpose(result, (2, 0, 1, 3)).reshape(TOK, kv_heads, groups * HD).astype(jnp.bfloat16)
    )


def solution(mesh):
    placed = (
        P("ctx", None),
        P(),
        P(),
        P(None, None, ("vis", "tp"), None),
        P(("vis", "tp"), None, None),
        P(),
        P(),
        P("ctx", ("vis", "tp")),
        P(),
        P("ctx"),
        P(),
        P(),
        P(),
        P("ctx", ("vis", "tp")),
        P(),
        P(None, "vis", "tp", None),
        P("tp", None, "vis", None),
    )
    return jax.shard_map(
        local, mesh=mesh, in_specs=placed, out_specs=P("ctx", "vis", "tp"), check_vma=False
    )
```

```python
import math

import jax
import jax.numpy as jnp
from jax import lax
from jax.sharding import PartitionSpec as P

D = 4096
HD = 128
VD = 1280
VHD = 80
TOK = 128
PCAP = 128
ICAP = 32


norm_eps = 1e-06
rope_base = 1000000.0
big_negative = -1e30


def swapped(value, axis, stride):
    return lax.ppermute(value, axis, [(i, i ^ 1 << stride) for i in range(lax.axis_size(axis))])


def layer_norm(values, scale_vec, shift_vec):
    centre = jnp.mean(values, axis=-1, keepdims=True)
    offset = values - centre
    spread = jnp.mean(offset * offset, axis=-1, keepdims=True)
    return offset * lax.rsqrt(spread + norm_eps) * scale_vec + shift_vec


def rotate(values, positions):
    half_dim = values.shape[-1] // 2
    exponent = jnp.arange(half_dim, dtype=jnp.float32) * (-2.0 / values.shape[-1])
    frequency = jnp.power(jnp.float32(rope_base), exponent)
    angles = positions.astype(jnp.float32)[:, None] * frequency[None, :]
    shape_out = (values.shape[0],) + (1,) * (values.ndim - 2) + (half_dim,)
    cosine = jnp.cos(angles).reshape(shape_out)
    sine_part = jnp.sin(angles).reshape(shape_out)
    lead_half = values[..., :half_dim]
    tail_half = values[..., half_dim:]
    return jnp.concatenate(
        [lead_half * cosine - tail_half * sine_part, tail_half * cosine + lead_half * sine_part],
        axis=-1,
    )


def row_positions(row_ids, slice_order, tokens_dev):
    shards = slice_order.shape[0]
    device_of = row_ids // tokens_dev
    local_row = row_ids % tokens_dev
    half_tok = tokens_dev // 2
    matches = device_of[:, None] == jnp.arange(shards, dtype=jnp.int32)[None, :]
    first_slice = jnp.sum(jnp.where(matches, slice_order[None, :], 0), axis=1)
    slice_ids = jnp.where(local_row < half_tok, first_slice, 2 * shards - 1 - first_slice)
    return slice_ids * half_tok + local_row % half_tok


def place_of(positions, slice_order, tokens_dev):
    shards = slice_order.shape[0]
    half_tok = tokens_dev // 2
    slice_ids = positions // half_tok
    paired = jnp.minimum(slice_ids, 2 * shards - 1 - slice_ids)
    owner_hot = (paired[..., None] == slice_order).astype(jnp.int32)
    owner_dev = jnp.sum(owner_hot * jnp.arange(shards, dtype=jnp.int32), axis=-1)
    local_row = jnp.where(slice_ids < shards, 0, half_tok) + positions % half_tok
    return (owner_dev, local_row, owner_hot)


def halving_scatter(blocks, index, count, axis="ctx"):
    remaining = count
    bit = 0
    while remaining > 1:
        lower = blocks.reshape((remaining // 2, 2) + blocks.shape[1:])
        mine = (index >> bit) & 1
        keep = jnp.where(mine == 0, lower[:, 0], lower[:, 1])
        give = jnp.where(mine == 0, lower[:, 1], lower[:, 0])
        blocks = keep + swapped(give, axis, bit)
        remaining //= 2
        bit += 1
    return blocks[0]


def doubling_gather(block, axis, index, count, bits):
    have = block[None]
    for bit in bits:
        arrived = swapped(have, axis, bit)
        mine = (index >> bit) & 1
        have = jnp.where(
            mine == 0,
            jnp.concatenate([have, arrived], axis=0),
            jnp.concatenate([arrived, have], axis=0),
        )
    order = list(bits)
    have = have.reshape((2,) * len(order) + block.shape)
    by_bit = {bit: len(order) - 1 - place for place, bit in enumerate(order)}
    wanted = [by_bit[bit] for bit in sorted(order, reverse=True)]
    have = jnp.transpose(have, wanted + list(range(len(order), have.ndim)))
    return have.reshape((count,) + block.shape)


def rotate_rows(values, positions):
    half_dim = values.shape[-1] // 2
    exponent = jnp.arange(half_dim, dtype=jnp.float32) * (-2.0 / values.shape[-1])
    frequency = jnp.power(jnp.float32(rope_base), exponent)
    angles = positions.astype(jnp.float32)[:, None] * frequency[None, :]
    cosine = jnp.cos(angles)
    sine_part = jnp.sin(angles)
    lead_half = values[..., :half_dim]
    tail_half = values[..., half_dim:]
    return jnp.concatenate(
        [lead_half * cosine - tail_half * sine_part, tail_half * cosine + lead_half * sine_part],
        axis=-1,
    )


def local(
    patch_rows,
    vit_gain,
    vit_bias,
    vit_qkv,
    vit_out,
    merge_gain,
    merge_bias,
    merge_weight,
    image_patches,
    window_ids,
    image_pos,
    slice_order,
    doc_ids,
    text_rows,
    norm_gain,
    w_query,
    w_keyval,
):
    shards = lax.axis_size("ctx")
    ctx_index = lax.axis_index("ctx")
    tp_index = lax.axis_index("tp")
    block_feats = merge_weight.shape[0]
    normed = layer_norm(patch_rows.astype(jnp.float32), vit_gain, vit_bias).astype(jnp.bfloat16)
    projected = jnp.einsum(
        "pf,fxhd->pxhd", normed, vit_qkv, preferred_element_type=jnp.float32
    ).astype(jnp.bfloat16)
    scores = jnp.einsum(
        "qhd,khd->hqk", projected[:, 0], projected[:, 1], preferred_element_type=jnp.float32
    ) / math.sqrt(VHD)
    allowed = window_ids[:, None] == window_ids[None, :]
    scores = jnp.where(allowed[None], scores, big_negative)
    powers = jnp.exp(scores - jnp.max(scores, axis=-1, keepdims=True))
    totals = jnp.sum(powers, axis=-1)
    blended = jnp.einsum(
        "hqk,khd->qhd",
        powers.astype(jnp.bfloat16),
        projected[:, 2],
        preferred_element_type=jnp.float32,
    )
    blended = (blended / jnp.transpose(totals)[:, :, None]).astype(jnp.bfloat16)
    branch_part = jnp.einsum("phd,hdf->pf", blended, vit_out, preferred_element_type=jnp.float32)
    tp_size = lax.axis_size("tp")
    vis_size = lax.axis_size("vis")
    vis_index = lax.axis_index("vis")
    tp_rows = PCAP // tp_size
    part_rows = tp_rows // vis_size
    branch_sum = halving_scatter(
        branch_part.reshape(tp_size, tp_rows, VD), tp_index, tp_size, "tp"
    )
    branch_sum = halving_scatter(
        branch_sum.reshape(vis_size, part_rows, VD), vis_index, vis_size, "vis"
    )
    first_row = tp_index * tp_rows + vis_index * part_rows
    hidden = lax.dynamic_slice_in_dim(patch_rows, first_row, part_rows, 0).astype(
        jnp.float32
    ) + branch_sum
    merged_part = layer_norm(hidden, merge_gain, merge_bias).astype(jnp.bfloat16).reshape(
        part_rows // 4, 4 * VD
    )
    merged_part = doubling_gather(
        merged_part, "vis", vis_index, vis_size, list(range(vis_size.bit_length() - 1))
    )
    merged = doubling_gather(merged_part, "tp", tp_index, tp_size, [0]).reshape(ICAP, 4 * VD)
    send_each = ICAP // shards
    slot_ids = jnp.arange(ICAP, dtype=jnp.int32)
    shard_ids = jnp.arange(shards, dtype=jnp.int32)
    live_count = jnp.sum(image_patches, axis=1) // 4
    all_pos = image_pos.reshape(shards, ICAP)
    owner_dev, local_row, owner_hot = place_of(all_pos, slice_order, TOK)
    before = jnp.cumsum(owner_hot, axis=1) - owner_hot
    rank_in = jnp.sum(before * owner_hot, axis=-1)
    is_live = slot_ids[None, :] < live_count[:, None]
    own_hot = (shard_ids == ctx_index)[:, None]
    own_owner = jnp.sum(jnp.where(own_hot, owner_dev, 0), axis=0)
    own_rank = jnp.sum(jnp.where(own_hot, rank_in, 0), axis=0)
    target_slot = own_owner * send_each + own_rank
    picker = (target_slot[None, :] == slot_ids[:, None]).astype(jnp.bfloat16)
    ordered = jnp.dot(picker, merged, preferred_element_type=jnp.float32).astype(jnp.bfloat16)
    blocks = jnp.transpose(ordered.reshape(ICAP, shards, block_feats), (1, 0, 2))
    received = lax.all_to_all(blocks, "ctx", split_axis=0, concat_axis=0, tiled=True)
    by_dest = jnp.transpose(
        received.reshape(shards, shards, send_each, block_feats), (1, 0, 2, 3)
    ).reshape(shards * ICAP, block_feats)
    partial = jnp.dot(by_dest, merge_weight, preferred_element_type=jnp.float32)
    incoming = halving_scatter(partial.reshape(shards, ICAP, -1), ctx_index, shards).astype(
        jnp.bfloat16
    )
    mine_live = ((owner_dev == ctx_index) & is_live).reshape(-1)
    column_of = (shard_ids[:, None] * send_each + rank_in).reshape(-1)
    row_hot = (
        (local_row.reshape(-1)[None, :] == jnp.arange(TOK, dtype=jnp.int32)[:, None])
        & mine_live[None, :]
    ).astype(jnp.bfloat16)
    column_hot = (column_of[:, None] == slot_ids[None, :]).astype(jnp.bfloat16)
    placing = jnp.dot(row_hot, column_hot, preferred_element_type=jnp.float32)
    is_image = jnp.sum(placing, axis=1) > 0.5
    image_part = jnp.dot(placing.astype(jnp.bfloat16), incoming, preferred_element_type=jnp.float32)
    embeds = jnp.where(is_image[:, None], image_part.astype(jnp.bfloat16), text_rows)
    full_rows = lax.all_gather(embeds, ("vis", "tp"), axis=1, tiled=True)
    widened = full_rows.astype(jnp.float32)
    normed_rows = (
        widened
        * lax.rsqrt(jnp.mean(widened * widened, axis=1, keepdims=True) + norm_eps)
        * norm_gain
    ).astype(jnp.bfloat16)
    own_positions = row_positions(
        ctx_index * TOK + jnp.arange(TOK, dtype=jnp.int32), slice_order, TOK
    )
    kv_heads = w_query.shape[1]
    groups = w_query.shape[2]
    queries = jnp.einsum(
        "td,dhgk->thgk", normed_rows, w_query, preferred_element_type=jnp.float32
    )
    queries = rotate(queries, own_positions).astype(jnp.bfloat16)
    projected_half = jnp.einsum(
        "td,dhk->thk", normed_rows, w_keyval[0], preferred_element_type=jnp.float32
    )
    own_half = jnp.where(
        tp_index == 0, rotate(projected_half, own_positions), projected_half
    ).astype(jnp.bfloat16)
    gathered = lax.all_gather(own_half, "ctx", axis=0, tiled=True)
    partner_all = swapped(gathered, "tp", 0)
    keys_every = jnp.where(tp_index == 0, gathered, partner_all)
    values_every = jnp.where(tp_index == 0, partner_all, gathered)
    key_count = keys_every.shape[0]
    key_pos = row_positions(jnp.arange(key_count, dtype=jnp.int32), slice_order, TOK)
    doc_slices = doc_ids.reshape(2 * shards, TOK // 2)
    slice_ids = jnp.stack([slice_order, 2 * shards - 1 - slice_order], axis=1)
    slice_hot = slice_ids[:, :, None] == jnp.arange(2 * shards, dtype=jnp.int32)[None, None, :]
    key_doc = jnp.sum(
        jnp.where(slice_hot[..., None], doc_slices[None, None], 0), axis=2
    ).reshape(shards * TOK)
    own_doc = jnp.sum(
        jnp.where((shard_ids == ctx_index)[:, None], key_doc.reshape(shards, TOK), 0), axis=0
    )
    allowed_now = (key_pos[None, :] <= own_positions[:, None]) & (
        key_doc[None, :] == own_doc[:, None]
    )
    scores_now = jnp.einsum(
        "qkgd,nkd->kgqn", queries, keys_every, preferred_element_type=jnp.float32
    ) / math.sqrt(HD)
    scores_now = jnp.where(allowed_now[None, None], scores_now, big_negative)
    best = jnp.max(scores_now, axis=-1, keepdims=True)
    powers_now = jnp.exp(scores_now - best)
    total_final = jnp.sum(powers_now, axis=-1)
    accum_final = jnp.einsum(
        "kgqn,nkd->kgqd",
        powers_now.astype(jnp.bfloat16),
        values_every,
        preferred_element_type=jnp.float32,
    )
    result = accum_final / total_final[..., None]
    return (
        jnp.transpose(result, (2, 0, 1, 3)).reshape(TOK, kv_heads, groups * HD).astype(jnp.bfloat16)
    )


def solution(mesh):
    placed = (
        P("ctx", None),
        P(),
        P(),
        P(None, None, ("vis", "tp"), None),
        P(("vis", "tp"), None, None),
        P(),
        P(),
        P("ctx", ("vis", "tp")),
        P(),
        P("ctx"),
        P(),
        P(),
        P(),
        P("ctx", ("vis", "tp")),
        P(),
        P(None, "vis", "tp", None),
        P("tp", None, "vis", None),
    )
    return jax.shard_map(
        local, mesh=mesh, in_specs=placed, out_specs=P("ctx", "vis", "tp"), check_vma=False
    )
```

```python
import math

import jax
import jax.numpy as jnp
from jax import lax
from jax.sharding import PartitionSpec as P

D = 4096
HD = 128
VD = 1280
VHD = 80
TOK = 128
PCAP = 128
ICAP = 32


norm_eps = 1e-06
rope_base = 1000000.0
big_negative = -1e30


def swapped(value, axis, stride):
    return lax.ppermute(value, axis, [(i, i ^ 1 << stride) for i in range(lax.axis_size(axis))])


def layer_norm(values, scale_vec, shift_vec):
    centre = jnp.mean(values, axis=-1, keepdims=True)
    offset = values - centre
    spread = jnp.mean(offset * offset, axis=-1, keepdims=True)
    return offset * lax.rsqrt(spread + norm_eps) * scale_vec + shift_vec


def rotate(values, positions):
    half_dim = values.shape[-1] // 2
    exponent = jnp.arange(half_dim, dtype=jnp.float32) * (-2.0 / values.shape[-1])
    frequency = jnp.power(jnp.float32(rope_base), exponent)
    angles = positions.astype(jnp.float32)[:, None] * frequency[None, :]
    shape_out = (values.shape[0],) + (1,) * (values.ndim - 2) + (half_dim,)
    cosine = jnp.cos(angles).reshape(shape_out)
    sine_part = jnp.sin(angles).reshape(shape_out)
    lead_half = values[..., :half_dim]
    tail_half = values[..., half_dim:]
    return jnp.concatenate(
        [lead_half * cosine - tail_half * sine_part, tail_half * cosine + lead_half * sine_part],
        axis=-1,
    )


def row_positions(row_ids, slice_order, tokens_dev):
    shards = slice_order.shape[0]
    device_of = row_ids // tokens_dev
    local_row = row_ids % tokens_dev
    half_tok = tokens_dev // 2
    matches = device_of[:, None] == jnp.arange(shards, dtype=jnp.int32)[None, :]
    first_slice = jnp.sum(jnp.where(matches, slice_order[None, :], 0), axis=1)
    slice_ids = jnp.where(local_row < half_tok, first_slice, 2 * shards - 1 - first_slice)
    return slice_ids * half_tok + local_row % half_tok


def place_of(positions, slice_order, tokens_dev):
    shards = slice_order.shape[0]
    half_tok = tokens_dev // 2
    slice_ids = positions // half_tok
    paired = jnp.minimum(slice_ids, 2 * shards - 1 - slice_ids)
    owner_hot = (paired[..., None] == slice_order).astype(jnp.int32)
    owner_dev = jnp.sum(owner_hot * jnp.arange(shards, dtype=jnp.int32), axis=-1)
    local_row = jnp.where(slice_ids < shards, 0, half_tok) + positions % half_tok
    return (owner_dev, local_row, owner_hot)


def halving_scatter(blocks, index, count, axis="ctx"):
    remaining = count
    bit = 0
    while remaining > 1:
        lower = blocks.reshape((remaining // 2, 2) + blocks.shape[1:])
        mine = (index >> bit) & 1
        keep = jnp.where(mine == 0, lower[:, 0], lower[:, 1])
        give = jnp.where(mine == 0, lower[:, 1], lower[:, 0])
        blocks = keep + swapped(give, axis, bit)
        remaining //= 2
        bit += 1
    return blocks[0]


def doubling_gather(block, axis, index, count, bits):
    have = block[None]
    for bit in bits:
        arrived = swapped(have, axis, bit)
        mine = (index >> bit) & 1
        have = jnp.where(
            mine == 0,
            jnp.concatenate([have, arrived], axis=0),
            jnp.concatenate([arrived, have], axis=0),
        )
    order = list(bits)
    have = have.reshape((2,) * len(order) + block.shape)
    by_bit = {bit: len(order) - 1 - place for place, bit in enumerate(order)}
    wanted = [by_bit[bit] for bit in sorted(order, reverse=True)]
    have = jnp.transpose(have, wanted + list(range(len(order), have.ndim)))
    return have.reshape((count,) + block.shape)


def rotate_rows(values, positions):
    half_dim = values.shape[-1] // 2
    exponent = jnp.arange(half_dim, dtype=jnp.float32) * (-2.0 / values.shape[-1])
    frequency = jnp.power(jnp.float32(rope_base), exponent)
    angles = positions.astype(jnp.float32)[:, None] * frequency[None, :]
    cosine = jnp.cos(angles)
    sine_part = jnp.sin(angles)
    lead_half = values[..., :half_dim]
    tail_half = values[..., half_dim:]
    return jnp.concatenate(
        [lead_half * cosine - tail_half * sine_part, tail_half * cosine + lead_half * sine_part],
        axis=-1,
    )


def local(
    patch_rows,
    vit_gain,
    vit_bias,
    vit_qkv,
    vit_out,
    merge_gain,
    merge_bias,
    merge_weight,
    image_patches,
    window_ids,
    image_pos,
    slice_order,
    doc_ids,
    text_rows,
    norm_gain,
    w_query,
    w_keyval,
):
    shards = lax.axis_size("ctx")
    ctx_index = lax.axis_index("ctx")
    tp_index = lax.axis_index("tp")
    block_feats = merge_weight.shape[0]
    normed = layer_norm(patch_rows.astype(jnp.float32), vit_gain, vit_bias).astype(jnp.bfloat16)
    projected = jnp.einsum(
        "pf,fxhd->pxhd", normed, vit_qkv, preferred_element_type=jnp.float32
    ).astype(jnp.bfloat16)
    scores = jnp.einsum(
        "qhd,khd->hqk", projected[:, 0], projected[:, 1], preferred_element_type=jnp.float32
    ) / math.sqrt(VHD)
    allowed = window_ids[:, None] == window_ids[None, :]
    scores = jnp.where(allowed[None], scores, big_negative)
    powers = jnp.exp(scores - jnp.max(scores, axis=-1, keepdims=True))
    totals = jnp.sum(powers, axis=-1)
    blended = jnp.einsum(
        "hqk,khd->qhd",
        powers.astype(jnp.bfloat16),
        projected[:, 2],
        preferred_element_type=jnp.float32,
    )
    blended = (blended / jnp.transpose(totals)[:, :, None]).astype(jnp.bfloat16)
    branch_part = jnp.einsum("phd,hdf->pf", blended, vit_out, preferred_element_type=jnp.float32)
    tp_size = lax.axis_size("tp")
    vis_size = lax.axis_size("vis")
    vis_index = lax.axis_index("vis")
    tp_rows = PCAP // tp_size
    part_rows = tp_rows // vis_size
    branch_sum = halving_scatter(
        branch_part.reshape(tp_size, tp_rows, VD), tp_index, tp_size, "tp"
    )
    branch_sum = halving_scatter(
        branch_sum.reshape(vis_size, part_rows, VD), vis_index, vis_size, "vis"
    )
    first_row = tp_index * tp_rows + vis_index * part_rows
    hidden = lax.dynamic_slice_in_dim(patch_rows, first_row, part_rows, 0).astype(
        jnp.float32
    ) + branch_sum
    merged_part = layer_norm(hidden, merge_gain, merge_bias).astype(jnp.bfloat16).reshape(
        part_rows // 4, 4 * VD
    )
    merged_part = doubling_gather(
        merged_part, "vis", vis_index, vis_size, list(range(vis_size.bit_length() - 1))
    )
    merged = doubling_gather(merged_part, "tp", tp_index, tp_size, [0]).reshape(ICAP, 4 * VD)
    send_each = ICAP // shards
    slot_ids = jnp.arange(ICAP, dtype=jnp.int32)
    shard_ids = jnp.arange(shards, dtype=jnp.int32)
    live_count = jnp.sum(image_patches, axis=1) // 4
    all_pos = image_pos.reshape(shards, ICAP)
    owner_dev, local_row, owner_hot = place_of(all_pos, slice_order, TOK)
    before = jnp.cumsum(owner_hot, axis=1) - owner_hot
    rank_in = jnp.sum(before * owner_hot, axis=-1)
    is_live = slot_ids[None, :] < live_count[:, None]
    own_hot = (shard_ids == ctx_index)[:, None]
    own_owner = jnp.sum(jnp.where(own_hot, owner_dev, 0), axis=0)
    own_rank = jnp.sum(jnp.where(own_hot, rank_in, 0), axis=0)
    target_slot = own_owner * send_each + own_rank
    picker = (target_slot[None, :] == slot_ids[:, None]).astype(jnp.bfloat16)
    ordered = jnp.dot(picker, merged, preferred_element_type=jnp.float32).astype(jnp.bfloat16)
    blocks = jnp.transpose(ordered.reshape(ICAP, shards, block_feats), (1, 0, 2))
    received = lax.all_to_all(blocks, "ctx", split_axis=0, concat_axis=0, tiled=True)
    by_dest = jnp.transpose(
        received.reshape(shards, shards, send_each, block_feats), (1, 0, 2, 3)
    ).reshape(shards * ICAP, block_feats)
    partial = jnp.dot(by_dest, merge_weight, preferred_element_type=jnp.float32)
    incoming = halving_scatter(partial.reshape(shards, ICAP, -1), ctx_index, shards).astype(
        jnp.bfloat16
    )
    mine_live = ((owner_dev == ctx_index) & is_live).reshape(-1)
    column_of = (shard_ids[:, None] * send_each + rank_in).reshape(-1)
    row_hot = (
        (local_row.reshape(-1)[None, :] == jnp.arange(TOK, dtype=jnp.int32)[:, None])
        & mine_live[None, :]
    ).astype(jnp.bfloat16)
    column_hot = (column_of[:, None] == slot_ids[None, :]).astype(jnp.bfloat16)
    placing = jnp.dot(row_hot, column_hot, preferred_element_type=jnp.float32)
    is_image = jnp.sum(placing, axis=1) > 0.5
    image_part = jnp.dot(placing.astype(jnp.bfloat16), incoming, preferred_element_type=jnp.float32)
    embeds = jnp.where(is_image[:, None], image_part.astype(jnp.bfloat16), text_rows)
    full_rows = lax.all_gather(embeds, ("vis", "tp"), axis=1, tiled=True)
    widened = full_rows.astype(jnp.float32)
    normed_rows = (
        widened
        * lax.rsqrt(jnp.mean(widened * widened, axis=1, keepdims=True) + norm_eps)
        * norm_gain
    ).astype(jnp.bfloat16)
    own_positions = row_positions(
        ctx_index * TOK + jnp.arange(TOK, dtype=jnp.int32), slice_order, TOK
    )
    kv_heads = w_query.shape[1]
    groups = w_query.shape[2]
    projected_half = jnp.einsum(
        "td,dhk->thk", normed_rows, w_keyval[0], preferred_element_type=jnp.float32
    )
    own_half = jnp.where(
        tp_index == 0, rotate(projected_half, own_positions), projected_half
    ).astype(jnp.bfloat16)
    query_weights, own_half = lax.optimization_barrier((w_query, own_half))
    gathered = lax.all_gather(own_half, "ctx", axis=0, tiled=True)
    queries = jnp.einsum(
        "td,dhgk->thgk", normed_rows, query_weights, preferred_element_type=jnp.float32
    )
    queries = rotate(queries, own_positions).astype(jnp.bfloat16)
    key_pos = row_positions(jnp.arange(shards * TOK, dtype=jnp.int32), slice_order, TOK)
    doc_slices = doc_ids.reshape(2 * shards, TOK // 2)
    slice_ids = jnp.stack([slice_order, 2 * shards - 1 - slice_order], axis=1)
    slice_hot = slice_ids[:, :, None] == jnp.arange(2 * shards, dtype=jnp.int32)[None, None, :]
    key_doc = jnp.sum(
        jnp.where(slice_hot[..., None], doc_slices[None, None], 0), axis=2
    ).reshape(shards * TOK)
    own_doc = jnp.sum(
        jnp.where((shard_ids == ctx_index)[:, None], key_doc.reshape(shards, TOK), 0), axis=0
    )
    allowed_now = (key_pos[None, :] <= own_positions[:, None]) & (
        key_doc[None, :] == own_doc[:, None]
    )
    queries, allowed_now, gathered = lax.optimization_barrier((queries, allowed_now, gathered))
    partner_all = swapped(gathered, "tp", 0)
    keys_every = jnp.where(tp_index == 0, gathered, partner_all)
    values_every = jnp.where(tp_index == 0, partner_all, gathered)
    key_count = keys_every.shape[0]
    scores_now = jnp.einsum(
        "qkgd,nkd->kgqn", queries, keys_every, preferred_element_type=jnp.float32
    ) / math.sqrt(HD)
    scores_now = jnp.where(allowed_now[None, None], scores_now, big_negative)
    best = jnp.max(scores_now, axis=-1, keepdims=True)
    powers_now = jnp.exp(scores_now - best)
    total_final = jnp.sum(powers_now, axis=-1)
    accum_final = jnp.einsum(
        "kgqn,nkd->kgqd",
        powers_now.astype(jnp.bfloat16),
        values_every,
        preferred_element_type=jnp.float32,
    )
    result = accum_final / total_final[..., None]
    return (
        jnp.transpose(result, (2, 0, 1, 3)).reshape(TOK, kv_heads, groups * HD).astype(jnp.bfloat16)
    )


def solution(mesh):
    placed = (
        P("ctx", None),
        P(),
        P(),
        P(None, None, ("vis", "tp"), None),
        P(("vis", "tp"), None, None),
        P(),
        P(),
        P("ctx", ("vis", "tp")),
        P(),
        P("ctx"),
        P(),
        P(),
        P(),
        P("ctx", ("vis", "tp")),
        P(),
        P(None, "vis", "tp", None),
        P("tp", None, "vis", None),
    )
    return jax.shard_map(
        local, mesh=mesh, in_specs=placed, out_specs=P("ctx", "vis", "tp"), check_vma=False
    )
```

```python
import math

import jax
import jax.numpy as jnp
from jax import lax
from jax.sharding import PartitionSpec as P

D = 4096
HD = 128
VD = 1280
VHD = 80
TOK = 128
PCAP = 128
ICAP = 32


norm_eps = 1e-06
rope_base = 1000000.0
big_negative = -1e30


def swapped(value, axis, stride):
    return lax.ppermute(value, axis, [(i, i ^ 1 << stride) for i in range(lax.axis_size(axis))])


def layer_norm(values, scale_vec, shift_vec):
    centre = jnp.mean(values, axis=-1, keepdims=True)
    offset = values - centre
    spread = jnp.mean(offset * offset, axis=-1, keepdims=True)
    return offset * lax.rsqrt(spread + norm_eps) * scale_vec + shift_vec


def rotate(values, positions):
    half_dim = values.shape[-1] // 2
    exponent = jnp.arange(half_dim, dtype=jnp.float32) * (-2.0 / values.shape[-1])
    frequency = jnp.power(jnp.float32(rope_base), exponent)
    angles = positions.astype(jnp.float32)[:, None] * frequency[None, :]
    shape_out = (values.shape[0],) + (1,) * (values.ndim - 2) + (half_dim,)
    cosine = jnp.cos(angles).reshape(shape_out)
    sine_part = jnp.sin(angles).reshape(shape_out)
    lead_half = values[..., :half_dim]
    tail_half = values[..., half_dim:]
    return jnp.concatenate(
        [lead_half * cosine - tail_half * sine_part, tail_half * cosine + lead_half * sine_part],
        axis=-1,
    )


def row_positions(row_ids, slice_order, tokens_dev):
    shards = slice_order.shape[0]
    device_of = row_ids // tokens_dev
    local_row = row_ids % tokens_dev
    half_tok = tokens_dev // 2
    matches = device_of[:, None] == jnp.arange(shards, dtype=jnp.int32)[None, :]
    first_slice = jnp.sum(jnp.where(matches, slice_order[None, :], 0), axis=1)
    slice_ids = jnp.where(local_row < half_tok, first_slice, 2 * shards - 1 - first_slice)
    return slice_ids * half_tok + local_row % half_tok


def place_of(positions, slice_order, tokens_dev):
    shards = slice_order.shape[0]
    half_tok = tokens_dev // 2
    slice_ids = positions // half_tok
    paired = jnp.minimum(slice_ids, 2 * shards - 1 - slice_ids)
    owner_hot = (paired[..., None] == slice_order).astype(jnp.int32)
    owner_dev = jnp.sum(owner_hot * jnp.arange(shards, dtype=jnp.int32), axis=-1)
    local_row = jnp.where(slice_ids < shards, 0, half_tok) + positions % half_tok
    return (owner_dev, local_row, owner_hot)


def halving_scatter(blocks, index, count, axis="ctx"):
    remaining = count
    bit = 0
    while remaining > 1:
        lower = blocks.reshape((remaining // 2, 2) + blocks.shape[1:])
        mine = (index >> bit) & 1
        keep = jnp.where(mine == 0, lower[:, 0], lower[:, 1])
        give = jnp.where(mine == 0, lower[:, 1], lower[:, 0])
        blocks = keep + swapped(give, axis, bit)
        remaining //= 2
        bit += 1
    return blocks[0]


def doubling_gather(block, axis, index, count, bits):
    have = block[None]
    for bit in bits:
        arrived = swapped(have, axis, bit)
        mine = (index >> bit) & 1
        have = jnp.where(
            mine == 0,
            jnp.concatenate([have, arrived], axis=0),
            jnp.concatenate([arrived, have], axis=0),
        )
    order = list(bits)
    have = have.reshape((2,) * len(order) + block.shape)
    by_bit = {bit: len(order) - 1 - place for place, bit in enumerate(order)}
    wanted = [by_bit[bit] for bit in sorted(order, reverse=True)]
    have = jnp.transpose(have, wanted + list(range(len(order), have.ndim)))
    return have.reshape((count,) + block.shape)


def rotate_rows(values, positions):
    half_dim = values.shape[-1] // 2
    exponent = jnp.arange(half_dim, dtype=jnp.float32) * (-2.0 / values.shape[-1])
    frequency = jnp.power(jnp.float32(rope_base), exponent)
    angles = positions.astype(jnp.float32)[:, None] * frequency[None, :]
    cosine = jnp.cos(angles)
    sine_part = jnp.sin(angles)
    lead_half = values[..., :half_dim]
    tail_half = values[..., half_dim:]
    return jnp.concatenate(
        [lead_half * cosine - tail_half * sine_part, tail_half * cosine + lead_half * sine_part],
        axis=-1,
    )


def local(
    patch_rows,
    vit_gain,
    vit_bias,
    vit_qkv,
    vit_out,
    merge_gain,
    merge_bias,
    merge_weight,
    image_patches,
    window_ids,
    image_pos,
    slice_order,
    doc_ids,
    text_rows,
    norm_gain,
    w_query,
    w_keyval,
):
    shards = lax.axis_size("ctx")
    ctx_index = lax.axis_index("ctx")
    tp_index = lax.axis_index("tp")
    block_feats = merge_weight.shape[0]
    normed = layer_norm(patch_rows.astype(jnp.float32), vit_gain, vit_bias).astype(jnp.bfloat16)
    projected = jnp.einsum(
        "pf,fxhd->pxhd", normed, vit_qkv, preferred_element_type=jnp.float32
    ).astype(jnp.bfloat16)
    scores = jnp.einsum(
        "qhd,khd->hqk", projected[:, 0], projected[:, 1], preferred_element_type=jnp.float32
    ) / math.sqrt(VHD)
    allowed = window_ids[:, None] == window_ids[None, :]
    scores = jnp.where(allowed[None], scores, big_negative)
    powers = jnp.exp(scores - jnp.max(scores, axis=-1, keepdims=True))
    totals = jnp.sum(powers, axis=-1)
    blended = jnp.einsum(
        "hqk,khd->qhd",
        powers.astype(jnp.bfloat16),
        projected[:, 2],
        preferred_element_type=jnp.float32,
    )
    blended = (blended / jnp.transpose(totals)[:, :, None]).astype(jnp.bfloat16)
    branch_part = jnp.einsum("phd,hdf->pf", blended, vit_out, preferred_element_type=jnp.float32)
    tp_size = lax.axis_size("tp")
    vis_size = lax.axis_size("vis")
    vis_index = lax.axis_index("vis")
    tp_rows = PCAP // tp_size
    part_rows = tp_rows // vis_size
    branch_sum = halving_scatter(
        branch_part.reshape(tp_size, tp_rows, VD), tp_index, tp_size, "tp"
    )
    branch_sum = halving_scatter(
        branch_sum.reshape(vis_size, part_rows, VD), vis_index, vis_size, "vis"
    )
    first_row = tp_index * tp_rows + vis_index * part_rows
    hidden = lax.dynamic_slice_in_dim(patch_rows, first_row, part_rows, 0).astype(
        jnp.float32
    ) + branch_sum
    merged_part = layer_norm(hidden, merge_gain, merge_bias).astype(jnp.bfloat16).reshape(
        part_rows // 4, 4 * VD
    )
    merged_part = doubling_gather(
        merged_part, "vis", vis_index, vis_size, list(range(vis_size.bit_length() - 1))
    )
    merged = doubling_gather(merged_part, "tp", tp_index, tp_size, [0]).reshape(ICAP, 4 * VD)
    send_each = ICAP // shards
    slot_ids = jnp.arange(ICAP, dtype=jnp.int32)
    shard_ids = jnp.arange(shards, dtype=jnp.int32)
    live_count = jnp.sum(image_patches, axis=1) // 4
    all_pos = image_pos.reshape(shards, ICAP)
    owner_dev, local_row, owner_hot = place_of(all_pos, slice_order, TOK)
    before = jnp.cumsum(owner_hot, axis=1) - owner_hot
    rank_in = jnp.sum(before * owner_hot, axis=-1)
    is_live = slot_ids[None, :] < live_count[:, None]
    own_hot = (shard_ids == ctx_index)[:, None]
    own_owner = jnp.sum(jnp.where(own_hot, owner_dev, 0), axis=0)
    own_rank = jnp.sum(jnp.where(own_hot, rank_in, 0), axis=0)
    target_slot = own_owner * send_each + own_rank
    picker = (target_slot[None, :] == slot_ids[:, None]).astype(jnp.bfloat16)
    ordered = jnp.dot(picker, merged, preferred_element_type=jnp.float32).astype(jnp.bfloat16)
    blocks = jnp.transpose(ordered.reshape(ICAP, shards, block_feats), (1, 0, 2))
    received = lax.all_to_all(blocks, "ctx", split_axis=0, concat_axis=0, tiled=True)
    by_dest = jnp.transpose(
        received.reshape(shards, shards, send_each, block_feats), (1, 0, 2, 3)
    ).reshape(shards * ICAP, block_feats)
    partial = jnp.dot(by_dest, merge_weight, preferred_element_type=jnp.float32)
    incoming = halving_scatter(partial.reshape(shards, ICAP, -1), ctx_index, shards).astype(
        jnp.bfloat16
    )
    mine_live = ((owner_dev == ctx_index) & is_live).reshape(-1)
    column_of = (shard_ids[:, None] * send_each + rank_in).reshape(-1)
    row_hot = (
        (local_row.reshape(-1)[None, :] == jnp.arange(TOK, dtype=jnp.int32)[:, None])
        & mine_live[None, :]
    ).astype(jnp.bfloat16)
    column_hot = (column_of[:, None] == slot_ids[None, :]).astype(jnp.bfloat16)
    placing = jnp.dot(row_hot, column_hot, preferred_element_type=jnp.float32)
    is_image = jnp.sum(placing, axis=1) > 0.5
    image_part = jnp.dot(placing.astype(jnp.bfloat16), incoming, preferred_element_type=jnp.float32)
    embeds = jnp.where(is_image[:, None], image_part.astype(jnp.bfloat16), text_rows)
    stacked = doubling_gather(embeds, "tp", tp_index, tp_size, [0])
    stacked = doubling_gather(
        stacked, "vis", vis_index, vis_size, list(range(vis_size.bit_length() - 1))
    )
    full_rows = jnp.transpose(stacked, (2, 0, 1, 3)).reshape(TOK, -1)
    widened = full_rows.astype(jnp.float32)
    normed_rows = (
        widened
        * lax.rsqrt(jnp.mean(widened * widened, axis=1, keepdims=True) + norm_eps)
        * norm_gain
    ).astype(jnp.bfloat16)
    own_positions = row_positions(
        ctx_index * TOK + jnp.arange(TOK, dtype=jnp.int32), slice_order, TOK
    )
    kv_heads = w_query.shape[1]
    groups = w_query.shape[2]
    projected_half = jnp.einsum(
        "td,dhk->thk", normed_rows, w_keyval[0], preferred_element_type=jnp.float32
    )
    own_half = jnp.where(
        tp_index == 0, rotate(projected_half, own_positions), projected_half
    ).astype(jnp.bfloat16)
    query_weights, own_half = lax.optimization_barrier((w_query, own_half))
    gathered = lax.all_gather(own_half, "ctx", axis=0, tiled=True)
    queries = jnp.einsum(
        "td,dhgk->thgk", normed_rows, query_weights, preferred_element_type=jnp.float32
    )
    queries = rotate(queries, own_positions).astype(jnp.bfloat16)
    key_pos = row_positions(jnp.arange(shards * TOK, dtype=jnp.int32), slice_order, TOK)
    doc_slices = doc_ids.reshape(2 * shards, TOK // 2)
    slice_ids = jnp.stack([slice_order, 2 * shards - 1 - slice_order], axis=1)
    slice_hot = slice_ids[:, :, None] == jnp.arange(2 * shards, dtype=jnp.int32)[None, None, :]
    key_doc = jnp.sum(
        jnp.where(slice_hot[..., None], doc_slices[None, None], 0), axis=2
    ).reshape(shards * TOK)
    own_doc = jnp.sum(
        jnp.where((shard_ids == ctx_index)[:, None], key_doc.reshape(shards, TOK), 0), axis=0
    )
    allowed_now = (key_pos[None, :] <= own_positions[:, None]) & (
        key_doc[None, :] == own_doc[:, None]
    )
    queries, allowed_now, gathered = lax.optimization_barrier((queries, allowed_now, gathered))
    partner_all = swapped(gathered, "tp", 0)
    keys_every = jnp.where(tp_index == 0, gathered, partner_all)
    values_every = jnp.where(tp_index == 0, partner_all, gathered)
    key_count = keys_every.shape[0]
    scores_now = jnp.einsum(
        "qkgd,nkd->kgqn", queries, keys_every, preferred_element_type=jnp.float32
    ) / math.sqrt(HD)
    scores_now = jnp.where(allowed_now[None, None], scores_now, big_negative)
    best = jnp.max(scores_now, axis=-1, keepdims=True)
    powers_now = jnp.exp(scores_now - best)
    total_final = jnp.sum(powers_now, axis=-1)
    accum_final = jnp.einsum(
        "kgqn,nkd->kgqd",
        powers_now.astype(jnp.bfloat16),
        values_every,
        preferred_element_type=jnp.float32,
    )
    result = accum_final / total_final[..., None]
    return (
        jnp.transpose(result, (2, 0, 1, 3)).reshape(TOK, kv_heads, groups * HD).astype(jnp.bfloat16)
    )


def solution(mesh):
    placed = (
        P("ctx", None),
        P(),
        P(),
        P(None, None, ("vis", "tp"), None),
        P(("vis", "tp"), None, None),
        P(),
        P(),
        P("ctx", ("vis", "tp")),
        P(),
        P("ctx"),
        P(),
        P(),
        P(),
        P("ctx", ("vis", "tp")),
        P(),
        P(None, "vis", "tp", None),
        P("tp", None, "vis", None),
    )
    return jax.shard_map(
        local, mesh=mesh, in_specs=placed, out_specs=P("ctx", "vis", "tp"), check_vma=False
    )
```

```python
import math

import jax
import jax.numpy as jnp
from jax import lax
from jax.experimental.layout import Layout, with_layout_constraint
from jax.sharding import PartitionSpec as P

D = 4096
HD = 128
VD = 1280
VHD = 80
TOK = 128
PCAP = 128
ICAP = 32


norm_eps = 1e-06
rope_base = 1000000.0
big_negative = -1e30


def swapped(value, axis, stride):
    return lax.ppermute(value, axis, [(i, i ^ 1 << stride) for i in range(lax.axis_size(axis))])


def layer_norm(values, scale_vec, shift_vec):
    centre = jnp.mean(values, axis=-1, keepdims=True)
    offset = values - centre
    spread = jnp.mean(offset * offset, axis=-1, keepdims=True)
    return offset * lax.rsqrt(spread + norm_eps) * scale_vec + shift_vec


def rotate(values, positions):
    half_dim = values.shape[-1] // 2
    exponent = jnp.arange(half_dim, dtype=jnp.float32) * (-2.0 / values.shape[-1])
    frequency = jnp.power(jnp.float32(rope_base), exponent)
    angles = positions.astype(jnp.float32)[:, None] * frequency[None, :]
    shape_out = (values.shape[0],) + (1,) * (values.ndim - 2) + (half_dim,)
    cosine = jnp.cos(angles).reshape(shape_out)
    sine_part = jnp.sin(angles).reshape(shape_out)
    lead_half = values[..., :half_dim]
    tail_half = values[..., half_dim:]
    return jnp.concatenate(
        [lead_half * cosine - tail_half * sine_part, tail_half * cosine + lead_half * sine_part],
        axis=-1,
    )


def row_positions(row_ids, slice_order, tokens_dev):
    shards = slice_order.shape[0]
    device_of = row_ids // tokens_dev
    local_row = row_ids % tokens_dev
    half_tok = tokens_dev // 2
    matches = device_of[:, None] == jnp.arange(shards, dtype=jnp.int32)[None, :]
    first_slice = jnp.sum(jnp.where(matches, slice_order[None, :], 0), axis=1)
    slice_ids = jnp.where(local_row < half_tok, first_slice, 2 * shards - 1 - first_slice)
    return slice_ids * half_tok + local_row % half_tok


def place_of(positions, slice_order, tokens_dev):
    shards = slice_order.shape[0]
    half_tok = tokens_dev // 2
    slice_ids = positions // half_tok
    paired = jnp.minimum(slice_ids, 2 * shards - 1 - slice_ids)
    owner_hot = (paired[..., None] == slice_order).astype(jnp.int32)
    owner_dev = jnp.sum(owner_hot * jnp.arange(shards, dtype=jnp.int32), axis=-1)
    local_row = jnp.where(slice_ids < shards, 0, half_tok) + positions % half_tok
    return (owner_dev, local_row, owner_hot)


def halving_scatter(blocks, index, count, axis="ctx"):
    remaining = count
    bit = 0
    while remaining > 1:
        lower = blocks.reshape((remaining // 2, 2) + blocks.shape[1:])
        mine = (index >> bit) & 1
        keep = jnp.where(mine == 0, lower[:, 0], lower[:, 1])
        give = jnp.where(mine == 0, lower[:, 1], lower[:, 0])
        blocks = keep + swapped(give, axis, bit)
        remaining //= 2
        bit += 1
    return blocks[0]


def doubling_gather(block, axis, index, count, bits):
    have = block[None]
    for bit in bits:
        arrived = swapped(have, axis, bit)
        mine = (index >> bit) & 1
        have = jnp.where(
            mine == 0,
            jnp.concatenate([have, arrived], axis=0),
            jnp.concatenate([arrived, have], axis=0),
        )
    order = list(bits)
    have = have.reshape((2,) * len(order) + block.shape)
    by_bit = {bit: len(order) - 1 - place for place, bit in enumerate(order)}
    wanted = [by_bit[bit] for bit in sorted(order, reverse=True)]
    have = jnp.transpose(have, wanted + list(range(len(order), have.ndim)))
    return have.reshape((count,) + block.shape)


def rotate_rows(values, positions):
    half_dim = values.shape[-1] // 2
    exponent = jnp.arange(half_dim, dtype=jnp.float32) * (-2.0 / values.shape[-1])
    frequency = jnp.power(jnp.float32(rope_base), exponent)
    angles = positions.astype(jnp.float32)[:, None] * frequency[None, :]
    cosine = jnp.cos(angles)
    sine_part = jnp.sin(angles)
    lead_half = values[..., :half_dim]
    tail_half = values[..., half_dim:]
    return jnp.concatenate(
        [lead_half * cosine - tail_half * sine_part, tail_half * cosine + lead_half * sine_part],
        axis=-1,
    )


def local(
    patch_rows,
    vit_gain,
    vit_bias,
    vit_qkv,
    vit_out,
    merge_gain,
    merge_bias,
    merge_weight,
    image_patches,
    window_ids,
    image_pos,
    slice_order,
    doc_ids,
    text_rows,
    norm_gain,
    w_query,
    w_keyval,
):
    shards = lax.axis_size("ctx")
    ctx_index = lax.axis_index("ctx")
    tp_index = lax.axis_index("tp")
    block_feats = merge_weight.shape[0]
    normed = layer_norm(patch_rows.astype(jnp.float32), vit_gain, vit_bias).astype(jnp.bfloat16)
    projected = jnp.einsum(
        "pf,fxhd->pxhd", normed, vit_qkv, preferred_element_type=jnp.float32
    ).astype(jnp.bfloat16)
    scores = jnp.einsum(
        "qhd,khd->hqk", projected[:, 0], projected[:, 1], preferred_element_type=jnp.float32
    ) / math.sqrt(VHD)
    allowed = window_ids[:, None] == window_ids[None, :]
    scores = jnp.where(allowed[None], scores, big_negative)
    powers = jnp.exp(scores - jnp.max(scores, axis=-1, keepdims=True))
    totals = jnp.sum(powers, axis=-1)
    blended = jnp.einsum(
        "hqk,khd->qhd",
        powers.astype(jnp.bfloat16),
        projected[:, 2],
        preferred_element_type=jnp.float32,
    )
    blended = (blended / jnp.transpose(totals)[:, :, None]).astype(jnp.bfloat16)
    branch_part = jnp.einsum("phd,hdf->pf", blended, vit_out, preferred_element_type=jnp.float32)
    tp_size = lax.axis_size("tp")
    vis_size = lax.axis_size("vis")
    vis_index = lax.axis_index("vis")
    tp_rows = PCAP // tp_size
    part_rows = tp_rows // vis_size
    branch_sum = halving_scatter(
        branch_part.reshape(tp_size, tp_rows, VD), tp_index, tp_size, "tp"
    )
    branch_sum = halving_scatter(
        branch_sum.reshape(vis_size, part_rows, VD), vis_index, vis_size, "vis"
    )
    first_row = tp_index * tp_rows + vis_index * part_rows
    hidden = lax.dynamic_slice_in_dim(patch_rows, first_row, part_rows, 0).astype(
        jnp.float32
    ) + branch_sum
    merged_part = layer_norm(hidden, merge_gain, merge_bias).astype(jnp.bfloat16).reshape(
        part_rows // 4, 4 * VD
    )
    merged_part = doubling_gather(
        merged_part, "vis", vis_index, vis_size, list(range(vis_size.bit_length() - 1))
    )
    merged = doubling_gather(merged_part, "tp", tp_index, tp_size, [0]).reshape(ICAP, 4 * VD)
    send_each = ICAP // shards
    slot_ids = jnp.arange(ICAP, dtype=jnp.int32)
    shard_ids = jnp.arange(shards, dtype=jnp.int32)
    live_count = jnp.sum(image_patches, axis=1) // 4
    all_pos = image_pos.reshape(shards, ICAP)
    owner_dev, local_row, owner_hot = place_of(all_pos, slice_order, TOK)
    before = jnp.cumsum(owner_hot, axis=1) - owner_hot
    rank_in = jnp.sum(before * owner_hot, axis=-1)
    is_live = slot_ids[None, :] < live_count[:, None]
    own_hot = (shard_ids == ctx_index)[:, None]
    own_owner = jnp.sum(jnp.where(own_hot, owner_dev, 0), axis=0)
    own_rank = jnp.sum(jnp.where(own_hot, rank_in, 0), axis=0)
    target_slot = own_owner * send_each + own_rank
    picker = (target_slot[None, :] == slot_ids[:, None]).astype(jnp.bfloat16)
    ordered = jnp.dot(picker, merged, preferred_element_type=jnp.float32).astype(jnp.bfloat16)
    blocks = jnp.transpose(ordered.reshape(ICAP, shards, block_feats), (1, 0, 2))
    received = lax.all_to_all(blocks, "ctx", split_axis=0, concat_axis=0, tiled=True)
    by_dest = jnp.transpose(
        received.reshape(shards, shards, send_each, block_feats), (1, 0, 2, 3)
    ).reshape(shards * ICAP, block_feats)
    partial = jnp.dot(by_dest, merge_weight, preferred_element_type=jnp.float32)
    incoming = halving_scatter(partial.reshape(shards, ICAP, -1), ctx_index, shards).astype(
        jnp.bfloat16
    )
    mine_live = ((owner_dev == ctx_index) & is_live).reshape(-1)
    column_of = (shard_ids[:, None] * send_each + rank_in).reshape(-1)
    row_hot = (
        (local_row.reshape(-1)[None, :] == jnp.arange(TOK, dtype=jnp.int32)[:, None])
        & mine_live[None, :]
    ).astype(jnp.bfloat16)
    column_hot = (column_of[:, None] == slot_ids[None, :]).astype(jnp.bfloat16)
    placing = jnp.dot(row_hot, column_hot, preferred_element_type=jnp.float32)
    is_image = jnp.sum(placing, axis=1) > 0.5
    image_part = jnp.dot(placing.astype(jnp.bfloat16), incoming, preferred_element_type=jnp.float32)
    embeds = jnp.where(is_image[:, None], image_part.astype(jnp.bfloat16), text_rows)
    full_rows = lax.all_gather(embeds, ("vis", "tp"), axis=1, tiled=True)
    widened = full_rows.astype(jnp.float32)
    normed_rows = (
        widened
        * lax.rsqrt(jnp.mean(widened * widened, axis=1, keepdims=True) + norm_eps)
        * norm_gain
    ).astype(jnp.bfloat16)
    own_positions = row_positions(
        ctx_index * TOK + jnp.arange(TOK, dtype=jnp.int32), slice_order, TOK
    )
    kv_heads = w_query.shape[1]
    groups = w_query.shape[2]
    projected_half = jnp.einsum(
        "td,dhk->thk", normed_rows, w_keyval[0], preferred_element_type=jnp.float32
    )
    own_half = jnp.where(
        tp_index == 0, rotate(projected_half, own_positions), projected_half
    ).astype(jnp.bfloat16)
    query_weights, own_half = lax.optimization_barrier((w_query, own_half))
    flat_half = with_layout_constraint(own_half.reshape(TOK, -1), Layout(major_to_minor=(0, 1)))
    gathered = lax.all_gather(flat_half, "ctx", axis=0, tiled=True)
    gathered = with_layout_constraint(gathered, Layout(major_to_minor=(0, 1)))
    gathered = gathered.reshape((shards * TOK,) + own_half.shape[1:])
    queries = jnp.einsum(
        "td,dhgk->thgk", normed_rows, query_weights, preferred_element_type=jnp.float32
    )
    queries = rotate(queries, own_positions).astype(jnp.bfloat16)
    key_pos = row_positions(jnp.arange(shards * TOK, dtype=jnp.int32), slice_order, TOK)
    doc_slices = doc_ids.reshape(2 * shards, TOK // 2)
    slice_ids = jnp.stack([slice_order, 2 * shards - 1 - slice_order], axis=1)
    slice_hot = slice_ids[:, :, None] == jnp.arange(2 * shards, dtype=jnp.int32)[None, None, :]
    key_doc = jnp.sum(
        jnp.where(slice_hot[..., None], doc_slices[None, None], 0), axis=2
    ).reshape(shards * TOK)
    own_doc = jnp.sum(
        jnp.where((shard_ids == ctx_index)[:, None], key_doc.reshape(shards, TOK), 0), axis=0
    )
    allowed_now = (key_pos[None, :] <= own_positions[:, None]) & (
        key_doc[None, :] == own_doc[:, None]
    )
    queries, allowed_now, gathered = lax.optimization_barrier((queries, allowed_now, gathered))
    partner_all = swapped(gathered, "tp", 0)
    keys_every = jnp.where(tp_index == 0, gathered, partner_all)
    values_every = jnp.where(tp_index == 0, partner_all, gathered)
    key_count = keys_every.shape[0]
    scores_now = jnp.einsum(
        "qkgd,nkd->kgqn", queries, keys_every, preferred_element_type=jnp.float32
    ) / math.sqrt(HD)
    scores_now = jnp.where(allowed_now[None, None], scores_now, big_negative)
    best = jnp.max(scores_now, axis=-1, keepdims=True)
    powers_now = jnp.exp(scores_now - best)
    total_final = jnp.sum(powers_now, axis=-1)
    accum_final = jnp.einsum(
        "kgqn,nkd->kgqd",
        powers_now.astype(jnp.bfloat16),
        values_every,
        preferred_element_type=jnp.float32,
    )
    result = accum_final / total_final[..., None]
    return (
        jnp.transpose(result, (2, 0, 1, 3)).reshape(TOK, kv_heads, groups * HD).astype(jnp.bfloat16)
    )


def solution(mesh):
    placed = (
        P("ctx", None),
        P(),
        P(),
        P(None, None, ("vis", "tp"), None),
        P(("vis", "tp"), None, None),
        P(),
        P(),
        P("ctx", ("vis", "tp")),
        P(),
        P("ctx"),
        P(),
        P(),
        P(),
        P("ctx", ("vis", "tp")),
        P(),
        P(None, "vis", "tp", None),
        P("tp", None, "vis", None),
    )
    return jax.shard_map(
        local, mesh=mesh, in_specs=placed, out_specs=P("ctx", "vis", "tp"), check_vma=False
    )
```

```python
import math

import jax
import jax.numpy as jnp
from jax import lax
from jax.sharding import PartitionSpec as P

D = 4096
HD = 128
VD = 1280
VHD = 80
TOK = 128
PCAP = 128
ICAP = 32


norm_eps = 1e-06
rope_base = 1000000.0
big_negative = -1e30


def swapped(value, axis, stride):
    return lax.ppermute(value, axis, [(i, i ^ 1 << stride) for i in range(lax.axis_size(axis))])


def layer_norm(values, scale_vec, shift_vec):
    centre = jnp.mean(values, axis=-1, keepdims=True)
    offset = values - centre
    spread = jnp.mean(offset * offset, axis=-1, keepdims=True)
    return offset * lax.rsqrt(spread + norm_eps) * scale_vec + shift_vec


def rotate(values, positions):
    half_dim = values.shape[-1] // 2
    exponent = jnp.arange(half_dim, dtype=jnp.float32) * (-2.0 / values.shape[-1])
    frequency = jnp.power(jnp.float32(rope_base), exponent)
    angles = positions.astype(jnp.float32)[:, None] * frequency[None, :]
    shape_out = (values.shape[0],) + (1,) * (values.ndim - 2) + (half_dim,)
    cosine = jnp.cos(angles).reshape(shape_out)
    sine_part = jnp.sin(angles).reshape(shape_out)
    lead_half = values[..., :half_dim]
    tail_half = values[..., half_dim:]
    return jnp.concatenate(
        [lead_half * cosine - tail_half * sine_part, tail_half * cosine + lead_half * sine_part],
        axis=-1,
    )


def row_positions(row_ids, slice_order, tokens_dev):
    shards = slice_order.shape[0]
    device_of = row_ids // tokens_dev
    local_row = row_ids % tokens_dev
    half_tok = tokens_dev // 2
    matches = device_of[:, None] == jnp.arange(shards, dtype=jnp.int32)[None, :]
    first_slice = jnp.sum(jnp.where(matches, slice_order[None, :], 0), axis=1)
    slice_ids = jnp.where(local_row < half_tok, first_slice, 2 * shards - 1 - first_slice)
    return slice_ids * half_tok + local_row % half_tok


def place_of(positions, slice_order, tokens_dev):
    shards = slice_order.shape[0]
    half_tok = tokens_dev // 2
    slice_ids = positions // half_tok
    paired = jnp.minimum(slice_ids, 2 * shards - 1 - slice_ids)
    owner_hot = (paired[..., None] == slice_order).astype(jnp.int32)
    owner_dev = jnp.sum(owner_hot * jnp.arange(shards, dtype=jnp.int32), axis=-1)
    local_row = jnp.where(slice_ids < shards, 0, half_tok) + positions % half_tok
    return (owner_dev, local_row, owner_hot)


def halving_scatter(blocks, index, count, axis="ctx"):
    remaining = count
    bit = 0
    while remaining > 1:
        lower = blocks.reshape((remaining // 2, 2) + blocks.shape[1:])
        mine = (index >> bit) & 1
        keep = jnp.where(mine == 0, lower[:, 0], lower[:, 1])
        give = jnp.where(mine == 0, lower[:, 1], lower[:, 0])
        blocks = keep + swapped(give, axis, bit)
        remaining //= 2
        bit += 1
    return blocks[0]


def doubling_gather(block, axis, index, count, bits):
    have = block[None]
    for bit in bits:
        arrived = swapped(have, axis, bit)
        mine = (index >> bit) & 1
        have = jnp.where(
            mine == 0,
            jnp.concatenate([have, arrived], axis=0),
            jnp.concatenate([arrived, have], axis=0),
        )
    order = list(bits)
    have = have.reshape((2,) * len(order) + block.shape)
    by_bit = {bit: len(order) - 1 - place for place, bit in enumerate(order)}
    wanted = [by_bit[bit] for bit in sorted(order, reverse=True)]
    have = jnp.transpose(have, wanted + list(range(len(order), have.ndim)))
    return have.reshape((count,) + block.shape)


def rotate_rows(values, positions):
    half_dim = values.shape[-1] // 2
    exponent = jnp.arange(half_dim, dtype=jnp.float32) * (-2.0 / values.shape[-1])
    frequency = jnp.power(jnp.float32(rope_base), exponent)
    angles = positions.astype(jnp.float32)[:, None] * frequency[None, :]
    cosine = jnp.cos(angles)
    sine_part = jnp.sin(angles)
    lead_half = values[..., :half_dim]
    tail_half = values[..., half_dim:]
    return jnp.concatenate(
        [lead_half * cosine - tail_half * sine_part, tail_half * cosine + lead_half * sine_part],
        axis=-1,
    )


def local(
    patch_rows,
    vit_gain,
    vit_bias,
    vit_qkv,
    vit_out,
    merge_gain,
    merge_bias,
    merge_weight,
    image_patches,
    window_ids,
    image_pos,
    slice_order,
    doc_ids,
    text_rows,
    norm_gain,
    w_query,
    w_keyval,
):
    shards = lax.axis_size("ctx")
    ctx_index = lax.axis_index("ctx")
    tp_index = lax.axis_index("tp")
    block_feats = merge_weight.shape[0]
    normed = layer_norm(patch_rows.astype(jnp.float32), vit_gain, vit_bias).astype(jnp.bfloat16)
    projected = jnp.einsum(
        "pf,fxhd->pxhd", normed, vit_qkv, preferred_element_type=jnp.float32
    ).astype(jnp.bfloat16)
    scores = jnp.einsum(
        "qhd,khd->hqk", projected[:, 0], projected[:, 1], preferred_element_type=jnp.float32
    ) / math.sqrt(VHD)
    allowed = window_ids[:, None] == window_ids[None, :]
    scores = jnp.where(allowed[None], scores, big_negative)
    powers = jnp.exp(scores - jnp.max(scores, axis=-1, keepdims=True))
    totals = jnp.sum(powers, axis=-1)
    blended = jnp.einsum(
        "hqk,khd->qhd",
        powers.astype(jnp.bfloat16),
        projected[:, 2],
        preferred_element_type=jnp.float32,
    )
    blended = (blended / jnp.transpose(totals)[:, :, None]).astype(jnp.bfloat16)
    branch_part = jnp.einsum("phd,hdf->pf", blended, vit_out, preferred_element_type=jnp.float32)
    tp_size = lax.axis_size("tp")
    vis_size = lax.axis_size("vis")
    vis_index = lax.axis_index("vis")
    tp_rows = PCAP // tp_size
    part_rows = tp_rows // vis_size
    branch_sum = halving_scatter(
        branch_part.reshape(tp_size, tp_rows, VD), tp_index, tp_size, "tp"
    )
    branch_sum = halving_scatter(
        branch_sum.reshape(vis_size, part_rows, VD), vis_index, vis_size, "vis"
    )
    first_row = tp_index * tp_rows + vis_index * part_rows
    hidden = lax.dynamic_slice_in_dim(patch_rows, first_row, part_rows, 0).astype(
        jnp.float32
    ) + branch_sum
    merged_part = layer_norm(hidden, merge_gain, merge_bias).astype(jnp.bfloat16).reshape(
        part_rows // 4, 4 * VD
    )
    merged_part = doubling_gather(
        merged_part, "vis", vis_index, vis_size, list(range(vis_size.bit_length() - 1))
    )
    merged = doubling_gather(merged_part, "tp", tp_index, tp_size, [0]).reshape(ICAP, 4 * VD)
    send_each = ICAP // shards
    slot_ids = jnp.arange(ICAP, dtype=jnp.int32)
    shard_ids = jnp.arange(shards, dtype=jnp.int32)
    live_count = jnp.sum(image_patches, axis=1) // 4
    all_pos = image_pos.reshape(shards, ICAP)
    owner_dev, local_row, owner_hot = place_of(all_pos, slice_order, TOK)
    before = jnp.cumsum(owner_hot, axis=1) - owner_hot
    rank_in = jnp.sum(before * owner_hot, axis=-1)
    is_live = slot_ids[None, :] < live_count[:, None]
    own_hot = (shard_ids == ctx_index)[:, None]
    own_owner = jnp.sum(jnp.where(own_hot, owner_dev, 0), axis=0)
    own_rank = jnp.sum(jnp.where(own_hot, rank_in, 0), axis=0)
    target_slot = own_owner * send_each + own_rank
    picker = (target_slot[None, :] == slot_ids[:, None]).astype(jnp.bfloat16)
    ordered = jnp.dot(picker, merged, preferred_element_type=jnp.float32).astype(jnp.bfloat16)
    blocks = jnp.transpose(ordered.reshape(ICAP, shards, block_feats), (1, 0, 2))
    received = lax.all_to_all(blocks, "ctx", split_axis=0, concat_axis=0, tiled=True)
    by_dest = jnp.transpose(
        received.reshape(shards, shards, send_each, block_feats), (1, 0, 2, 3)
    ).reshape(shards * ICAP, block_feats)
    partial = jnp.dot(by_dest, merge_weight, preferred_element_type=jnp.float32)
    incoming = halving_scatter(partial.reshape(shards, ICAP, -1), ctx_index, shards).astype(
        jnp.bfloat16
    )
    mine_live = ((owner_dev == ctx_index) & is_live).reshape(-1)
    column_of = (shard_ids[:, None] * send_each + rank_in).reshape(-1)
    row_hot = (
        (local_row.reshape(-1)[None, :] == jnp.arange(TOK, dtype=jnp.int32)[:, None])
        & mine_live[None, :]
    ).astype(jnp.bfloat16)
    column_hot = (column_of[:, None] == slot_ids[None, :]).astype(jnp.bfloat16)
    placing = jnp.dot(row_hot, column_hot, preferred_element_type=jnp.float32)
    is_image = jnp.sum(placing, axis=1) > 0.5
    image_part = jnp.dot(placing.astype(jnp.bfloat16), incoming, preferred_element_type=jnp.float32)
    embeds = jnp.where(is_image[:, None], image_part.astype(jnp.bfloat16), text_rows)
    full_rows = lax.all_gather(embeds, ("vis", "tp"), axis=1, tiled=True)
    widened = full_rows.astype(jnp.float32)
    normed_rows = (
        widened
        * lax.rsqrt(jnp.mean(widened * widened, axis=1, keepdims=True) + norm_eps)
        * norm_gain
    ).astype(jnp.bfloat16)
    own_positions = row_positions(
        ctx_index * TOK + jnp.arange(TOK, dtype=jnp.int32), slice_order, TOK
    )
    kv_heads = w_query.shape[1]
    groups = w_query.shape[2]
    projected_half = jnp.einsum(
        "td,dhk->thk", normed_rows, w_keyval[0], preferred_element_type=jnp.float32
    )
    own_half = jnp.where(
        tp_index == 0, rotate(projected_half, own_positions), projected_half
    ).astype(jnp.bfloat16)
    partner_half = swapped(own_half, "tp", 0)
    both_halves = jnp.where(
        tp_index == 0,
        jnp.stack([own_half, partner_half], axis=1),
        jnp.stack([partner_half, own_half], axis=1),
    )
    query_weights, both_halves = lax.optimization_barrier((w_query, both_halves))
    gathered = lax.all_gather(both_halves, "ctx", axis=0, tiled=True)
    queries = jnp.einsum(
        "td,dhgk->thgk", normed_rows, query_weights, preferred_element_type=jnp.float32
    )
    queries = rotate(queries, own_positions).astype(jnp.bfloat16)
    key_pos = row_positions(jnp.arange(shards * TOK, dtype=jnp.int32), slice_order, TOK)
    doc_slices = doc_ids.reshape(2 * shards, TOK // 2)
    slice_ids = jnp.stack([slice_order, 2 * shards - 1 - slice_order], axis=1)
    slice_hot = slice_ids[:, :, None] == jnp.arange(2 * shards, dtype=jnp.int32)[None, None, :]
    key_doc = jnp.sum(
        jnp.where(slice_hot[..., None], doc_slices[None, None], 0), axis=2
    ).reshape(shards * TOK)
    own_doc = jnp.sum(
        jnp.where((shard_ids == ctx_index)[:, None], key_doc.reshape(shards, TOK), 0), axis=0
    )
    allowed_now = (key_pos[None, :] <= own_positions[:, None]) & (
        key_doc[None, :] == own_doc[:, None]
    )
    queries, allowed_now, gathered = lax.optimization_barrier((queries, allowed_now, gathered))
    keys_every = gathered[:, 0]
    values_every = gathered[:, 1]
    key_count = keys_every.shape[0]
    scores_now = jnp.einsum(
        "qkgd,nkd->kgqn", queries, keys_every, preferred_element_type=jnp.float32
    ) / math.sqrt(HD)
    scores_now = jnp.where(allowed_now[None, None], scores_now, big_negative)
    best = jnp.max(scores_now, axis=-1, keepdims=True)
    powers_now = jnp.exp(scores_now - best)
    total_final = jnp.sum(powers_now, axis=-1)
    accum_final = jnp.einsum(
        "kgqn,nkd->kgqd",
        powers_now.astype(jnp.bfloat16),
        values_every,
        preferred_element_type=jnp.float32,
    )
    result = accum_final / total_final[..., None]
    return (
        jnp.transpose(result, (2, 0, 1, 3)).reshape(TOK, kv_heads, groups * HD).astype(jnp.bfloat16)
    )


def solution(mesh):
    placed = (
        P("ctx", None),
        P(),
        P(),
        P(None, None, ("vis", "tp"), None),
        P(("vis", "tp"), None, None),
        P(),
        P(),
        P("ctx", ("vis", "tp")),
        P(),
        P("ctx"),
        P(),
        P(),
        P(),
        P("ctx", ("vis", "tp")),
        P(),
        P(None, "vis", "tp", None),
        P("tp", None, "vis", None),
    )
    return jax.shard_map(
        local, mesh=mesh, in_specs=placed, out_specs=P("ctx", "vis", "tp"), check_vma=False
    )
```

```python
import math

import jax
import jax.numpy as jnp
from jax import lax
from jax.sharding import PartitionSpec as P

D = 4096
HD = 128
VD = 1280
VHD = 80
TOK = 128
PCAP = 128
ICAP = 32


norm_eps = 1e-06
rope_base = 1000000.0
big_negative = -1e30


def swapped(value, axis, stride):
    return lax.ppermute(value, axis, [(i, i ^ 1 << stride) for i in range(lax.axis_size(axis))])


def layer_norm(values, scale_vec, shift_vec):
    centre = jnp.mean(values, axis=-1, keepdims=True)
    offset = values - centre
    spread = jnp.mean(offset * offset, axis=-1, keepdims=True)
    return offset * lax.rsqrt(spread + norm_eps) * scale_vec + shift_vec


def rotate(values, positions):
    half_dim = values.shape[-1] // 2
    exponent = jnp.arange(half_dim, dtype=jnp.float32) * (-2.0 / values.shape[-1])
    frequency = jnp.power(jnp.float32(rope_base), exponent)
    angles = positions.astype(jnp.float32)[:, None] * frequency[None, :]
    shape_out = (values.shape[0],) + (1,) * (values.ndim - 2) + (half_dim,)
    cosine = jnp.cos(angles).reshape(shape_out)
    sine_part = jnp.sin(angles).reshape(shape_out)
    lead_half = values[..., :half_dim]
    tail_half = values[..., half_dim:]
    return jnp.concatenate(
        [lead_half * cosine - tail_half * sine_part, tail_half * cosine + lead_half * sine_part],
        axis=-1,
    )


def row_positions(row_ids, slice_order, tokens_dev):
    shards = slice_order.shape[0]
    device_of = row_ids // tokens_dev
    local_row = row_ids % tokens_dev
    half_tok = tokens_dev // 2
    matches = device_of[:, None] == jnp.arange(shards, dtype=jnp.int32)[None, :]
    first_slice = jnp.sum(jnp.where(matches, slice_order[None, :], 0), axis=1)
    slice_ids = jnp.where(local_row < half_tok, first_slice, 2 * shards - 1 - first_slice)
    return slice_ids * half_tok + local_row % half_tok


def place_of(positions, slice_order, tokens_dev):
    shards = slice_order.shape[0]
    half_tok = tokens_dev // 2
    slice_ids = positions // half_tok
    paired = jnp.minimum(slice_ids, 2 * shards - 1 - slice_ids)
    owner_hot = (paired[..., None] == slice_order).astype(jnp.int32)
    owner_dev = jnp.sum(owner_hot * jnp.arange(shards, dtype=jnp.int32), axis=-1)
    local_row = jnp.where(slice_ids < shards, 0, half_tok) + positions % half_tok
    return (owner_dev, local_row, owner_hot)


def halving_scatter(blocks, index, count, axis="ctx"):
    remaining = count
    bit = 0
    while remaining > 1:
        lower = blocks.reshape((remaining // 2, 2) + blocks.shape[1:])
        mine = (index >> bit) & 1
        keep = jnp.where(mine == 0, lower[:, 0], lower[:, 1])
        give = jnp.where(mine == 0, lower[:, 1], lower[:, 0])
        blocks = keep + swapped(give, axis, bit)
        remaining //= 2
        bit += 1
    return blocks[0]


def doubling_gather(block, axis, index, count, bits):
    have = block[None]
    for bit in bits:
        arrived = swapped(have, axis, bit)
        mine = (index >> bit) & 1
        have = jnp.where(
            mine == 0,
            jnp.concatenate([have, arrived], axis=0),
            jnp.concatenate([arrived, have], axis=0),
        )
    order = list(bits)
    have = have.reshape((2,) * len(order) + block.shape)
    by_bit = {bit: len(order) - 1 - place for place, bit in enumerate(order)}
    wanted = [by_bit[bit] for bit in sorted(order, reverse=True)]
    have = jnp.transpose(have, wanted + list(range(len(order), have.ndim)))
    return have.reshape((count,) + block.shape)


def rotate_rows(values, positions):
    half_dim = values.shape[-1] // 2
    exponent = jnp.arange(half_dim, dtype=jnp.float32) * (-2.0 / values.shape[-1])
    frequency = jnp.power(jnp.float32(rope_base), exponent)
    angles = positions.astype(jnp.float32)[:, None] * frequency[None, :]
    cosine = jnp.cos(angles)
    sine_part = jnp.sin(angles)
    lead_half = values[..., :half_dim]
    tail_half = values[..., half_dim:]
    return jnp.concatenate(
        [lead_half * cosine - tail_half * sine_part, tail_half * cosine + lead_half * sine_part],
        axis=-1,
    )


def local(
    patch_rows,
    vit_gain,
    vit_bias,
    vit_qkv,
    vit_out,
    merge_gain,
    merge_bias,
    merge_weight,
    image_patches,
    window_ids,
    image_pos,
    slice_order,
    doc_ids,
    text_rows,
    norm_gain,
    w_query,
    w_keyval,
):
    shards = lax.axis_size("ctx")
    ctx_index = lax.axis_index("ctx")
    tp_index = lax.axis_index("tp")
    block_feats = merge_weight.shape[0]
    normed = layer_norm(patch_rows.astype(jnp.float32), vit_gain, vit_bias).astype(jnp.bfloat16)
    projected = jnp.einsum(
        "pf,fxhd->pxhd", normed, vit_qkv, preferred_element_type=jnp.float32
    ).astype(jnp.bfloat16)
    scores = jnp.einsum(
        "qhd,khd->hqk", projected[:, 0], projected[:, 1], preferred_element_type=jnp.float32
    ) / math.sqrt(VHD)
    allowed = window_ids[:, None] == window_ids[None, :]
    scores = jnp.where(allowed[None], scores, big_negative)
    powers = jnp.exp(scores - jnp.max(scores, axis=-1, keepdims=True))
    totals = jnp.sum(powers, axis=-1)
    blended = jnp.einsum(
        "hqk,khd->qhd",
        powers.astype(jnp.bfloat16),
        projected[:, 2],
        preferred_element_type=jnp.float32,
    )
    blended = (blended / jnp.transpose(totals)[:, :, None]).astype(jnp.bfloat16)
    branch_part = jnp.einsum("phd,hdf->pf", blended, vit_out, preferred_element_type=jnp.float32)
    tp_size = lax.axis_size("tp")
    vis_size = lax.axis_size("vis")
    vis_index = lax.axis_index("vis")
    tp_rows = PCAP // tp_size
    part_rows = tp_rows // vis_size
    branch_sum = halving_scatter(
        branch_part.reshape(tp_size, tp_rows, VD), tp_index, tp_size, "tp"
    )
    branch_sum = halving_scatter(
        branch_sum.reshape(vis_size, part_rows, VD), vis_index, vis_size, "vis"
    )
    first_row = tp_index * tp_rows + vis_index * part_rows
    hidden = lax.dynamic_slice_in_dim(patch_rows, first_row, part_rows, 0).astype(
        jnp.float32
    ) + branch_sum
    merged_part = layer_norm(hidden, merge_gain, merge_bias).astype(jnp.bfloat16).reshape(
        part_rows // 4, 4 * VD
    )
    merged_part = doubling_gather(
        merged_part, "vis", vis_index, vis_size, list(range(vis_size.bit_length() - 1))
    )
    merged = doubling_gather(merged_part, "tp", tp_index, tp_size, [0]).reshape(ICAP, 4 * VD)
    send_each = ICAP // shards
    slot_ids = jnp.arange(ICAP, dtype=jnp.int32)
    shard_ids = jnp.arange(shards, dtype=jnp.int32)
    live_count = jnp.sum(image_patches, axis=1) // 4
    all_pos = image_pos.reshape(shards, ICAP)
    owner_dev, local_row, owner_hot = place_of(all_pos, slice_order, TOK)
    before = jnp.cumsum(owner_hot, axis=1) - owner_hot
    rank_in = jnp.sum(before * owner_hot, axis=-1)
    is_live = slot_ids[None, :] < live_count[:, None]
    own_hot = (shard_ids == ctx_index)[:, None]
    own_owner = jnp.sum(jnp.where(own_hot, owner_dev, 0), axis=0)
    own_rank = jnp.sum(jnp.where(own_hot, rank_in, 0), axis=0)
    target_slot = own_owner * send_each + own_rank
    picker = (target_slot[None, :] == slot_ids[:, None]).astype(jnp.bfloat16)
    ordered = jnp.dot(picker, merged, preferred_element_type=jnp.float32).astype(jnp.bfloat16)
    blocks = jnp.transpose(ordered.reshape(ICAP, shards, block_feats), (1, 0, 2))
    by_shift = [lax.dynamic_index_in_dim(blocks, ctx_index, 0, keepdims=False)]
    for shift in range(1, shards):
        outgoing = lax.dynamic_index_in_dim(blocks, (ctx_index + shift) % shards, 0, keepdims=False)
        by_shift.append(
            lax.ppermute(outgoing, "ctx", [(i, (i + shift) % shards) for i in range(shards)])
        )
    by_shift = jnp.stack(by_shift, axis=0)
    source_hot = (
        shard_ids[None, :] == (ctx_index - shard_ids[:, None]) % shards
    ).astype(jnp.bfloat16)
    received = jnp.einsum(
        "sk,kqf->sqf", source_hot, by_shift, preferred_element_type=jnp.float32
    ).astype(jnp.bfloat16)
    by_dest = jnp.transpose(
        received.reshape(shards, shards, send_each, block_feats), (1, 0, 2, 3)
    ).reshape(shards * ICAP, block_feats)
    partial = jnp.dot(by_dest, merge_weight, preferred_element_type=jnp.float32)
    incoming = halving_scatter(partial.reshape(shards, ICAP, -1), ctx_index, shards).astype(
        jnp.bfloat16
    )
    mine_live = ((owner_dev == ctx_index) & is_live).reshape(-1)
    column_of = (shard_ids[:, None] * send_each + rank_in).reshape(-1)
    row_hot = (
        (local_row.reshape(-1)[None, :] == jnp.arange(TOK, dtype=jnp.int32)[:, None])
        & mine_live[None, :]
    ).astype(jnp.bfloat16)
    column_hot = (column_of[:, None] == slot_ids[None, :]).astype(jnp.bfloat16)
    placing = jnp.dot(row_hot, column_hot, preferred_element_type=jnp.float32)
    is_image = jnp.sum(placing, axis=1) > 0.5
    image_part = jnp.dot(placing.astype(jnp.bfloat16), incoming, preferred_element_type=jnp.float32)
    embeds = jnp.where(is_image[:, None], image_part.astype(jnp.bfloat16), text_rows)
    full_rows = lax.all_gather(embeds, ("vis", "tp"), axis=1, tiled=True)
    widened = full_rows.astype(jnp.float32)
    normed_rows = (
        widened
        * lax.rsqrt(jnp.mean(widened * widened, axis=1, keepdims=True) + norm_eps)
        * norm_gain
    ).astype(jnp.bfloat16)
    own_positions = row_positions(
        ctx_index * TOK + jnp.arange(TOK, dtype=jnp.int32), slice_order, TOK
    )
    kv_heads = w_query.shape[1]
    groups = w_query.shape[2]
    projected_half = jnp.einsum(
        "td,dhk->thk", normed_rows, w_keyval[0], preferred_element_type=jnp.float32
    )
    own_half = jnp.where(
        tp_index == 0, rotate(projected_half, own_positions), projected_half
    ).astype(jnp.bfloat16)
    query_weights, own_half = lax.optimization_barrier((w_query, own_half))
    gathered = lax.all_gather(own_half, "ctx", axis=0, tiled=True)
    queries = jnp.einsum(
        "td,dhgk->thgk", normed_rows, query_weights, preferred_element_type=jnp.float32
    )
    queries = rotate(queries, own_positions).astype(jnp.bfloat16)
    key_pos = row_positions(jnp.arange(shards * TOK, dtype=jnp.int32), slice_order, TOK)
    doc_slices = doc_ids.reshape(2 * shards, TOK // 2)
    slice_ids = jnp.stack([slice_order, 2 * shards - 1 - slice_order], axis=1)
    slice_hot = slice_ids[:, :, None] == jnp.arange(2 * shards, dtype=jnp.int32)[None, None, :]
    key_doc = jnp.sum(
        jnp.where(slice_hot[..., None], doc_slices[None, None], 0), axis=2
    ).reshape(shards * TOK)
    own_doc = jnp.sum(
        jnp.where((shard_ids == ctx_index)[:, None], key_doc.reshape(shards, TOK), 0), axis=0
    )
    allowed_now = (key_pos[None, :] <= own_positions[:, None]) & (
        key_doc[None, :] == own_doc[:, None]
    )
    queries, allowed_now, gathered = lax.optimization_barrier((queries, allowed_now, gathered))
    partner_all = swapped(gathered, "tp", 0)
    keys_every = jnp.where(tp_index == 0, gathered, partner_all)
    values_every = jnp.where(tp_index == 0, partner_all, gathered)
    key_count = keys_every.shape[0]
    scores_now = jnp.einsum(
        "qkgd,nkd->kgqn", queries, keys_every, preferred_element_type=jnp.float32
    ) / math.sqrt(HD)
    scores_now = jnp.where(allowed_now[None, None], scores_now, big_negative)
    best = jnp.max(scores_now, axis=-1, keepdims=True)
    powers_now = jnp.exp(scores_now - best)
    total_final = jnp.sum(powers_now, axis=-1)
    accum_final = jnp.einsum(
        "kgqn,nkd->kgqd",
        powers_now.astype(jnp.bfloat16),
        values_every,
        preferred_element_type=jnp.float32,
    )
    result = accum_final / total_final[..., None]
    return (
        jnp.transpose(result, (2, 0, 1, 3)).reshape(TOK, kv_heads, groups * HD).astype(jnp.bfloat16)
    )


def solution(mesh):
    placed = (
        P("ctx", None),
        P(),
        P(),
        P(None, None, ("vis", "tp"), None),
        P(("vis", "tp"), None, None),
        P(),
        P(),
        P("ctx", ("vis", "tp")),
        P(),
        P("ctx"),
        P(),
        P(),
        P(),
        P("ctx", ("vis", "tp")),
        P(),
        P(None, "vis", "tp", None),
        P("tp", None, "vis", None),
    )
    return jax.shard_map(
        local, mesh=mesh, in_specs=placed, out_specs=P("ctx", "vis", "tp"), check_vma=False
    )
```

```python
import math

import jax
import jax.numpy as jnp
from jax import lax
from jax.sharding import PartitionSpec as P

D = 4096
HD = 128
VD = 1280
VHD = 80
TOK = 128
PCAP = 128
ICAP = 32


norm_eps = 1e-06
rope_base = 1000000.0
big_negative = -1e30


def swapped(value, axis, stride):
    return lax.ppermute(value, axis, [(i, i ^ 1 << stride) for i in range(lax.axis_size(axis))])


def layer_norm(values, scale_vec, shift_vec):
    centre = jnp.mean(values, axis=-1, keepdims=True)
    offset = values - centre
    spread = jnp.mean(offset * offset, axis=-1, keepdims=True)
    return offset * lax.rsqrt(spread + norm_eps) * scale_vec + shift_vec


def rotate(values, positions):
    half_dim = values.shape[-1] // 2
    exponent = jnp.arange(half_dim, dtype=jnp.float32) * (-2.0 / values.shape[-1])
    frequency = jnp.power(jnp.float32(rope_base), exponent)
    angles = positions.astype(jnp.float32)[:, None] * frequency[None, :]
    shape_out = (values.shape[0],) + (1,) * (values.ndim - 2) + (half_dim,)
    cosine = jnp.cos(angles).reshape(shape_out)
    sine_part = jnp.sin(angles).reshape(shape_out)
    lead_half = values[..., :half_dim]
    tail_half = values[..., half_dim:]
    return jnp.concatenate(
        [lead_half * cosine - tail_half * sine_part, tail_half * cosine + lead_half * sine_part],
        axis=-1,
    )


def row_positions(row_ids, slice_order, tokens_dev):
    shards = slice_order.shape[0]
    device_of = row_ids // tokens_dev
    local_row = row_ids % tokens_dev
    half_tok = tokens_dev // 2
    matches = device_of[:, None] == jnp.arange(shards, dtype=jnp.int32)[None, :]
    first_slice = jnp.sum(jnp.where(matches, slice_order[None, :], 0), axis=1)
    slice_ids = jnp.where(local_row < half_tok, first_slice, 2 * shards - 1 - first_slice)
    return slice_ids * half_tok + local_row % half_tok


def place_of(positions, slice_order, tokens_dev):
    shards = slice_order.shape[0]
    half_tok = tokens_dev // 2
    slice_ids = positions // half_tok
    paired = jnp.minimum(slice_ids, 2 * shards - 1 - slice_ids)
    owner_hot = (paired[..., None] == slice_order).astype(jnp.int32)
    owner_dev = jnp.sum(owner_hot * jnp.arange(shards, dtype=jnp.int32), axis=-1)
    local_row = jnp.where(slice_ids < shards, 0, half_tok) + positions % half_tok
    return (owner_dev, local_row, owner_hot)


def halving_scatter(blocks, index, count, axis="ctx"):
    remaining = count
    bit = 0
    while remaining > 1:
        lower = blocks.reshape((remaining // 2, 2) + blocks.shape[1:])
        mine = (index >> bit) & 1
        keep = jnp.where(mine == 0, lower[:, 0], lower[:, 1])
        give = jnp.where(mine == 0, lower[:, 1], lower[:, 0])
        blocks = keep + swapped(give, axis, bit)
        remaining //= 2
        bit += 1
    return blocks[0]


def doubling_gather(block, axis, index, count, bits):
    have = block[None]
    for bit in bits:
        arrived = swapped(have, axis, bit)
        mine = (index >> bit) & 1
        have = jnp.where(
            mine == 0,
            jnp.concatenate([have, arrived], axis=0),
            jnp.concatenate([arrived, have], axis=0),
        )
    order = list(bits)
    have = have.reshape((2,) * len(order) + block.shape)
    by_bit = {bit: len(order) - 1 - place for place, bit in enumerate(order)}
    wanted = [by_bit[bit] for bit in sorted(order, reverse=True)]
    have = jnp.transpose(have, wanted + list(range(len(order), have.ndim)))
    return have.reshape((count,) + block.shape)


def rotate_rows(values, positions):
    half_dim = values.shape[-1] // 2
    exponent = jnp.arange(half_dim, dtype=jnp.float32) * (-2.0 / values.shape[-1])
    frequency = jnp.power(jnp.float32(rope_base), exponent)
    angles = positions.astype(jnp.float32)[:, None] * frequency[None, :]
    cosine = jnp.cos(angles)
    sine_part = jnp.sin(angles)
    lead_half = values[..., :half_dim]
    tail_half = values[..., half_dim:]
    return jnp.concatenate(
        [lead_half * cosine - tail_half * sine_part, tail_half * cosine + lead_half * sine_part],
        axis=-1,
    )


def local(
    patch_rows,
    vit_gain,
    vit_bias,
    vit_qkv,
    vit_out,
    merge_gain,
    merge_bias,
    merge_weight,
    image_patches,
    window_ids,
    image_pos,
    slice_order,
    doc_ids,
    text_rows,
    norm_gain,
    w_query,
    w_keyval,
):
    shards = lax.axis_size("ctx")
    ctx_index = lax.axis_index("ctx")
    tp_index = lax.axis_index("tp")
    block_feats = merge_weight.shape[0]
    normed = layer_norm(patch_rows.astype(jnp.float32), vit_gain, vit_bias).astype(jnp.bfloat16)
    projected = jnp.einsum(
        "pf,fxhd->pxhd", normed, vit_qkv, preferred_element_type=jnp.float32
    ).astype(jnp.bfloat16)
    scores = jnp.einsum(
        "qhd,khd->hqk", projected[:, 0], projected[:, 1], preferred_element_type=jnp.float32
    ) / math.sqrt(VHD)
    allowed = window_ids[:, None] == window_ids[None, :]
    scores = jnp.where(allowed[None], scores, big_negative)
    powers = jnp.exp(scores - jnp.max(scores, axis=-1, keepdims=True))
    totals = jnp.sum(powers, axis=-1)
    blended = jnp.einsum(
        "hqk,khd->qhd",
        powers.astype(jnp.bfloat16),
        projected[:, 2],
        preferred_element_type=jnp.float32,
    )
    blended = (blended / jnp.transpose(totals)[:, :, None]).astype(jnp.bfloat16)
    branch_part = jnp.einsum("phd,hdf->pf", blended, vit_out, preferred_element_type=jnp.float32)
    tp_size = lax.axis_size("tp")
    vis_size = lax.axis_size("vis")
    vis_index = lax.axis_index("vis")
    tp_rows = PCAP // tp_size
    part_rows = tp_rows // vis_size
    branch_sum = halving_scatter(
        branch_part.reshape(tp_size, tp_rows, VD), tp_index, tp_size, "tp"
    )
    branch_sum = halving_scatter(
        branch_sum.reshape(vis_size, part_rows, VD), vis_index, vis_size, "vis"
    )
    first_row = tp_index * tp_rows + vis_index * part_rows
    hidden = lax.dynamic_slice_in_dim(patch_rows, first_row, part_rows, 0).astype(
        jnp.float32
    ) + branch_sum
    merged_part = layer_norm(hidden, merge_gain, merge_bias).astype(jnp.bfloat16).reshape(
        part_rows // 4, 4 * VD
    )
    merged_part = doubling_gather(
        merged_part, "vis", vis_index, vis_size, list(range(vis_size.bit_length() - 1))
    )
    merged = doubling_gather(merged_part, "tp", tp_index, tp_size, [0]).reshape(ICAP, 4 * VD)
    send_each = ICAP // shards
    slot_ids = jnp.arange(ICAP, dtype=jnp.int32)
    shard_ids = jnp.arange(shards, dtype=jnp.int32)
    live_count = jnp.sum(image_patches, axis=1) // 4
    all_pos = image_pos.reshape(shards, ICAP)
    owner_dev, local_row, owner_hot = place_of(all_pos, slice_order, TOK)
    before = jnp.cumsum(owner_hot, axis=1) - owner_hot
    rank_in = jnp.sum(before * owner_hot, axis=-1)
    is_live = slot_ids[None, :] < live_count[:, None]
    own_hot = (shard_ids == ctx_index)[:, None]
    own_owner = jnp.sum(jnp.where(own_hot, owner_dev, 0), axis=0)
    own_rank = jnp.sum(jnp.where(own_hot, rank_in, 0), axis=0)
    target_slot = own_owner * send_each + own_rank
    picker = (target_slot[None, :] == slot_ids[:, None]).astype(jnp.bfloat16)
    ordered = jnp.dot(picker, merged, preferred_element_type=jnp.float32).astype(jnp.bfloat16)
    blocks = jnp.transpose(ordered.reshape(ICAP, shards, block_feats), (1, 0, 2))
    by_shift = [lax.dynamic_index_in_dim(blocks, ctx_index, 0, keepdims=False)]
    for shift in range(1, shards):
        outgoing = lax.dynamic_index_in_dim(blocks, (ctx_index + shift) % shards, 0, keepdims=False)
        by_shift.append(
            lax.ppermute(outgoing, "ctx", [(i, (i + shift) % shards) for i in range(shards)])
        )
    by_shift = jnp.stack(by_shift, axis=0)
    source_hot = (
        shard_ids[None, :] == (ctx_index - shard_ids[:, None]) % shards
    ).astype(jnp.bfloat16)
    received = jnp.einsum(
        "sk,kqf->sqf", source_hot, by_shift, preferred_element_type=jnp.float32
    ).astype(jnp.bfloat16)
    by_dest = jnp.transpose(
        received.reshape(shards, shards, send_each, block_feats), (1, 0, 2, 3)
    ).reshape(shards * ICAP, block_feats)
    partial = jnp.dot(by_dest, merge_weight, preferred_element_type=jnp.float32)
    partial = partial.reshape(shards, ICAP, -1)
    summed = lax.dynamic_index_in_dim(partial, ctx_index, 0, keepdims=False)
    for shift in range(1, shards):
        outgoing = lax.dynamic_index_in_dim(partial, (ctx_index + shift) % shards, 0, keepdims=False)
        summed = summed + lax.ppermute(
            outgoing, "ctx", [(i, (i + shift) % shards) for i in range(shards)]
        )
    incoming = summed.astype(jnp.bfloat16)
    mine_live = ((owner_dev == ctx_index) & is_live).reshape(-1)
    column_of = (shard_ids[:, None] * send_each + rank_in).reshape(-1)
    row_hot = (
        (local_row.reshape(-1)[None, :] == jnp.arange(TOK, dtype=jnp.int32)[:, None])
        & mine_live[None, :]
    ).astype(jnp.bfloat16)
    column_hot = (column_of[:, None] == slot_ids[None, :]).astype(jnp.bfloat16)
    placing = jnp.dot(row_hot, column_hot, preferred_element_type=jnp.float32)
    is_image = jnp.sum(placing, axis=1) > 0.5
    image_part = jnp.dot(placing.astype(jnp.bfloat16), incoming, preferred_element_type=jnp.float32)
    embeds = jnp.where(is_image[:, None], image_part.astype(jnp.bfloat16), text_rows)
    full_rows = lax.all_gather(embeds, ("vis", "tp"), axis=1, tiled=True)
    widened = full_rows.astype(jnp.float32)
    normed_rows = (
        widened
        * lax.rsqrt(jnp.mean(widened * widened, axis=1, keepdims=True) + norm_eps)
        * norm_gain
    ).astype(jnp.bfloat16)
    own_positions = row_positions(
        ctx_index * TOK + jnp.arange(TOK, dtype=jnp.int32), slice_order, TOK
    )
    kv_heads = w_query.shape[1]
    groups = w_query.shape[2]
    projected_half = jnp.einsum(
        "td,dhk->thk", normed_rows, w_keyval[0], preferred_element_type=jnp.float32
    )
    own_half = jnp.where(
        tp_index == 0, rotate(projected_half, own_positions), projected_half
    ).astype(jnp.bfloat16)
    query_weights, own_half = lax.optimization_barrier((w_query, own_half))
    gathered = lax.all_gather(own_half, "ctx", axis=0, tiled=True)
    queries = jnp.einsum(
        "td,dhgk->thgk", normed_rows, query_weights, preferred_element_type=jnp.float32
    )
    queries = rotate(queries, own_positions).astype(jnp.bfloat16)
    key_pos = row_positions(jnp.arange(shards * TOK, dtype=jnp.int32), slice_order, TOK)
    doc_slices = doc_ids.reshape(2 * shards, TOK // 2)
    slice_ids = jnp.stack([slice_order, 2 * shards - 1 - slice_order], axis=1)
    slice_hot = slice_ids[:, :, None] == jnp.arange(2 * shards, dtype=jnp.int32)[None, None, :]
    key_doc = jnp.sum(
        jnp.where(slice_hot[..., None], doc_slices[None, None], 0), axis=2
    ).reshape(shards * TOK)
    own_doc = jnp.sum(
        jnp.where((shard_ids == ctx_index)[:, None], key_doc.reshape(shards, TOK), 0), axis=0
    )
    allowed_now = (key_pos[None, :] <= own_positions[:, None]) & (
        key_doc[None, :] == own_doc[:, None]
    )
    queries, allowed_now, gathered = lax.optimization_barrier((queries, allowed_now, gathered))
    partner_all = swapped(gathered, "tp", 0)
    keys_every = jnp.where(tp_index == 0, gathered, partner_all)
    values_every = jnp.where(tp_index == 0, partner_all, gathered)
    key_count = keys_every.shape[0]
    scores_now = jnp.einsum(
        "qkgd,nkd->kgqn", queries, keys_every, preferred_element_type=jnp.float32
    ) / math.sqrt(HD)
    scores_now = jnp.where(allowed_now[None, None], scores_now, big_negative)
    best = jnp.max(scores_now, axis=-1, keepdims=True)
    powers_now = jnp.exp(scores_now - best)
    total_final = jnp.sum(powers_now, axis=-1)
    accum_final = jnp.einsum(
        "kgqn,nkd->kgqd",
        powers_now.astype(jnp.bfloat16),
        values_every,
        preferred_element_type=jnp.float32,
    )
    result = accum_final / total_final[..., None]
    return (
        jnp.transpose(result, (2, 0, 1, 3)).reshape(TOK, kv_heads, groups * HD).astype(jnp.bfloat16)
    )


def solution(mesh):
    placed = (
        P("ctx", None),
        P(),
        P(),
        P(None, None, ("vis", "tp"), None),
        P(("vis", "tp"), None, None),
        P(),
        P(),
        P("ctx", ("vis", "tp")),
        P(),
        P("ctx"),
        P(),
        P(),
        P(),
        P("ctx", ("vis", "tp")),
        P(),
        P(None, "vis", "tp", None),
        P("tp", None, "vis", None),
    )
    return jax.shard_map(
        local, mesh=mesh, in_specs=placed, out_specs=P("ctx", "vis", "tp"), check_vma=False
    )
```

```python
import math

import jax
import jax.numpy as jnp
from jax import lax
from jax.sharding import PartitionSpec as P

D = 4096
HD = 128
VD = 1280
VHD = 80
TOK = 128
PCAP = 128
ICAP = 32


norm_eps = 1e-06
rope_base = 1000000.0
big_negative = -1e30


def swapped(value, axis, stride):
    return lax.ppermute(value, axis, [(i, i ^ 1 << stride) for i in range(lax.axis_size(axis))])


def layer_norm(values, scale_vec, shift_vec):
    centre = jnp.mean(values, axis=-1, keepdims=True)
    offset = values - centre
    spread = jnp.mean(offset * offset, axis=-1, keepdims=True)
    return offset * lax.rsqrt(spread + norm_eps) * scale_vec + shift_vec


def rotate(values, positions):
    half_dim = values.shape[-1] // 2
    exponent = jnp.arange(half_dim, dtype=jnp.float32) * (-2.0 / values.shape[-1])
    frequency = jnp.power(jnp.float32(rope_base), exponent)
    angles = positions.astype(jnp.float32)[:, None] * frequency[None, :]
    shape_out = (values.shape[0],) + (1,) * (values.ndim - 2) + (half_dim,)
    cosine = jnp.cos(angles).reshape(shape_out)
    sine_part = jnp.sin(angles).reshape(shape_out)
    lead_half = values[..., :half_dim]
    tail_half = values[..., half_dim:]
    return jnp.concatenate(
        [lead_half * cosine - tail_half * sine_part, tail_half * cosine + lead_half * sine_part],
        axis=-1,
    )


def row_positions(row_ids, slice_order, tokens_dev):
    shards = slice_order.shape[0]
    device_of = row_ids // tokens_dev
    local_row = row_ids % tokens_dev
    half_tok = tokens_dev // 2
    matches = device_of[:, None] == jnp.arange(shards, dtype=jnp.int32)[None, :]
    first_slice = jnp.sum(jnp.where(matches, slice_order[None, :], 0), axis=1)
    slice_ids = jnp.where(local_row < half_tok, first_slice, 2 * shards - 1 - first_slice)
    return slice_ids * half_tok + local_row % half_tok


def place_of(positions, slice_order, tokens_dev):
    shards = slice_order.shape[0]
    half_tok = tokens_dev // 2
    slice_ids = positions // half_tok
    paired = jnp.minimum(slice_ids, 2 * shards - 1 - slice_ids)
    owner_hot = (paired[..., None] == slice_order).astype(jnp.int32)
    owner_dev = jnp.sum(owner_hot * jnp.arange(shards, dtype=jnp.int32), axis=-1)
    local_row = jnp.where(slice_ids < shards, 0, half_tok) + positions % half_tok
    return (owner_dev, local_row, owner_hot)


def halving_scatter(blocks, index, count, axis="ctx"):
    remaining = count
    bit = 0
    while remaining > 1:
        lower = blocks.reshape((remaining // 2, 2) + blocks.shape[1:])
        mine = (index >> bit) & 1
        keep = jnp.where(mine == 0, lower[:, 0], lower[:, 1])
        give = jnp.where(mine == 0, lower[:, 1], lower[:, 0])
        blocks = keep + swapped(give, axis, bit)
        remaining //= 2
        bit += 1
    return blocks[0]


def doubling_gather(block, axis, index, count, bits):
    have = block[None]
    for bit in bits:
        arrived = swapped(have, axis, bit)
        mine = (index >> bit) & 1
        have = jnp.where(
            mine == 0,
            jnp.concatenate([have, arrived], axis=0),
            jnp.concatenate([arrived, have], axis=0),
        )
    order = list(bits)
    have = have.reshape((2,) * len(order) + block.shape)
    by_bit = {bit: len(order) - 1 - place for place, bit in enumerate(order)}
    wanted = [by_bit[bit] for bit in sorted(order, reverse=True)]
    have = jnp.transpose(have, wanted + list(range(len(order), have.ndim)))
    return have.reshape((count,) + block.shape)


def rotate_rows(values, positions):
    half_dim = values.shape[-1] // 2
    exponent = jnp.arange(half_dim, dtype=jnp.float32) * (-2.0 / values.shape[-1])
    frequency = jnp.power(jnp.float32(rope_base), exponent)
    angles = positions.astype(jnp.float32)[:, None] * frequency[None, :]
    cosine = jnp.cos(angles)
    sine_part = jnp.sin(angles)
    lead_half = values[..., :half_dim]
    tail_half = values[..., half_dim:]
    return jnp.concatenate(
        [lead_half * cosine - tail_half * sine_part, tail_half * cosine + lead_half * sine_part],
        axis=-1,
    )


def local(
    patch_rows,
    vit_gain,
    vit_bias,
    vit_qkv,
    vit_out,
    merge_gain,
    merge_bias,
    merge_weight,
    image_patches,
    window_ids,
    image_pos,
    slice_order,
    doc_ids,
    text_rows,
    norm_gain,
    w_query,
    w_keyval,
):
    shards = lax.axis_size("ctx")
    ctx_index = lax.axis_index("ctx")
    tp_index = lax.axis_index("tp")
    block_feats = merge_weight.shape[0]
    normed = layer_norm(patch_rows.astype(jnp.float32), vit_gain, vit_bias).astype(jnp.bfloat16)
    projected = jnp.einsum(
        "pf,fxhd->pxhd", normed, vit_qkv, preferred_element_type=jnp.float32
    ).astype(jnp.bfloat16)
    scores = jnp.einsum(
        "qhd,khd->hqk", projected[:, 0], projected[:, 1], preferred_element_type=jnp.float32
    ) / math.sqrt(VHD)
    allowed = window_ids[:, None] == window_ids[None, :]
    scores = jnp.where(allowed[None], scores, big_negative)
    powers = jnp.exp(scores - jnp.max(scores, axis=-1, keepdims=True))
    totals = jnp.sum(powers, axis=-1)
    blended = jnp.einsum(
        "hqk,khd->qhd",
        powers.astype(jnp.bfloat16),
        projected[:, 2],
        preferred_element_type=jnp.float32,
    )
    blended = (blended / jnp.transpose(totals)[:, :, None]).astype(jnp.bfloat16)
    branch_part = jnp.einsum("phd,hdf->pf", blended, vit_out, preferred_element_type=jnp.float32)
    tp_size = lax.axis_size("tp")
    vis_size = lax.axis_size("vis")
    vis_index = lax.axis_index("vis")
    tp_rows = PCAP // tp_size
    part_rows = tp_rows // vis_size
    branch_sum = halving_scatter(
        branch_part.reshape(tp_size, tp_rows, VD), tp_index, tp_size, "tp"
    )
    branch_sum = halving_scatter(
        branch_sum.reshape(vis_size, part_rows, VD), vis_index, vis_size, "vis"
    )
    first_row = tp_index * tp_rows + vis_index * part_rows
    hidden = lax.dynamic_slice_in_dim(patch_rows, first_row, part_rows, 0).astype(
        jnp.float32
    ) + branch_sum
    merged_part = layer_norm(hidden, merge_gain, merge_bias).astype(jnp.bfloat16).reshape(
        part_rows // 4, 4 * VD
    )
    merged_part = doubling_gather(
        merged_part, "vis", vis_index, vis_size, list(range(vis_size.bit_length() - 1))
    )
    merged = doubling_gather(merged_part, "tp", tp_index, tp_size, [0]).reshape(ICAP, 4 * VD)
    send_each = ICAP // shards
    slot_ids = jnp.arange(ICAP, dtype=jnp.int32)
    shard_ids = jnp.arange(shards, dtype=jnp.int32)
    live_count = jnp.sum(image_patches, axis=1) // 4
    all_pos = image_pos.reshape(shards, ICAP)
    owner_dev, local_row, owner_hot = place_of(all_pos, slice_order, TOK)
    before = jnp.cumsum(owner_hot, axis=1) - owner_hot
    rank_in = jnp.sum(before * owner_hot, axis=-1)
    is_live = slot_ids[None, :] < live_count[:, None]
    own_hot = (shard_ids == ctx_index)[:, None]
    own_owner = jnp.sum(jnp.where(own_hot, owner_dev, 0), axis=0)
    own_rank = jnp.sum(jnp.where(own_hot, rank_in, 0), axis=0)
    target_slot = own_owner * send_each + own_rank
    picker = (target_slot[None, :] == slot_ids[:, None]).astype(jnp.bfloat16)
    ordered = jnp.dot(picker, merged, preferred_element_type=jnp.float32).astype(jnp.bfloat16)
    blocks = jnp.transpose(ordered.reshape(ICAP, shards, block_feats), (1, 0, 2))
    by_shift = [lax.dynamic_index_in_dim(blocks, ctx_index, 0, keepdims=False)]
    for shift in range(1, shards):
        outgoing = lax.dynamic_index_in_dim(blocks, (ctx_index + shift) % shards, 0, keepdims=False)
        by_shift.append(
            lax.ppermute(outgoing, "ctx", [(i, (i + shift) % shards) for i in range(shards)])
        )
    by_shift = jnp.stack(by_shift, axis=0)
    source_hot = (
        shard_ids[None, :] == (ctx_index - shard_ids[:, None]) % shards
    ).astype(jnp.bfloat16)
    received = jnp.einsum(
        "sk,kqf->sqf", source_hot, by_shift, preferred_element_type=jnp.float32
    ).astype(jnp.bfloat16)
    by_dest = jnp.transpose(
        received.reshape(shards, shards, send_each, block_feats), (1, 0, 2, 3)
    ).reshape(shards * ICAP, block_feats)
    partial = jnp.dot(by_dest, merge_weight, preferred_element_type=jnp.float32)
    partial = partial.reshape(shards, ICAP, -1)
    summed = lax.dynamic_index_in_dim(partial, ctx_index, 0, keepdims=False)
    for shift in range(1, shards):
        outgoing = lax.dynamic_index_in_dim(partial, (ctx_index + shift) % shards, 0, keepdims=False)
        summed = summed + lax.ppermute(
            outgoing, "ctx", [(i, (i + shift) % shards) for i in range(shards)]
        )
    incoming = summed.astype(jnp.bfloat16)
    mine_live = ((owner_dev == ctx_index) & is_live).reshape(-1)
    column_of = (shard_ids[:, None] * send_each + rank_in).reshape(-1)
    row_hot = (
        (local_row.reshape(-1)[None, :] == jnp.arange(TOK, dtype=jnp.int32)[:, None])
        & mine_live[None, :]
    ).astype(jnp.bfloat16)
    column_hot = (column_of[:, None] == slot_ids[None, :]).astype(jnp.bfloat16)
    placing = jnp.dot(row_hot, column_hot, preferred_element_type=jnp.float32)
    is_image = jnp.sum(placing, axis=1) > 0.5
    image_part = jnp.dot(placing.astype(jnp.bfloat16), incoming, preferred_element_type=jnp.float32)
    embeds = jnp.where(is_image[:, None], image_part.astype(jnp.bfloat16), text_rows)
    group = vis_size * tp_size
    group_index = vis_index * tp_size + tp_index
    by_shift = [embeds]
    for shift in range(1, group):
        by_shift.append(
            lax.ppermute(embeds, ("vis", "tp"), [(i, (i + shift) % group) for i in range(group)])
        )
    group_ids = jnp.arange(group, dtype=jnp.int32)
    group_hot = (
        group_ids[None, :] == (group_index - group_ids[:, None]) % group
    ).astype(jnp.bfloat16)
    full_rows = jnp.einsum(
        "sk,ktc->tsc", group_hot, jnp.stack(by_shift, axis=0), preferred_element_type=jnp.float32
    ).astype(jnp.bfloat16).reshape(TOK, -1)
    widened = full_rows.astype(jnp.float32)
    normed_rows = (
        widened
        * lax.rsqrt(jnp.mean(widened * widened, axis=1, keepdims=True) + norm_eps)
        * norm_gain
    ).astype(jnp.bfloat16)
    own_positions = row_positions(
        ctx_index * TOK + jnp.arange(TOK, dtype=jnp.int32), slice_order, TOK
    )
    kv_heads = w_query.shape[1]
    groups = w_query.shape[2]
    projected_half = jnp.einsum(
        "td,dhk->thk", normed_rows, w_keyval[0], preferred_element_type=jnp.float32
    )
    own_half = jnp.where(
        tp_index == 0, rotate(projected_half, own_positions), projected_half
    ).astype(jnp.bfloat16)
    query_weights, own_half = lax.optimization_barrier((w_query, own_half))
    gathered = lax.all_gather(own_half, "ctx", axis=0, tiled=True)
    queries = jnp.einsum(
        "td,dhgk->thgk", normed_rows, query_weights, preferred_element_type=jnp.float32
    )
    queries = rotate(queries, own_positions).astype(jnp.bfloat16)
    key_pos = row_positions(jnp.arange(shards * TOK, dtype=jnp.int32), slice_order, TOK)
    doc_slices = doc_ids.reshape(2 * shards, TOK // 2)
    slice_ids = jnp.stack([slice_order, 2 * shards - 1 - slice_order], axis=1)
    slice_hot = slice_ids[:, :, None] == jnp.arange(2 * shards, dtype=jnp.int32)[None, None, :]
    key_doc = jnp.sum(
        jnp.where(slice_hot[..., None], doc_slices[None, None], 0), axis=2
    ).reshape(shards * TOK)
    own_doc = jnp.sum(
        jnp.where((shard_ids == ctx_index)[:, None], key_doc.reshape(shards, TOK), 0), axis=0
    )
    allowed_now = (key_pos[None, :] <= own_positions[:, None]) & (
        key_doc[None, :] == own_doc[:, None]
    )
    queries, allowed_now, gathered = lax.optimization_barrier((queries, allowed_now, gathered))
    partner_all = swapped(gathered, "tp", 0)
    keys_every = jnp.where(tp_index == 0, gathered, partner_all)
    values_every = jnp.where(tp_index == 0, partner_all, gathered)
    key_count = keys_every.shape[0]
    scores_now = jnp.einsum(
        "qkgd,nkd->kgqn", queries, keys_every, preferred_element_type=jnp.float32
    ) / math.sqrt(HD)
    scores_now = jnp.where(allowed_now[None, None], scores_now, big_negative)
    best = jnp.max(scores_now, axis=-1, keepdims=True)
    powers_now = jnp.exp(scores_now - best)
    total_final = jnp.sum(powers_now, axis=-1)
    accum_final = jnp.einsum(
        "kgqn,nkd->kgqd",
        powers_now.astype(jnp.bfloat16),
        values_every,
        preferred_element_type=jnp.float32,
    )
    result = accum_final / total_final[..., None]
    return (
        jnp.transpose(result, (2, 0, 1, 3)).reshape(TOK, kv_heads, groups * HD).astype(jnp.bfloat16)
    )


def solution(mesh):
    placed = (
        P("ctx", None),
        P(),
        P(),
        P(None, None, ("vis", "tp"), None),
        P(("vis", "tp"), None, None),
        P(),
        P(),
        P("ctx", ("vis", "tp")),
        P(),
        P("ctx"),
        P(),
        P(),
        P(),
        P("ctx", ("vis", "tp")),
        P(),
        P(None, "vis", "tp", None),
        P("tp", None, "vis", None),
    )
    return jax.shard_map(
        local, mesh=mesh, in_specs=placed, out_specs=P("ctx", "vis", "tp"), check_vma=False
    )
```
